128 devices in a mesh: req: 4 (over y_hi, core), tp: 32 (over z, y_lo, x).
Axes of the slice: x: 4, y: 4 (y_hi: 2, y_lo: 2; y = y_hi * 2 + y_lo), z: 4, core: 2. Of those that a mesh axis runs over, the one named last changes fastest.
Arguments:
- tokens: bfloat16 [16384, 1536], P(('req', 'tp')), may hold values from -8 to 8
- segment_ids: int32 [4, 4096], P('req', 'tp'), may hold values from 0 to 3, never falling along the last dimension, each value on 1 to 2048 neighbouring positions
- attention_gain: float32 [1536], replicated, may hold values from 0.1 to 1.9
- joined_qkv: bfloat16 [1536, 2048], replicated, may hold values from -5 to 5
- output_proj: bfloat16 [1536, 1536], replicated, may hold values from -0.15625 to 0.15625
- expert_gain: float32 [1536], replicated, may hold values from 0.1 to 1.9
- expert_ids: int32 [16384, 4], P(('req', 'tp')), may hold values from 0 to 31, all different within a row; in each aligned block of 128 rows (0 to 127, 128 to 255, ...) at most 32 rows name the same one
- gate_weights: float32 [16384, 4], P(('req', 'tp')), may hold values from 0.05 to 0.6
- expert_inner: bfloat16 [32, 1536, 1536], P('tp'), may hold values from -0.15625 to 0.15625
- expert_outer: bfloat16 [32, 768, 1536], P('tp'), may hold values from -0.21875 to 0.21875
- cache_pool: bfloat16 [320, 1024, 512], P('req', 'tp'), may hold values from -6 to 6
- finished: int32 [4, 64], P('req'), may hold values from 0 to 79, as said below
- cache_len: int32 [4, 64], P('req'), may hold values from 1 to 1024, as said below
- destination: int32 [4, 64], P('req'), may hold values from 0 to 127, as said below
Outputs:
- layer_out: bfloat16 [16384, 1536], P(('req', 'tp'))
- decode_cache: bfloat16 [512, 1024, 512], P(('req', 'tp'))
The draws below stay inside these ranges and needn't reach their ends.
Inputs may be any that keep to these rules, and one draw needn't show every extreme that they name: `expert_ids`: the 128 rows of one device name each expert at most 32 times; in every draw some expert is named exactly 32 times by the rows of some device. `finished`: the entries of one group are distinct. `cache_len`: every draw has a length of exactly 1024. `destination`: each group sends exactly two requests to each index of tp, to two different indices of req; so a device receives at most one request from each group, and in every draw some device receives one from every group.
All inputs are finite; a program needn't handle non-finite values.
Results may differ from the reference program's by a relative error of at most 0.012.
Values may be sent and summed in bfloat16 or wider, within the bound.
No kernel may reach another device: no remote copies, remote signals or barrier semaphores. Data moves between devices by JAX's collectives and lax.ppermute only.
A program may use at most 192 MiB of HBM per device.

```python
import math
import jax
import jax.numpy as jnp
import numpy as np
from jax import lax

D = 1536
QUERY_HEADS = 12
KEY_VALUE_HEADS = 2
HEAD_SIZE = 128
FFE = 768
TOPK = 4
SEGS = 4
TOK_DEV = 128
EXPERTS = 32
TOK = 4096
TOKEN_TOTAL = 16384
CAP = 32
KVW = 512
MAXLEN = 1024
FIN = 64
POOL = 80
N_REQ = 4
N_TP = 32


def draw_tokens(key, part):
    first_key, second_key, third_key = jax.random.split(key, 3)
    drawn = jax.random.normal(first_key, (TOKEN_TOTAL, D), jnp.float32)
    row_scale = jnp.exp(jax.random.uniform(second_key, (TOKEN_TOTAL, 1), jnp.float32, math.log(0.3), math.log(3.0)))
    column_scale = jnp.exp(jax.random.uniform(third_key, (1, D), jnp.float32, math.log(0.3), math.log(3.0)))
    return jnp.clip(drawn * row_scale * column_scale, -8.0, 8.0).astype(jnp.bfloat16)


def draw_joined_qkv(key, part):
    combined_width = QUERY_HEADS * HEAD_SIZE + 2 * KEY_VALUE_HEADS * HEAD_SIZE
    drawn = jax.random.normal(key, (D, combined_width), jnp.float32) * D ** (-0.5)
    return jnp.clip(drawn, -5.0, 5.0).astype(jnp.bfloat16)


def draw_finished(key, part):
    group_keys = jax.random.split(key, N_REQ)
    return jax.vmap(lambda one_key: jax.random.permutation(one_key, POOL)[:FIN])(group_keys).astype(jnp.int32)


def draw_cache_len(key, part):
    first_key, second_key = jax.random.split(key)
    lengths = jax.random.randint(first_key, (N_REQ, FIN), 1, MAXLEN + 1, dtype=jnp.int32)
    longest = jax.random.randint(second_key, (N_REQ, 1), 0, FIN, dtype=jnp.int32)
    return jnp.where(jnp.arange(FIN, dtype=jnp.int32)[None, :] == longest, MAXLEN, lengths).astype(jnp.int32)


def draw_destination(key, part):
    first_key, second_key, third_key = jax.random.split(key, 3)
    tp_order = jax.vmap(lambda one_key: jax.random.permutation(one_key, N_TP))(jax.random.split(first_key, N_REQ)).astype(jnp.int32)
    first_req = jax.random.randint(second_key, (N_REQ, N_TP), 0, N_REQ, dtype=jnp.int32)
    first_req = jnp.where(tp_order == 0, 0, first_req)
    step_size = jax.random.randint(third_key, (N_REQ, N_TP), 1, N_REQ, dtype=jnp.int32)
    second_req = (first_req + step_size) % N_REQ
    req_index = jnp.concatenate([first_req, second_req], axis=1)
    tp_index = jnp.concatenate([tp_order, tp_order], axis=1)
    return (req_index * N_TP + tp_index).astype(jnp.int32)


def level_of(key, extent, cuts, low, largest):
    def one(position, parts):
        draws = jax.random.uniform(jax.random.fold_in(jax.random.fold_in(key, 6), position), (parts,), jnp.float32, low / len(cuts), largest / len(cuts))
        return jnp.repeat(jnp.exp(draws), extent[position] // parts).reshape((-1,) + (1,) * (len(extent) - position - 1))

    loudness = one(*cuts[0])
    for cut in cuts[1:]:
        loudness = loudness * one(*cut)
    return loudness


def split_up(number_of, total, bound, lean):
    portions = [(1 << 20) // math.isqrt(standing ** lean) + 1 for standing in range(2, number_of + 1)]
    surplus, holding = total - bound - (number_of - 1), [1] * (number_of - 1)
    while surplus > 0:
        candidates = [i for i in range(number_of - 1) if holding[i] < bound]
        mass, budget = sum([portions[i] for i in candidates]), surplus
        for i in candidates:
            addition = min(bound - holding[i], max(1, budget * portions[i] // mass), surplus)
            holding[i] = holding[i] + addition
            surplus = surplus - addition
    return np.array([bound] + holding)


def ragged_sizes(stream_key, number_of, total, bound, lean):
    if number_of == 2:
        one = jax.random.randint(stream_key, (), max(1, total - bound), min(bound, total - 1) + 1)
        return jnp.stack([one, total - one])
    sizes = jnp.asarray(split_up(number_of, total, bound, lean), jnp.int32)
    pairs = (number_of - 1) // 2
    giver, receiver = sizes[1:1 + 2 * pairs:2], sizes[2:2 + 2 * pairs:2]
    slack = jnp.minimum(giver - 1, bound - receiver)
    passed = jax.random.randint(jax.random.fold_in(stream_key, 1), (pairs,), 0, 1 << 20) % (slack + 1)
    sizes = sizes.at[1:1 + 2 * pairs:2].set(giver - passed).at[2:2 + 2 * pairs:2].set(receiver + passed)
    return sizes[jax.random.permutation(jax.random.fold_in(stream_key, 2), number_of)]


def assign_block(own_key, own, number, rows, number_of, top, limit, skew):
    sequence = jax.random.permutation(own_key, number_of)
    crowded, ordinary = load_shares(number_of, rows * top, limit, skew, True), load_shares(number_of, rows * top, limit, skew, False)
    places = jnp.arange(number_of)

    def named(sizes, offset_by):
        used = int((sizes > 0).sum())
        fixed = max(1, used // 4)
        passed = fixed + (places - fixed + offset_by * (used - fixed)) % max(1, number_of - fixed)
        return jnp.zeros((number_of,), jnp.int32).at[sequence[jnp.where(places < fixed, places, passed)]].set(jnp.asarray(sizes, jnp.int32))

    sizes = jnp.where(number % 4 == 0, named(crowded, number // 4), named(ordinary, number - number // 4 - 1))
    mixed = jax.random.permutation(jax.random.fold_in(own, 3), number_of)
    giver, taker = mixed[0:number_of // 2 * 2:2], mixed[1:number_of // 2 * 2:2]
    margin = jnp.minimum(sizes[giver] - 1, limit - sizes[taker]) // 2
    margin = jnp.where((giver == sequence[0]) | (taker == sequence[0]) | (sizes[taker] == 0), 0, jnp.maximum(margin, 0))
    passed = jax.random.randint(jax.random.fold_in(own, 4), (number_of // 2,), 0, 1 << 20) % (margin + 1)
    sizes = sizes.at[giver].add(-passed).at[taker].add(passed)
    members = jnp.searchsorted(jnp.cumsum(sizes), jnp.arange(rows * top), side="right").astype(jnp.int32)
    listing = members.reshape(top, rows).T
    listing = listing[jax.random.permutation(jax.random.fold_in(own, 1), rows)]
    offset_by = jax.random.randint(jax.random.fold_in(own, 2), (rows, 1), 0, top)
    return jnp.take_along_axis(listing, (jnp.arange(top)[None, :] + offset_by) % top, axis=1)


def load_shares(number_of, total, limit, slope, full):
    weights = [(1 << 20) // math.isqrt(standing ** slope) + 1 for standing in range(1, number_of + 1)]
    largest = limit if full else min(limit, max(-(-total // number_of), total * weights[0] // sum(weights)))
    least = 1 if total - largest >= number_of - 1 else 0
    holding, surplus = [largest] + [least] * (number_of - 1), total - largest - least * (number_of - 1)
    while surplus > 0:
        movable = [i for i in range(1, number_of) if holding[i] < largest] or [i for i in range(1, number_of) if holding[i] < limit]
        mass, remaining = sum([weights[i] for i in movable]), surplus
        for i in movable:
            addition = min(limit - holding[i], max(1, remaining * weights[i] // mass), surplus)
            holding[i] = holding[i] + addition
            surplus = surplus - addition
    return np.array(holding)


def bell_draw(own_key, dims, deviation, most, shards=(), kind=jnp.bfloat16):
    gain = level_of(own_key, dims, shards, -0.22, 0.18) if shards else 1.0
    array = jax.random.normal(own_key, dims, jnp.float32) * deviation * gain
    return jnp.minimum(jnp.maximum(array, -most), most).astype(kind)


def setup_inputs(seed: int = 0) -> dict:
    key_of = jax.random.split(jax.random.key(seed), 15)
    tokens = draw_tokens(jax.random.fold_in(key_of[14], 71), 0)
    segment_ids = jax.vmap(lambda own: jnp.searchsorted(jnp.cumsum(ragged_sizes(own, SEGS, TOK, TOK // 2, 2)), jnp.arange(TOK), side="right"))(jax.random.split(key_of[1], N_REQ)).reshape((N_REQ, TOK)).astype(jnp.int32)
    attention_gain = jnp.clip(1.0 + 0.18 * jax.random.normal(key_of[2], (D,), jnp.float32), 0.1, 1.9)
    joined_qkv = draw_joined_qkv(jax.random.fold_in(key_of[14], 71), 0)
    output_proj = bell_draw(key_of[4], (QUERY_HEADS * HEAD_SIZE, D), (QUERY_HEADS * HEAD_SIZE) ** -0.5, 0.15625)
    expert_gain = jnp.clip(1.0 + 0.18 * jax.random.normal(key_of[5], (D,), jnp.float32), 0.1, 1.9)
    expert_ids_keys = jax.random.split(jax.random.fold_in(key_of[6], 1), TOKEN_TOTAL // TOK_DEV)
    expert_ids_turns = jax.random.permutation(jax.random.fold_in(key_of[6], 3), TOKEN_TOTAL // TOK_DEV)
    expert_ids = jax.vmap(lambda own, number: assign_block(jax.random.fold_in(key_of[6], 2), own, number, TOK_DEV, EXPERTS, TOPK, CAP, 2))(expert_ids_keys, expert_ids_turns).reshape((TOKEN_TOTAL, TOPK))
    gate_weights = jnp.clip(0.05 + 0.55 * jax.random.uniform(key_of[7], (TOKEN_TOTAL, TOPK), jnp.float32) ** level_of(key_of[7], (TOKEN_TOTAL, TOPK), ((0, 128),), -0.2, 0.2), 0.05, 0.6)
    expert_inner = bell_draw(key_of[8], (EXPERTS, D, 2 * FFE), D ** -0.5, 0.15625, ((0, 32),))
    expert_outer = bell_draw(key_of[9], (EXPERTS, FFE, D), FFE ** -0.5, 0.21875, ((0, 32),))
    cache_pool = bell_draw(key_of[10], (N_REQ * POOL, MAXLEN, KVW), 1.0, 6.0, ((0, 4), (1, 32)))
    finished = draw_finished(jax.random.fold_in(key_of[14], 71), 0)
    cache_len = draw_cache_len(jax.random.fold_in(key_of[14], 71), 0)
    destination = draw_destination(jax.random.fold_in(key_of[14], 71), 0)
    return {"tokens": tokens, "segment_ids": segment_ids, "attention_gain": attention_gain, "joined_qkv": joined_qkv, "output_proj": output_proj, "expert_gain": expert_gain, "expert_ids": expert_ids, "gate_weights": gate_weights, "expert_inner": expert_inner, "expert_outer": expert_outer, "cache_pool": cache_pool, "finished": finished, "cache_len": cache_len, "destination": destination}


epsilon = 1e-06
rope_base = 1000000.0
NEGATIVE_FILL = -1e+30

def rms_gain(values_in, gain_row):
    as_float = values_in.astype(jnp.float32)
    scale = lax.rsqrt(lax.optimization_barrier(jnp.mean(as_float * as_float, axis=-1, keepdims=True)) + epsilon)
    return (as_float * scale * gain_row).astype(jnp.bfloat16)

def apply_rotary(vectors, token_positions):
    half_dim = vectors.shape[-1] // 2
    frequency = rope_base ** (-jnp.arange(half_dim, dtype=jnp.float32) * 2.0 / vectors.shape[-1])
    angles = token_positions[:, None] * frequency[None, :]
    cosine = jnp.cos(angles)[:, None, :]
    sine_values = jnp.sin(angles)[:, None, :]
    first_half = vectors[..., :half_dim]
    second_half = vectors[..., half_dim:]
    return jnp.concatenate([first_half * cosine - second_half * sine_values, second_half * cosine + first_half * sine_values], axis=-1)

def reference(tokens, segment_ids, attention_gain, joined_qkv, output_proj, expert_gain, expert_ids, gate_weights, expert_inner, expert_outer, cache_pool, finished, cache_len, destination):
    hidden = rms_gain(tokens, attention_gain)
    joined_everything = jnp.dot(hidden, joined_qkv, preferred_element_type=jnp.float32)
    token_positions = (jnp.arange(TOKEN_TOTAL, dtype=jnp.int32) % TOK).astype(jnp.float32)
    query_span_width = QUERY_HEADS * HEAD_SIZE
    key_span_width = KEY_VALUE_HEADS * HEAD_SIZE
    query_rows = apply_rotary(joined_everything[:, :query_span_width].reshape(TOKEN_TOTAL, QUERY_HEADS, HEAD_SIZE), token_positions).astype(jnp.bfloat16)
    key_row_list = apply_rotary(joined_everything[:, query_span_width:query_span_width + key_span_width].reshape(TOKEN_TOTAL, KEY_VALUE_HEADS, HEAD_SIZE), token_positions).astype(jnp.bfloat16)
    value_rows = joined_everything[:, query_span_width + key_span_width:].reshape(TOKEN_TOTAL, KEY_VALUE_HEADS, HEAD_SIZE).astype(jnp.bfloat16)
    heads_per_group = QUERY_HEADS // KEY_VALUE_HEADS
    rows_per_block = min(512, TOK)
    block_count = TOK // rows_per_block

    def one_block(block_index):
        group_index = block_index // block_count
        inner_start = block_index % block_count * rows_per_block
        first_row = (group_index * TOK + inner_start).astype(jnp.int32)
        query_tile_rows = lax.dynamic_slice_in_dim(query_rows, first_row, rows_per_block, 0)
        key_block = lax.dynamic_slice_in_dim(key_row_list, (group_index * TOK).astype(jnp.int32), TOK, 0)
        value_block = lax.dynamic_slice_in_dim(value_rows, (group_index * TOK).astype(jnp.int32), TOK, 0)
        seg_group = lax.dynamic_index_in_dim(segment_ids, group_index.astype(jnp.int32), 0, keepdims=False)
        query_seg = lax.dynamic_slice_in_dim(seg_group, inner_start.astype(jnp.int32), rows_per_block, 0)
        grouped_queries = query_tile_rows.reshape(rows_per_block, KEY_VALUE_HEADS, heads_per_group, HEAD_SIZE).transpose(1, 2, 0, 3).reshape(KEY_VALUE_HEADS, heads_per_group * rows_per_block, HEAD_SIZE)
        scores = jnp.einsum('gqd,kgd->gqk', grouped_queries.astype(jnp.float32), key_block.astype(jnp.float32)) * HEAD_SIZE ** (-0.5)
        query_places = jnp.tile(inner_start + jnp.arange(rows_per_block, dtype=jnp.int32), heads_per_group)
        query_segs = jnp.tile(query_seg, heads_per_group)
        key_places = jnp.arange(TOK, dtype=jnp.int32)
        visible = (key_places[None, :] <= query_places[:, None]) & (seg_group[None, :] == query_segs[:, None])
        row_max = lax.optimization_barrier(jnp.max(jnp.where(visible[None], scores, NEGATIVE_FILL), axis=2, keepdims=True))
        weights = jnp.where(visible[None], jnp.exp(scores - row_max), 0.0)
        running_totals = lax.optimization_barrier(jnp.sum(weights, axis=2, keepdims=True))
        weighted_total = jnp.einsum('gqk,kgd->gqd', weights.astype(jnp.bfloat16).astype(jnp.float32), value_block.astype(jnp.float32))
        final_output = (weighted_total / running_totals).reshape(KEY_VALUE_HEADS, heads_per_group, rows_per_block, HEAD_SIZE).transpose(2, 0, 1, 3).reshape(rows_per_block, QUERY_HEADS * HEAD_SIZE)
        return final_output.astype(jnp.bfloat16)
    results = lax.map(one_block, jnp.arange(N_REQ * block_count, dtype=jnp.int32))
    attended = results.reshape(TOKEN_TOTAL, QUERY_HEADS * HEAD_SIZE)
    projected = jnp.dot(attended, output_proj, preferred_element_type=jnp.float32)
    middle = (tokens.astype(jnp.float32) + projected).astype(jnp.bfloat16)
    normed = rms_gain(middle, expert_gain)
    flat_ids = expert_ids.reshape(-1).astype(jnp.int32)
    owner_block = jnp.arange(TOKEN_TOTAL * TOPK, dtype=jnp.int32) // (TOK_DEV * TOPK)
    onehot = (flat_ids[:, None] == jnp.arange(EXPERTS, dtype=jnp.int32)[None, :]).astype(jnp.int32)
    running = jnp.cumsum(onehot.reshape(N_REQ * N_TP, TOK_DEV * TOPK, EXPERTS), axis=1).reshape(TOKEN_TOTAL * TOPK, EXPERTS)
    slot_rank = lax.optimization_barrier(jnp.sum(running * onehot, axis=1)) - 1
    column_index = (owner_block * CAP + slot_rank).astype(jnp.int32)
    token_of = jnp.arange(TOKEN_TOTAL * TOPK, dtype=jnp.int32) // TOPK
    slot_token = jnp.zeros((EXPERTS, N_REQ * N_TP * CAP), jnp.int32).at[flat_ids, column_index].set(token_of)
    slot_gate = jnp.zeros((EXPERTS, N_REQ * N_TP * CAP), jnp.float32).at[flat_ids, column_index].set(gate_weights.reshape(-1))

    def one_expert(running_totals, expert_index):
        rows_in = slot_token[expert_index]
        gathered = normed[rows_in]
        inner_out = jnp.dot(gathered, expert_inner[expert_index], preferred_element_type=jnp.float32)
        active = (jnp.maximum(inner_out[:, :FFE], 0.0) * inner_out[:, FFE:]).astype(jnp.bfloat16)
        final_output = jnp.dot(active, expert_outer[expert_index], preferred_element_type=jnp.float32).astype(jnp.bfloat16)
        return (running_totals.at[rows_in].add(slot_gate[expert_index][:, None] * final_output.astype(jnp.float32)), None)
    mixed, _ = lax.scan(one_expert, jnp.zeros((TOKEN_TOTAL, D), jnp.float32), jnp.arange(EXPERTS, dtype=jnp.int32))
    layer_out = (middle.astype(jnp.float32) + mixed).astype(jnp.bfloat16)
    groups = jnp.arange(N_REQ, dtype=jnp.int32)[:, None]
    sender_device = (groups * POOL + finished).reshape(-1).astype(jnp.int32)
    pieces = cache_pool[sender_device]
    kept_mask = jnp.arange(MAXLEN, dtype=jnp.int32)[None, :] < cache_len.reshape(-1)[:, None]
    pieces = jnp.where(kept_mask[:, :, None], pieces, jnp.zeros((), pieces.dtype))
    slot_index = (destination * N_REQ + groups).reshape(-1).astype(jnp.int32)
    decode_cache = jnp.zeros((N_REQ * N_TP * N_REQ, MAXLEN, KVW), cache_pool.dtype).at[slot_index].set(pieces)
    return (layer_out, decode_cache)
```

```python
import functools

import jax
import jax.numpy as jnp
from jax import lax
from jax.experimental import pallas as pl
from jax.experimental.pallas import tpu as pltpu
from jax.sharding import PartitionSpec as P

QUERY_HEADS = 12
KEY_VALUE_HEADS = 2
HEAD_SIZE = 128
KEY_BLOCK = 256


epsilon = 1e-06
rope_base = 1000000.0
NEGATIVE_FILL = -1e30


def rms_gain(values_in, gain_row):
    as_float = values_in.astype(jnp.float32)
    scale = lax.rsqrt(jnp.mean(as_float * as_float, axis=-1, keepdims=True) + epsilon)
    return (as_float * scale * gain_row).astype(jnp.bfloat16)


def apply_rotary(vectors, token_positions):
    half_dim = vectors.shape[-1] // 2
    frequency = rope_base ** (-jnp.arange(half_dim, dtype=jnp.float32) * 2.0 / vectors.shape[-1])
    angles = token_positions[:, None] * frequency[None, :]
    cosine = jnp.cos(angles)[:, None, :]
    sine_values = jnp.sin(angles)[:, None, :]
    first_half = vectors[..., :half_dim]
    second_half = vectors[..., half_dim:]
    return jnp.concatenate(
        [
            first_half * cosine - second_half * sine_values,
            second_half * cosine + first_half * sine_values,
        ],
        axis=-1,
    )


def attention_kernel(bounds_ref, q_ref, k_ref, v_ref, lo_ref, hi_ref, o_ref):
    first_block = bounds_ref[0]
    end_block = bounds_ref[1]
    queries = q_ref[...]
    low = lo_ref[...]
    high = hi_ref[...]
    rows = queries.shape[0]
    scale = HEAD_SIZE ** (-0.5)

    def scores_of(block):
        start = pl.multiple_of(block * KEY_BLOCK, KEY_BLOCK)
        keys = k_ref[pl.ds(start, KEY_BLOCK), :]
        scores = (
            lax.dot_general(
                queries, keys, (((1,), (1,)), ((), ())), preferred_element_type=jnp.float32
            )
            * scale
        )
        places = start + lax.broadcasted_iota(jnp.int32, (1, KEY_BLOCK), 1)
        visible = (places >= low) & (places <= high)
        return scores, visible, start

    def max_step(block, best):
        scores, visible, _ = scores_of(block)
        masked = jnp.where(visible, scores, NEGATIVE_FILL)
        return jnp.maximum(best, jnp.max(masked, axis=1, keepdims=True))

    best = lax.fori_loop(
        first_block, end_block, max_step, jnp.full((rows, 1), NEGATIVE_FILL, jnp.float32)
    )

    def sum_step(block, carry):
        totals, running = carry
        scores, visible, start = scores_of(block)
        weights = jnp.where(visible, jnp.exp(scores - best), 0.0)
        totals = totals + jnp.sum(weights, axis=1, keepdims=True)
        values = v_ref[pl.ds(start, KEY_BLOCK), :]
        running = running + jnp.dot(
            weights.astype(jnp.bfloat16), values, preferred_element_type=jnp.float32
        )
        return totals, running

    totals, running = lax.fori_loop(
        first_block,
        end_block,
        sum_step,
        (jnp.zeros((rows, 1), jnp.float32), jnp.zeros((rows, HEAD_SIZE), jnp.float32)),
    )
    o_ref[...] = (running / totals).astype(o_ref.dtype)


def attention(bounds, query_rows, key_vals, low, high):
    device_rows = query_rows.shape[0]
    prompt_length = key_vals.shape[0]
    heads_per_group = QUERY_HEADS // KEY_VALUE_HEADS
    grid_spec = pltpu.PrefetchScalarGridSpec(
        num_scalar_prefetch=1,
        grid=(KEY_VALUE_HEADS, heads_per_group),
        in_specs=[
            pl.BlockSpec(
                (device_rows, HEAD_SIZE), lambda g, h, b: (0, g * heads_per_group + h)
            ),
            pl.BlockSpec((prompt_length, HEAD_SIZE), lambda g, h, b: (0, g)),
            pl.BlockSpec(
                (prompt_length, HEAD_SIZE), lambda g, h, b: (0, KEY_VALUE_HEADS + g)
            ),
            pl.BlockSpec((device_rows, 1), lambda g, h, b: (0, 0)),
            pl.BlockSpec((device_rows, 1), lambda g, h, b: (0, 0)),
        ],
        out_specs=pl.BlockSpec(
            (device_rows, HEAD_SIZE), lambda g, h, b: (0, g * heads_per_group + h)
        ),
    )
    return pl.pallas_call(
        attention_kernel,
        grid_spec=grid_spec,
        out_shape=jax.ShapeDtypeStruct((device_rows, QUERY_HEADS * HEAD_SIZE), jnp.bfloat16),
    )(bounds, query_rows, key_vals, key_vals, low, high)


def local(
    tokens,
    segment_ids,
    attention_gain,
    joined_qkv,
    output_proj,
    expert_gain,
    expert_ids,
    gate_weights,
    expert_inner,
    expert_outer,
    cache_pool,
    finished,
    cache_len,
    destination,
):
    tp_count = lax.axis_size("tp")
    where_tp = lax.axis_index("tp")
    replicas = lax.axis_size("req")

    chosen = finished.reshape(-1)
    lengths = cache_len.reshape(-1)
    target = destination.reshape(-1)
    cache_depth = cache_pool.shape[1]
    kv_width = cache_pool.shape[2]
    pieces = cache_pool[chosen]
    positions = where_tp * cache_depth + jnp.arange(cache_depth, dtype=jnp.int32)
    kept_mask = positions[None, :] < lengths[:, None]
    pieces = jnp.where(kept_mask[:, :, None], pieces, jnp.zeros((), jnp.bfloat16))
    outgoing_cache = (
        jnp.zeros((replicas * tp_count, cache_depth, kv_width), jnp.bfloat16).at[target].set(pieces)
    )
    arrived_cache = lax.all_to_all(
        outgoing_cache, ("req", "tp"), split_axis=0, concat_axis=1, tiled=True
    )
    decode_cache = arrived_cache.reshape(replicas, tp_count * cache_depth, kv_width)

    device_rows = tokens.shape[0]
    width = tokens.shape[1]
    seg_local = segment_ids.reshape(device_rows)
    row_span = jnp.arange(device_rows, dtype=jnp.int32)
    token_positions = where_tp * device_rows + row_span
    segment_count = 4
    below = jnp.sum(
        (seg_local[None, :] < jnp.arange(segment_count, dtype=jnp.int32)[:, None]).astype(
            jnp.float32
        ),
        axis=1,
    )
    segment_start = lax.psum(below, "tp").astype(jnp.int32)
    low = segment_start[seg_local]
    high = token_positions
    prompt_length = device_rows * tp_count
    first_block = jnp.min(low) // KEY_BLOCK
    end_block = jnp.max(high) // KEY_BLOCK + 1
    bounds = jnp.stack([first_block, end_block]).astype(jnp.int32)

    hidden = rms_gain(tokens, attention_gain)
    joined_everything = jnp.dot(hidden, joined_qkv, preferred_element_type=jnp.float32)
    query_span_width = QUERY_HEADS * HEAD_SIZE
    key_span_width = KEY_VALUE_HEADS * HEAD_SIZE
    float_places = token_positions.astype(jnp.float32)
    query_rows = apply_rotary(
        joined_everything[:, :query_span_width].reshape(device_rows, QUERY_HEADS, HEAD_SIZE),
        float_places,
    ).astype(jnp.bfloat16)
    key_row_list = apply_rotary(
        joined_everything[:, query_span_width : query_span_width + key_span_width].reshape(
            device_rows, KEY_VALUE_HEADS, HEAD_SIZE
        ),
        float_places,
    ).astype(jnp.bfloat16)
    value_rows = joined_everything[:, query_span_width + key_span_width :].astype(jnp.bfloat16)
    key_vals = jnp.concatenate(
        [key_row_list.reshape(device_rows, key_span_width), value_rows], axis=1
    )
    key_value_portion = lax.all_gather(key_vals, "tp", axis=0, tiled=True)
    attended = attention(
        bounds,
        query_rows.reshape(device_rows, query_span_width),
        key_value_portion,
        low.reshape(device_rows, 1),
        high.reshape(device_rows, 1),
    )
    projected = jnp.dot(attended, output_proj, preferred_element_type=jnp.float32)
    middle = (tokens.astype(jnp.float32) + projected).astype(jnp.bfloat16)
    normed = rms_gain(middle, expert_gain)
    top_count = expert_ids.shape[1]
    held_count = expert_inner.shape[0]
    total_experts = held_count * tp_count
    capacity = 2 * device_rows * top_count // total_experts
    flat_ids = expert_ids.reshape(device_rows * top_count)
    onehot = (flat_ids[:, None] == jnp.arange(total_experts, dtype=jnp.int32)[None, :]).astype(
        jnp.int32
    )
    slot_rank = jnp.sum(jnp.cumsum(onehot, axis=0) * onehot, axis=1) - 1
    column_index = flat_ids * capacity + slot_rank
    token_of = jnp.arange(device_rows * top_count, dtype=jnp.int32) // top_count
    outgoing = (
        jnp.zeros((total_experts * capacity, width), jnp.bfloat16)
        .at[column_index]
        .set(normed[token_of])
    )
    outgoing = outgoing.reshape(tp_count, held_count, capacity, width)
    hidden_width = expert_outer.shape[1]
    inner_out = jnp.einsum(
        "sgcd,gdf->sgcf",
        lax.all_to_all(outgoing, "tp", split_axis=0, concat_axis=0, tiled=True),
        expert_inner,
        preferred_element_type=jnp.float32,
    )
    active = (
        jnp.maximum(inner_out[..., :hidden_width], 0.0) * inner_out[..., hidden_width:]
    ).astype(jnp.bfloat16)
    final_output = jnp.einsum(
        "sgcf,gfd->sgcd", active, expert_outer, preferred_element_type=jnp.float32
    ).astype(jnp.bfloat16)
    returned = lax.all_to_all(final_output, "tp", split_axis=0, concat_axis=0, tiled=True)
    answers = returned.reshape(total_experts * capacity, width)[column_index].reshape(
        device_rows, top_count, width
    )
    mixed = jnp.sum(answers.astype(jnp.float32) * gate_weights[..., None], axis=1)
    layer_out = (middle.astype(jnp.float32) + mixed).astype(jnp.bfloat16)
    return (layer_out, decode_cache)


def solution(mesh):
    placed = (
        P(("req", "tp"), None),
        P("req", "tp"),
        P(),
        P(),
        P(),
        P(),
        P(("req", "tp"), None),
        P(("req", "tp"), None),
        P("tp", None, None),
        P("tp", None, None),
        P("req", "tp", None),
        P("req", None),
        P("req", None),
        P("req", None),
    )
    return jax.shard_map(
        local,
        mesh=mesh,
        in_specs=placed,
        out_specs=(P(("req", "tp"), None), P(("req", "tp"), None, None)),
        check_vma=False,
    )
```

```python
import functools

import jax
import jax.numpy as jnp
from jax import lax
from jax.experimental import pallas as pl
from jax.experimental.pallas import tpu as pltpu
from jax.sharding import PartitionSpec as P

QUERY_HEADS = 12
KEY_VALUE_HEADS = 2
HEAD_SIZE = 128
KEY_BLOCK = 128
LONGEST_SEGMENT = 2048


epsilon = 1e-06
rope_base = 1000000.0
NEGATIVE_FILL = -1e30


def rms_gain(values_in, gain_row):
    as_float = values_in.astype(jnp.float32)
    scale = lax.rsqrt(jnp.mean(as_float * as_float, axis=-1, keepdims=True) + epsilon)
    return (as_float * scale * gain_row).astype(jnp.bfloat16)


def apply_rotary(vectors, token_positions):
    half_dim = vectors.shape[-1] // 2
    frequency = rope_base ** (-jnp.arange(half_dim, dtype=jnp.float32) * 2.0 / vectors.shape[-1])
    angles = token_positions[:, None] * frequency[None, :]
    cosine = jnp.cos(angles)[:, None, :]
    sine_values = jnp.sin(angles)[:, None, :]
    first_half = vectors[..., :half_dim]
    second_half = vectors[..., half_dim:]
    return jnp.concatenate(
        [
            first_half * cosine - second_half * sine_values,
            second_half * cosine + first_half * sine_values,
        ],
        axis=-1,
    )


def attention_kernel(bounds_ref, q_ref, k_ref, v_ref, lo_ref, hi_ref, o_ref):
    first_block = bounds_ref[0]
    end_block = bounds_ref[1]
    queries = q_ref[...]
    low = lo_ref[...]
    high = hi_ref[...]
    rows = queries.shape[0]
    scale = HEAD_SIZE ** (-0.5)

    def scores_of(block):
        start = pl.multiple_of(block * KEY_BLOCK, KEY_BLOCK)
        keys = k_ref[pl.ds(start, KEY_BLOCK), :]
        scores = (
            lax.dot_general(
                queries, keys, (((1,), (1,)), ((), ())), preferred_element_type=jnp.float32
            )
            * scale
        )
        places = start + lax.broadcasted_iota(jnp.int32, (1, KEY_BLOCK), 1)
        visible = (places >= low) & (places <= high)
        return scores, visible, start

    def max_step(block, best):
        scores, visible, _ = scores_of(block)
        masked = jnp.where(visible, scores, NEGATIVE_FILL)
        return jnp.maximum(best, jnp.max(masked, axis=1, keepdims=True))

    best = lax.fori_loop(
        first_block, end_block, max_step, jnp.full((rows, 1), NEGATIVE_FILL, jnp.float32)
    )

    def sum_step(block, carry):
        totals, running = carry
        scores, visible, start = scores_of(block)
        weights = jnp.where(visible, jnp.exp(scores - best), 0.0)
        totals = totals + jnp.sum(weights, axis=1, keepdims=True)
        values = v_ref[pl.ds(start, KEY_BLOCK), :]
        running = running + jnp.dot(
            weights.astype(jnp.bfloat16), values, preferred_element_type=jnp.float32
        )
        return totals, running

    totals, running = lax.fori_loop(
        first_block,
        end_block,
        sum_step,
        (jnp.zeros((rows, 1), jnp.float32), jnp.zeros((rows, HEAD_SIZE), jnp.float32)),
    )
    o_ref[...] = (running / totals).astype(o_ref.dtype)


def attention(bounds, query_rows, key_vals, low, high):
    device_rows = query_rows.shape[0]
    prompt_length = key_vals.shape[0]
    heads_per_group = QUERY_HEADS // KEY_VALUE_HEADS
    grid_spec = pltpu.PrefetchScalarGridSpec(
        num_scalar_prefetch=1,
        grid=(KEY_VALUE_HEADS, heads_per_group),
        in_specs=[
            pl.BlockSpec(
                (device_rows, HEAD_SIZE), lambda g, h, b: (0, g * heads_per_group + h)
            ),
            pl.BlockSpec((prompt_length, HEAD_SIZE), lambda g, h, b: (0, g)),
            pl.BlockSpec(
                (prompt_length, HEAD_SIZE), lambda g, h, b: (0, KEY_VALUE_HEADS + g)
            ),
            pl.BlockSpec((device_rows, 1), lambda g, h, b: (0, 0)),
            pl.BlockSpec((device_rows, 1), lambda g, h, b: (0, 0)),
        ],
        out_specs=pl.BlockSpec(
            (device_rows, HEAD_SIZE), lambda g, h, b: (0, g * heads_per_group + h)
        ),
    )
    return pl.pallas_call(
        attention_kernel,
        grid_spec=grid_spec,
        out_shape=jax.ShapeDtypeStruct((device_rows, QUERY_HEADS * HEAD_SIZE), jnp.bfloat16),
    )(bounds, query_rows, key_vals, key_vals, low, high)


def local(
    tokens,
    segment_ids,
    attention_gain,
    joined_qkv,
    output_proj,
    expert_gain,
    expert_ids,
    gate_weights,
    expert_inner,
    expert_outer,
    cache_pool,
    finished,
    cache_len,
    destination,
):
    tp_count = lax.axis_size("tp")
    where_tp = lax.axis_index("tp")
    replicas = lax.axis_size("req")

    chosen = finished.reshape(-1)
    lengths = cache_len.reshape(-1)
    target = destination.reshape(-1)
    cache_depth = cache_pool.shape[1]
    kv_width = cache_pool.shape[2]
    pieces = cache_pool[chosen]
    positions = where_tp * cache_depth + jnp.arange(cache_depth, dtype=jnp.int32)
    kept_mask = positions[None, :] < lengths[:, None]
    pieces = jnp.where(kept_mask[:, :, None], pieces, jnp.zeros((), jnp.bfloat16))
    outgoing_cache = (
        jnp.zeros((replicas * tp_count, cache_depth, kv_width), jnp.bfloat16).at[target].set(pieces)
    )
    arrived_cache = lax.all_to_all(
        outgoing_cache, ("req", "tp"), split_axis=0, concat_axis=1, tiled=True
    )
    decode_cache = arrived_cache.reshape(replicas, tp_count * cache_depth, kv_width)

    device_rows = tokens.shape[0]
    width = tokens.shape[1]
    seg_local = segment_ids.reshape(device_rows)
    row_span = jnp.arange(device_rows, dtype=jnp.int32)
    token_positions = where_tp * device_rows + row_span
    hidden = rms_gain(tokens, attention_gain)
    joined_everything = jnp.dot(hidden, joined_qkv, preferred_element_type=jnp.float32)
    query_span_width = QUERY_HEADS * HEAD_SIZE
    key_span_width = KEY_VALUE_HEADS * HEAD_SIZE
    float_places = token_positions.astype(jnp.float32)
    query_rows = apply_rotary(
        joined_everything[:, :query_span_width].reshape(device_rows, QUERY_HEADS, HEAD_SIZE),
        float_places,
    ).astype(jnp.bfloat16)
    key_row_list = apply_rotary(
        joined_everything[:, query_span_width : query_span_width + key_span_width].reshape(
            device_rows, KEY_VALUE_HEADS, HEAD_SIZE
        ),
        float_places,
    ).astype(jnp.bfloat16)
    value_rows = joined_everything[:, query_span_width + key_span_width :].astype(jnp.bfloat16)
    key_vals = jnp.concatenate(
        [key_row_list.reshape(device_rows, key_span_width), value_rows], axis=1
    )
    reach = -(-(LONGEST_SEGMENT - 1) // device_rows)
    seg_rows = jnp.zeros((16, key_vals.shape[1]), jnp.bfloat16)
    seg_rows = seg_rows.at[0, :device_rows].set(seg_local.astype(jnp.bfloat16))
    block = jnp.concatenate([key_vals, seg_rows], axis=0)
    received = [block]
    for shift in range(1, reach + 1):
        pairs = [(i, i + shift) for i in range(tp_count - shift)]
        received.append(lax.ppermute(block, "tp", pairs))
    window = jnp.stack(received[::-1])
    window_rows = (reach + 1) * device_rows
    kv_window = window[:, :device_rows, :].reshape(window_rows, key_vals.shape[1])
    seg_window = window[:, device_rows, :device_rows].astype(jnp.int32).reshape(window_rows)
    base = (where_tp - reach) * device_rows
    window_places = base + jnp.arange(window_rows, dtype=jnp.int32)
    segment_count = 4
    below = jnp.sum(
        (
            (window_places[None, :] >= 0)
            & (seg_window[None, :] < jnp.arange(segment_count, dtype=jnp.int32)[:, None])
        ).astype(jnp.int32),
        axis=1,
    )
    low = jnp.maximum(base, 0) + below[seg_local] - base
    high = token_positions - base
    first_block = jnp.min(low) // KEY_BLOCK
    end_block = jnp.max(high) // KEY_BLOCK + 1
    bounds = jnp.stack([first_block, end_block]).astype(jnp.int32)
    attended = attention(
        bounds,
        query_rows.reshape(device_rows, query_span_width),
        kv_window,
        low.reshape(device_rows, 1),
        high.reshape(device_rows, 1),
    )
    projected = jnp.dot(attended, output_proj, preferred_element_type=jnp.float32)
    middle = (tokens.astype(jnp.float32) + projected).astype(jnp.bfloat16)
    normed = rms_gain(middle, expert_gain)
    top_count = expert_ids.shape[1]
    held_count = expert_inner.shape[0]
    total_experts = held_count * tp_count
    capacity = 2 * device_rows * top_count // total_experts
    flat_ids = expert_ids.reshape(device_rows * top_count)
    onehot = (flat_ids[:, None] == jnp.arange(total_experts, dtype=jnp.int32)[None, :]).astype(
        jnp.int32
    )
    slot_rank = jnp.sum(jnp.cumsum(onehot, axis=0) * onehot, axis=1) - 1
    column_index = flat_ids * capacity + slot_rank
    token_of = jnp.arange(device_rows * top_count, dtype=jnp.int32) // top_count
    outgoing = (
        jnp.zeros((total_experts * capacity, width), jnp.bfloat16)
        .at[column_index]
        .set(normed[token_of])
    )
    outgoing = outgoing.reshape(tp_count, held_count, capacity, width)
    hidden_width = expert_outer.shape[1]
    inner_out = jnp.einsum(
        "sgcd,gdf->sgcf",
        lax.all_to_all(outgoing, "tp", split_axis=0, concat_axis=0, tiled=True),
        expert_inner,
        preferred_element_type=jnp.float32,
    )
    active = (
        jnp.maximum(inner_out[..., :hidden_width], 0.0) * inner_out[..., hidden_width:]
    ).astype(jnp.bfloat16)
    final_output = jnp.einsum(
        "sgcf,gfd->sgcd", active, expert_outer, preferred_element_type=jnp.float32
    ).astype(jnp.bfloat16)
    returned = lax.all_to_all(final_output, "tp", split_axis=0, concat_axis=0, tiled=True)
    answers = returned.reshape(total_experts * capacity, width)[column_index].reshape(
        device_rows, top_count, width
    )
    mixed = jnp.sum(answers.astype(jnp.float32) * gate_weights[..., None], axis=1)
    layer_out = (middle.astype(jnp.float32) + mixed).astype(jnp.bfloat16)
    return (layer_out, decode_cache)


def solution(mesh):
    placed = (
        P(("req", "tp"), None),
        P("req", "tp"),
        P(),
        P(),
        P(),
        P(),
        P(("req", "tp"), None),
        P(("req", "tp"), None),
        P("tp", None, None),
        P("tp", None, None),
        P("req", "tp", None),
        P("req", None),
        P("req", None),
        P("req", None),
    )
    return jax.shard_map(
        local,
        mesh=mesh,
        in_specs=placed,
        out_specs=(P(("req", "tp"), None), P(("req", "tp"), None, None)),
        check_vma=False,
    )
```

```python
import functools

import jax
import jax.numpy as jnp
from jax import lax
from jax.experimental import pallas as pl
from jax.experimental.pallas import tpu as pltpu
from jax.sharding import PartitionSpec as P

QUERY_HEADS = 12
KEY_VALUE_HEADS = 2
HEAD_SIZE = 128
KEY_BLOCK = 256
LONGEST_SEGMENT = 2048


epsilon = 1e-06
rope_base = 1000000.0
NEGATIVE_FILL = -1e30


def rms_gain(values_in, gain_row):
    as_float = values_in.astype(jnp.float32)
    scale = lax.rsqrt(jnp.mean(as_float * as_float, axis=-1, keepdims=True) + epsilon)
    return (as_float * scale * gain_row).astype(jnp.bfloat16)


def apply_rotary(vectors, token_positions):
    half_dim = vectors.shape[-1] // 2
    frequency = rope_base ** (-jnp.arange(half_dim, dtype=jnp.float32) * 2.0 / vectors.shape[-1])
    angles = token_positions[:, None] * frequency[None, :]
    cosine = jnp.cos(angles)[:, None, :]
    sine_values = jnp.sin(angles)[:, None, :]
    first_half = vectors[..., :half_dim]
    second_half = vectors[..., half_dim:]
    return jnp.concatenate(
        [
            first_half * cosine - second_half * sine_values,
            second_half * cosine + first_half * sine_values,
        ],
        axis=-1,
    )


def attention_kernel(bounds_ref, q_ref, k_ref, v_ref, lo_ref, hi_ref, o_ref):
    first_block = bounds_ref[0]
    end_block = bounds_ref[1]
    top_low = bounds_ref[2]
    bottom_high = bounds_ref[3]
    queries = q_ref[...]
    low = lo_ref[...]
    high = hi_ref[...]
    rows = queries.shape[0]
    scale = HEAD_SIZE ** (-0.5)

    def scores_of(start):
        keys = k_ref[pl.ds(start, KEY_BLOCK), :]
        return (
            lax.dot_general(
                queries, keys, (((1,), (1,)), ((), ())), preferred_element_type=jnp.float32
            )
            * scale
        )

    def visible_of(start):
        places = start + lax.broadcasted_iota(jnp.int32, (1, KEY_BLOCK), 1)
        return (places >= low) & (places <= high)

    def whole(start):
        return (start >= top_low) & (start + KEY_BLOCK - 1 <= bottom_high)

    def max_step(block, best):
        start = pl.multiple_of(block * KEY_BLOCK, KEY_BLOCK)
        scores = scores_of(start)
        top = lax.cond(
            whole(start),
            lambda: jnp.max(scores, axis=1, keepdims=True),
            lambda: jnp.max(
                jnp.where(visible_of(start), scores, NEGATIVE_FILL), axis=1, keepdims=True
            ),
        )
        return jnp.maximum(best, top)

    best = lax.fori_loop(
        first_block, end_block, max_step, jnp.full((rows, 1), NEGATIVE_FILL, jnp.float32)
    )

    def sum_step(block, carry):
        totals, running = carry
        start = pl.multiple_of(block * KEY_BLOCK, KEY_BLOCK)
        scores = scores_of(start)
        weights = lax.cond(
            whole(start),
            lambda: jnp.exp(scores - best),
            lambda: jnp.where(visible_of(start), jnp.exp(scores - best), 0.0),
        )
        totals = totals + jnp.sum(weights, axis=1, keepdims=True)
        values = v_ref[pl.ds(start, KEY_BLOCK), :]
        running = running + jnp.dot(
            weights.astype(jnp.bfloat16), values, preferred_element_type=jnp.float32
        )
        return totals, running

    totals, running = lax.fori_loop(
        first_block,
        end_block,
        sum_step,
        (jnp.zeros((rows, 1), jnp.float32), jnp.zeros((rows, HEAD_SIZE), jnp.float32)),
    )
    o_ref[...] = (running / totals).astype(o_ref.dtype)


def attention(bounds, grouped_queries, key_vals, low, high):
    groups, rows, _ = grouped_queries.shape
    prompt_length = key_vals.shape[0]
    grid_spec = pltpu.PrefetchScalarGridSpec(
        num_scalar_prefetch=1,
        grid=(groups,),
        in_specs=[
            pl.BlockSpec((None, rows, HEAD_SIZE), lambda g, b: (g, 0, 0)),
            pl.BlockSpec((prompt_length, HEAD_SIZE), lambda g, b: (0, g)),
            pl.BlockSpec((prompt_length, HEAD_SIZE), lambda g, b: (0, groups + g)),
            pl.BlockSpec((rows, 1), lambda g, b: (0, 0)),
            pl.BlockSpec((rows, 1), lambda g, b: (0, 0)),
        ],
        out_specs=pl.BlockSpec((None, rows, HEAD_SIZE), lambda g, b: (g, 0, 0)),
    )
    return pl.pallas_call(
        attention_kernel,
        grid_spec=grid_spec,
        out_shape=jax.ShapeDtypeStruct((groups, rows, HEAD_SIZE), jnp.bfloat16),
    )(bounds, grouped_queries, key_vals, key_vals, low, high)


def local(
    tokens,
    segment_ids,
    attention_gain,
    joined_qkv,
    output_proj,
    expert_gain,
    expert_ids,
    gate_weights,
    expert_inner,
    expert_outer,
    cache_pool,
    finished,
    cache_len,
    destination,
):
    tp_count = lax.axis_size("tp")
    where_tp = lax.axis_index("tp")
    replicas = lax.axis_size("req")

    chosen = finished.reshape(-1)
    lengths = cache_len.reshape(-1)
    target = destination.reshape(-1)
    cache_depth = cache_pool.shape[1]
    kv_width = cache_pool.shape[2]
    pieces = cache_pool[chosen]
    positions = where_tp * cache_depth + jnp.arange(cache_depth, dtype=jnp.int32)
    kept_mask = positions[None, :] < lengths[:, None]
    pieces = jnp.where(kept_mask[:, :, None], pieces, jnp.zeros((), jnp.bfloat16))
    outgoing_cache = (
        jnp.zeros((replicas * tp_count, cache_depth, kv_width), jnp.bfloat16).at[target].set(pieces)
    )
    arrived_cache = lax.all_to_all(
        outgoing_cache, ("req", "tp"), split_axis=0, concat_axis=1, tiled=True
    )
    decode_cache = arrived_cache.reshape(replicas, tp_count * cache_depth, kv_width)

    device_rows = tokens.shape[0]
    width = tokens.shape[1]
    seg_local = segment_ids.reshape(device_rows)
    row_span = jnp.arange(device_rows, dtype=jnp.int32)
    token_positions = where_tp * device_rows + row_span
    hidden = rms_gain(tokens, attention_gain)
    joined_everything = jnp.dot(hidden, joined_qkv, preferred_element_type=jnp.float32)
    query_span_width = QUERY_HEADS * HEAD_SIZE
    key_span_width = KEY_VALUE_HEADS * HEAD_SIZE
    float_places = token_positions.astype(jnp.float32)
    query_rows = apply_rotary(
        joined_everything[:, :query_span_width].reshape(device_rows, QUERY_HEADS, HEAD_SIZE),
        float_places,
    ).astype(jnp.bfloat16)
    key_row_list = apply_rotary(
        joined_everything[:, query_span_width : query_span_width + key_span_width].reshape(
            device_rows, KEY_VALUE_HEADS, HEAD_SIZE
        ),
        float_places,
    ).astype(jnp.bfloat16)
    value_rows = joined_everything[:, query_span_width + key_span_width :].astype(jnp.bfloat16)
    key_vals = jnp.concatenate(
        [key_row_list.reshape(device_rows, key_span_width), value_rows], axis=1
    )
    reach = -(-(LONGEST_SEGMENT - 1) // device_rows)
    seg_rows = jnp.zeros((16, key_vals.shape[1]), jnp.bfloat16)
    seg_rows = seg_rows.at[0, :device_rows].set(seg_local.astype(jnp.bfloat16))
    block = jnp.concatenate([key_vals, seg_rows], axis=0)
    near = 4

    def shifted(piece, shift):
        pairs = [(i, i + shift) for i in range(tp_count - shift)]
        return lax.ppermute(piece, "tp", pairs)

    bundle = jnp.stack([shifted(block, s) for s in range(near - 1, 0, -1)] + [block])
    top = (reach + 1) // near * near - near
    far = [shifted(block, s)[None] for s in range(reach, top + near - 1, -1)]
    spans = [shifted(bundle, s) for s in range(top, 0, -near)]
    window = jnp.concatenate(far + spans + [bundle], axis=0)
    window_rows = (reach + 1) * device_rows
    kv_window = window[:, :device_rows, :].reshape(window_rows, key_vals.shape[1])
    seg_window = window[:, device_rows, :device_rows].astype(jnp.int32).reshape(window_rows)
    padded_rows = -(-window_rows // KEY_BLOCK) * KEY_BLOCK
    kv_window = jnp.pad(kv_window, ((0, padded_rows - window_rows), (0, 0)))
    base = (where_tp - reach) * device_rows
    window_places = base + jnp.arange(window_rows, dtype=jnp.int32)
    segment_count = 4
    below = jnp.sum(
        (
            (window_places[None, :] >= 0)
            & (seg_window[None, :] < jnp.arange(segment_count, dtype=jnp.int32)[:, None])
        ).astype(jnp.int32),
        axis=1,
    )
    low = jnp.maximum(base, 0) + below[seg_local] - base
    high = token_positions - base
    first_block = jnp.min(low) // KEY_BLOCK
    end_block = jnp.max(high) // KEY_BLOCK + 1
    bounds = jnp.stack([first_block, end_block, jnp.max(low), jnp.min(high)]).astype(jnp.int32)
    heads_per_group = QUERY_HEADS // KEY_VALUE_HEADS
    grouped_queries = (
        query_rows.reshape(device_rows, KEY_VALUE_HEADS, heads_per_group, HEAD_SIZE)
        .transpose(1, 2, 0, 3)
        .reshape(KEY_VALUE_HEADS, heads_per_group * device_rows, HEAD_SIZE)
    )
    grouped_out = attention(
        bounds,
        grouped_queries,
        kv_window,
        jnp.tile(low, heads_per_group).reshape(-1, 1),
        jnp.tile(high, heads_per_group).reshape(-1, 1),
    )
    attended = (
        grouped_out.reshape(KEY_VALUE_HEADS, heads_per_group, device_rows, HEAD_SIZE)
        .transpose(2, 0, 1, 3)
        .reshape(device_rows, query_span_width)
    )
    projected = jnp.dot(attended, output_proj, preferred_element_type=jnp.float32)
    middle = (tokens.astype(jnp.float32) + projected).astype(jnp.bfloat16)
    normed = rms_gain(middle, expert_gain)
    top_count = expert_ids.shape[1]
    held_count = expert_inner.shape[0]
    total_experts = held_count * tp_count
    capacity = 2 * device_rows * top_count // total_experts
    flat_ids = expert_ids.reshape(device_rows * top_count)
    onehot = (flat_ids[:, None] == jnp.arange(total_experts, dtype=jnp.int32)[None, :]).astype(
        jnp.int32
    )
    slot_rank = jnp.sum(jnp.cumsum(onehot, axis=0) * onehot, axis=1) - 1
    column_index = flat_ids * capacity + slot_rank
    token_of = jnp.arange(device_rows * top_count, dtype=jnp.int32) // top_count
    outgoing = (
        jnp.zeros((total_experts * capacity, width), jnp.bfloat16)
        .at[column_index]
        .set(normed[token_of])
    )
    outgoing = outgoing.reshape(tp_count, held_count, capacity, width)
    hidden_width = expert_outer.shape[1]
    inner_out = jnp.einsum(
        "sgcd,gdf->sgcf",
        lax.all_to_all(outgoing, "tp", split_axis=0, concat_axis=0, tiled=True),
        expert_inner,
        preferred_element_type=jnp.float32,
    )
    active = (
        jnp.maximum(inner_out[..., :hidden_width], 0.0) * inner_out[..., hidden_width:]
    ).astype(jnp.bfloat16)
    final_output = jnp.einsum(
        "sgcf,gfd->sgcd", active, expert_outer, preferred_element_type=jnp.float32
    ).astype(jnp.bfloat16)
    returned = lax.all_to_all(final_output, "tp", split_axis=0, concat_axis=0, tiled=True)
    answers = returned.reshape(total_experts * capacity, width)[column_index].reshape(
        device_rows, top_count, width
    )
    mixed = jnp.sum(answers.astype(jnp.float32) * gate_weights[..., None], axis=1)
    layer_out = (middle.astype(jnp.float32) + mixed).astype(jnp.bfloat16)
    return (layer_out, decode_cache)


def solution(mesh):
    placed = (
        P(("req", "tp"), None),
        P("req", "tp"),
        P(),
        P(),
        P(),
        P(),
        P(("req", "tp"), None),
        P(("req", "tp"), None),
        P("tp", None, None),
        P("tp", None, None),
        P("req", "tp", None),
        P("req", None),
        P("req", None),
        P("req", None),
    )
    return jax.shard_map(
        local,
        mesh=mesh,
        in_specs=placed,
        out_specs=(P(("req", "tp"), None), P(("req", "tp"), None, None)),
        check_vma=False,
    )
```

```python
import functools

import jax
import jax.numpy as jnp
from jax import lax
from jax.experimental import pallas as pl
from jax.experimental.pallas import tpu as pltpu
from jax.sharding import PartitionSpec as P

QUERY_HEADS = 12
KEY_VALUE_HEADS = 2
HEAD_SIZE = 128
KEY_BLOCK = 256
LONGEST_SEGMENT = 2048


epsilon = 1e-06
rope_base = 1000000.0
NEGATIVE_FILL = -1e30


def rms_gain(values_in, gain_row):
    as_float = values_in.astype(jnp.float32)
    scale = lax.rsqrt(jnp.mean(as_float * as_float, axis=-1, keepdims=True) + epsilon)
    return (as_float * scale * gain_row).astype(jnp.bfloat16)


def apply_rotary(vectors, token_positions):
    half_dim = vectors.shape[-1] // 2
    frequency = rope_base ** (-jnp.arange(half_dim, dtype=jnp.float32) * 2.0 / vectors.shape[-1])
    angles = token_positions[:, None] * frequency[None, :]
    cosine = jnp.cos(angles)[:, None, :]
    sine_values = jnp.sin(angles)[:, None, :]
    first_half = vectors[..., :half_dim]
    second_half = vectors[..., half_dim:]
    return jnp.concatenate(
        [
            first_half * cosine - second_half * sine_values,
            second_half * cosine + first_half * sine_values,
        ],
        axis=-1,
    )


def attention_kernel(bounds_ref, q_ref, k_ref, v_ref, lo_ref, hi_ref, o_ref):
    first_block = bounds_ref[0]
    end_block = bounds_ref[1]
    top_low = bounds_ref[2]
    bottom_high = bounds_ref[3]
    queries = q_ref[...]
    low = lo_ref[...]
    high = hi_ref[...]
    rows = queries.shape[0]
    scale = HEAD_SIZE ** (-0.5)

    def scores_of(start):
        keys = k_ref[pl.ds(start, KEY_BLOCK), :]
        return (
            lax.dot_general(
                queries, keys, (((1,), (1,)), ((), ())), preferred_element_type=jnp.float32
            )
            * scale
        )

    def visible_of(start):
        places = start + lax.broadcasted_iota(jnp.int32, (1, KEY_BLOCK), 1)
        return (places >= low) & (places <= high)

    def whole(start):
        return (start >= top_low) & (start + KEY_BLOCK - 1 <= bottom_high)

    def max_step(block, best):
        start = pl.multiple_of(block * KEY_BLOCK, KEY_BLOCK)
        scores = scores_of(start)
        top = lax.cond(
            whole(start),
            lambda: jnp.max(scores, axis=1, keepdims=True),
            lambda: jnp.max(
                jnp.where(visible_of(start), scores, NEGATIVE_FILL), axis=1, keepdims=True
            ),
        )
        return jnp.maximum(best, top)

    best = lax.fori_loop(
        first_block, end_block, max_step, jnp.full((rows, 1), NEGATIVE_FILL, jnp.float32)
    )

    def sum_step(block, carry):
        totals, running = carry
        start = pl.multiple_of(block * KEY_BLOCK, KEY_BLOCK)
        scores = scores_of(start)
        weights = lax.cond(
            whole(start),
            lambda: jnp.exp(scores - best),
            lambda: jnp.where(visible_of(start), jnp.exp(scores - best), 0.0),
        )
        totals = totals + jnp.sum(weights, axis=1, keepdims=True)
        values = v_ref[pl.ds(start, KEY_BLOCK), :]
        running = running + jnp.dot(
            weights.astype(jnp.bfloat16), values, preferred_element_type=jnp.float32
        )
        return totals, running

    totals, running = lax.fori_loop(
        first_block,
        end_block,
        sum_step,
        (jnp.zeros((rows, 1), jnp.float32), jnp.zeros((rows, HEAD_SIZE), jnp.float32)),
    )
    o_ref[...] = (running / totals).astype(o_ref.dtype)


def attention(bounds, grouped_queries, key_vals, low, high):
    groups, rows, _ = grouped_queries.shape
    prompt_length = key_vals.shape[0]
    grid_spec = pltpu.PrefetchScalarGridSpec(
        num_scalar_prefetch=1,
        grid=(groups,),
        in_specs=[
            pl.BlockSpec((None, rows, HEAD_SIZE), lambda g, b: (g, 0, 0)),
            pl.BlockSpec((prompt_length, HEAD_SIZE), lambda g, b: (0, g)),
            pl.BlockSpec((prompt_length, HEAD_SIZE), lambda g, b: (0, groups + g)),
            pl.BlockSpec((rows, 1), lambda g, b: (0, 0)),
            pl.BlockSpec((rows, 1), lambda g, b: (0, 0)),
        ],
        out_specs=pl.BlockSpec((None, rows, HEAD_SIZE), lambda g, b: (g, 0, 0)),
    )
    return pl.pallas_call(
        attention_kernel,
        grid_spec=grid_spec,
        out_shape=jax.ShapeDtypeStruct((groups, rows, HEAD_SIZE), jnp.bfloat16),
    )(bounds, grouped_queries, key_vals, key_vals, low, high)


def local(
    tokens,
    segment_ids,
    attention_gain,
    joined_qkv,
    output_proj,
    expert_gain,
    expert_ids,
    gate_weights,
    expert_inner,
    expert_outer,
    cache_pool,
    finished,
    cache_len,
    destination,
):
    tp_count = lax.axis_size("tp")
    where_tp = lax.axis_index("tp")
    replicas = lax.axis_size("req")

    chosen = finished.reshape(-1)
    lengths = cache_len.reshape(-1)
    target = destination.reshape(-1)
    cache_depth = cache_pool.shape[1]
    kv_width = cache_pool.shape[2]
    pieces = cache_pool[chosen]
    positions = where_tp * cache_depth + jnp.arange(cache_depth, dtype=jnp.int32)
    kept_mask = positions[None, :] < lengths[:, None]
    pieces = jnp.where(kept_mask[:, :, None], pieces, jnp.zeros((), jnp.bfloat16))
    outgoing_cache = (
        jnp.zeros((replicas * tp_count, cache_depth, kv_width), jnp.bfloat16).at[target].set(pieces)
    )
    arrived_cache = lax.all_to_all(
        outgoing_cache, ("req", "tp"), split_axis=0, concat_axis=1, tiled=True
    )
    decode_cache = arrived_cache.reshape(replicas, tp_count * cache_depth, kv_width)

    device_rows = tokens.shape[0]
    width = tokens.shape[1]
    seg_local = segment_ids.reshape(device_rows)
    row_span = jnp.arange(device_rows, dtype=jnp.int32)
    token_positions = where_tp * device_rows + row_span
    hidden = rms_gain(tokens, attention_gain)
    joined_everything = jnp.dot(hidden, joined_qkv, preferred_element_type=jnp.float32)
    query_span_width = QUERY_HEADS * HEAD_SIZE
    key_span_width = KEY_VALUE_HEADS * HEAD_SIZE
    float_places = token_positions.astype(jnp.float32)
    query_rows = apply_rotary(
        joined_everything[:, :query_span_width].reshape(device_rows, QUERY_HEADS, HEAD_SIZE),
        float_places,
    ).astype(jnp.bfloat16)
    key_row_list = apply_rotary(
        joined_everything[:, query_span_width : query_span_width + key_span_width].reshape(
            device_rows, KEY_VALUE_HEADS, HEAD_SIZE
        ),
        float_places,
    ).astype(jnp.bfloat16)
    value_rows = joined_everything[:, query_span_width + key_span_width :].astype(jnp.bfloat16)
    key_vals = jnp.concatenate(
        [key_row_list.reshape(device_rows, key_span_width), value_rows], axis=1
    )
    reach = -(-(LONGEST_SEGMENT - 1) // device_rows)
    seg_rows = jnp.zeros((16, key_vals.shape[1]), jnp.bfloat16)
    seg_rows = seg_rows.at[0, :device_rows].set(seg_local.astype(jnp.bfloat16))
    block = jnp.concatenate([key_vals, seg_rows], axis=0)
    near = 4

    def shifted(piece, shift):
        pairs = [(i, i + shift) for i in range(tp_count - shift)]
        return lax.ppermute(piece, "tp", pairs)

    bundle = jnp.stack([shifted(block, s) for s in range(near - 1, 0, -1)] + [block])
    top = (reach + 1) // near * near - near
    far = [shifted(block, s)[None] for s in range(reach, top + near - 1, -1)]
    spans = [shifted(bundle, s) for s in range(top, 0, -near)]
    window = jnp.concatenate(far + spans + [bundle], axis=0)
    window_rows = (reach + 1) * device_rows
    kv_window = window[:, :device_rows, :].reshape(window_rows, key_vals.shape[1])
    seg_window = window[:, device_rows, :device_rows].astype(jnp.int32).reshape(window_rows)
    padded_rows = -(-window_rows // KEY_BLOCK) * KEY_BLOCK
    kv_window = jnp.pad(kv_window, ((0, padded_rows - window_rows), (0, 0)))
    base = (where_tp - reach) * device_rows
    window_places = base + jnp.arange(window_rows, dtype=jnp.int32)
    segment_count = 4
    below = jnp.sum(
        (
            (window_places[None, :] >= 0)
            & (seg_window[None, :] < jnp.arange(segment_count, dtype=jnp.int32)[:, None])
        ).astype(jnp.int32),
        axis=1,
    )
    low = jnp.maximum(base, 0) + below[seg_local] - base
    high = token_positions - base
    first_block = jnp.min(low) // KEY_BLOCK
    end_block = jnp.max(high) // KEY_BLOCK + 1
    bounds = jnp.stack([first_block, end_block, jnp.max(low), jnp.min(high)]).astype(jnp.int32)
    heads_per_group = QUERY_HEADS // KEY_VALUE_HEADS
    grouped_queries = (
        query_rows.reshape(device_rows, KEY_VALUE_HEADS, heads_per_group, HEAD_SIZE)
        .transpose(1, 2, 0, 3)
        .reshape(KEY_VALUE_HEADS, heads_per_group * device_rows, HEAD_SIZE)
    )
    grouped_out = attention(
        bounds,
        grouped_queries,
        kv_window,
        jnp.tile(low, heads_per_group).reshape(-1, 1),
        jnp.tile(high, heads_per_group).reshape(-1, 1),
    )
    attended = (
        grouped_out.reshape(KEY_VALUE_HEADS, heads_per_group, device_rows, HEAD_SIZE)
        .transpose(2, 0, 1, 3)
        .reshape(device_rows, query_span_width)
    )
    projected = jnp.dot(attended, output_proj, preferred_element_type=jnp.float32)
    middle = (tokens.astype(jnp.float32) + projected).astype(jnp.bfloat16)
    normed = rms_gain(middle, expert_gain)
    decode_cache, normed = lax.optimization_barrier((decode_cache, normed))
    top_count = expert_ids.shape[1]
    held_count = expert_inner.shape[0]
    total_experts = held_count * tp_count
    capacity = 2 * device_rows * top_count // total_experts
    slots = total_experts * capacity
    pair_count = device_rows * top_count
    flat_ids = expert_ids.reshape(pair_count)
    onehot = (flat_ids[:, None] == jnp.arange(total_experts, dtype=jnp.int32)[None, :]).astype(
        jnp.bfloat16
    )
    pair_span = jnp.arange(pair_count, dtype=jnp.int32)
    earlier = (pair_span[None, :] <= pair_span[:, None]).astype(jnp.bfloat16)
    running_count = jnp.dot(earlier, onehot, preferred_element_type=jnp.float32)
    slot_rank = jnp.sum(running_count * onehot.astype(jnp.float32), axis=1).astype(jnp.int32) - 1
    column_index = flat_ids * capacity + slot_rank
    slot_span = jnp.arange(slots, dtype=jnp.int32)
    pick = (column_index[:, None] == slot_span[None, :]).astype(jnp.bfloat16)
    place = jnp.sum(pick.reshape(device_rows, top_count, slots), axis=1)
    outgoing = jnp.dot(place.T, normed, preferred_element_type=jnp.float32).astype(jnp.bfloat16)
    outgoing = outgoing.reshape(tp_count, held_count, capacity, width)
    hidden_width = expert_outer.shape[1]
    inner_out = jnp.einsum(
        "sgcd,gdf->sgcf",
        lax.all_to_all(outgoing, "tp", split_axis=0, concat_axis=0, tiled=True),
        expert_inner,
        preferred_element_type=jnp.float32,
    )
    active = (
        jnp.maximum(inner_out[..., :hidden_width], 0.0) * inner_out[..., hidden_width:]
    ).astype(jnp.bfloat16)
    final_output = jnp.einsum(
        "sgcf,gfd->sgcd", active, expert_outer, preferred_element_type=jnp.float32
    ).astype(jnp.bfloat16)
    returned = lax.all_to_all(final_output, "tp", split_axis=0, concat_axis=0, tiled=True)
    answers = jnp.dot(
        pick, returned.reshape(slots, width), preferred_element_type=jnp.float32
    ).reshape(device_rows, top_count, width)
    mixed = jnp.sum(answers * gate_weights[..., None], axis=1)
    layer_out = (middle.astype(jnp.float32) + mixed).astype(jnp.bfloat16)
    return (layer_out, decode_cache)


def solution(mesh):
    placed = (
        P(("req", "tp"), None),
        P("req", "tp"),
        P(),
        P(),
        P(),
        P(),
        P(("req", "tp"), None),
        P(("req", "tp"), None),
        P("tp", None, None),
        P("tp", None, None),
        P("req", "tp", None),
        P("req", None),
        P("req", None),
        P("req", None),
    )
    return jax.shard_map(
        local,
        mesh=mesh,
        in_specs=placed,
        out_specs=(P(("req", "tp"), None), P(("req", "tp"), None, None)),
        check_vma=False,
    )
```

```python
import functools

import jax
import jax.numpy as jnp
from jax import lax
from jax.experimental import pallas as pl
from jax.experimental.pallas import tpu as pltpu
from jax.sharding import PartitionSpec as P

QUERY_HEADS = 12
KEY_VALUE_HEADS = 2
HEAD_SIZE = 128
KEY_BLOCK = 256
LONGEST_SEGMENT = 2048


epsilon = 1e-06
rope_base = 1000000.0
NEGATIVE_FILL = -1e30


def rms_gain(values_in, gain_row):
    as_float = values_in.astype(jnp.float32)
    scale = lax.rsqrt(jnp.mean(as_float * as_float, axis=-1, keepdims=True) + epsilon)
    return (as_float * scale * gain_row).astype(jnp.bfloat16)


def apply_rotary(vectors, token_positions):
    half_dim = vectors.shape[-1] // 2
    frequency = rope_base ** (-jnp.arange(half_dim, dtype=jnp.float32) * 2.0 / vectors.shape[-1])
    angles = token_positions[:, None] * frequency[None, :]
    cosine = jnp.cos(angles)[:, None, :]
    sine_values = jnp.sin(angles)[:, None, :]
    first_half = vectors[..., :half_dim]
    second_half = vectors[..., half_dim:]
    return jnp.concatenate(
        [
            first_half * cosine - second_half * sine_values,
            second_half * cosine + first_half * sine_values,
        ],
        axis=-1,
    )


def attention_kernel(bounds_ref, q_ref, k_ref, v_ref, lo_ref, hi_ref, o_ref):
    first_block = bounds_ref[0]
    end_block = bounds_ref[1]
    top_low = bounds_ref[2]
    bottom_high = bounds_ref[3]
    queries = q_ref[...]
    low = lo_ref[...]
    high = hi_ref[...]
    rows = queries.shape[0]
    scale = HEAD_SIZE ** (-0.5)

    def scores_of(start):
        keys = k_ref[pl.ds(start, KEY_BLOCK), :]
        return (
            lax.dot_general(
                queries, keys, (((1,), (1,)), ((), ())), preferred_element_type=jnp.float32
            )
            * scale
        )

    def visible_of(start):
        places = start + lax.broadcasted_iota(jnp.int32, (1, KEY_BLOCK), 1)
        return (places >= low) & (places <= high)

    def whole(start):
        return (start >= top_low) & (start + KEY_BLOCK - 1 <= bottom_high)

    def max_step(block, best):
        start = pl.multiple_of(block * KEY_BLOCK, KEY_BLOCK)
        scores = scores_of(start)
        top = lax.cond(
            whole(start),
            lambda: jnp.max(scores, axis=1, keepdims=True),
            lambda: jnp.max(
                jnp.where(visible_of(start), scores, NEGATIVE_FILL), axis=1, keepdims=True
            ),
        )
        return jnp.maximum(best, top)

    best = lax.fori_loop(
        first_block, end_block, max_step, jnp.full((rows, 1), NEGATIVE_FILL, jnp.float32)
    )

    def sum_step(block, carry):
        totals, running = carry
        start = pl.multiple_of(block * KEY_BLOCK, KEY_BLOCK)
        scores = scores_of(start)
        weights = lax.cond(
            whole(start),
            lambda: jnp.exp(scores - best),
            lambda: jnp.where(visible_of(start), jnp.exp(scores - best), 0.0),
        )
        totals = totals + jnp.sum(weights, axis=1, keepdims=True)
        values = v_ref[pl.ds(start, KEY_BLOCK), :]
        running = running + jnp.dot(
            weights.astype(jnp.bfloat16), values, preferred_element_type=jnp.float32
        )
        return totals, running

    totals, running = lax.fori_loop(
        first_block,
        end_block,
        sum_step,
        (jnp.zeros((rows, 1), jnp.float32), jnp.zeros((rows, HEAD_SIZE), jnp.float32)),
    )
    o_ref[...] = (running / totals).astype(o_ref.dtype)


def attention(bounds, grouped_queries, key_vals, low, high):
    groups, rows, _ = grouped_queries.shape
    prompt_length = key_vals.shape[0]
    grid_spec = pltpu.PrefetchScalarGridSpec(
        num_scalar_prefetch=1,
        grid=(groups,),
        in_specs=[
            pl.BlockSpec((None, rows, HEAD_SIZE), lambda g, b: (g, 0, 0)),
            pl.BlockSpec((prompt_length, HEAD_SIZE), lambda g, b: (0, g)),
            pl.BlockSpec((prompt_length, HEAD_SIZE), lambda g, b: (0, groups + g)),
            pl.BlockSpec((rows, 1), lambda g, b: (0, 0)),
            pl.BlockSpec((rows, 1), lambda g, b: (0, 0)),
        ],
        out_specs=pl.BlockSpec((None, rows, HEAD_SIZE), lambda g, b: (g, 0, 0)),
    )
    return pl.pallas_call(
        attention_kernel,
        grid_spec=grid_spec,
        out_shape=jax.ShapeDtypeStruct((groups, rows, HEAD_SIZE), jnp.bfloat16),
    )(bounds, grouped_queries, key_vals, key_vals, low, high)


def local(
    tokens,
    segment_ids,
    attention_gain,
    joined_qkv,
    output_proj,
    expert_gain,
    expert_ids,
    gate_weights,
    expert_inner,
    expert_outer,
    cache_pool,
    finished,
    cache_len,
    destination,
):
    tp_count = lax.axis_size("tp")
    where_tp = lax.axis_index("tp")
    replicas = lax.axis_size("req")

    chosen = finished.reshape(-1)
    lengths = cache_len.reshape(-1)
    target = destination.reshape(-1)
    cache_depth = cache_pool.shape[1]
    kv_width = cache_pool.shape[2]
    pieces = cache_pool[chosen]
    positions = where_tp * cache_depth + jnp.arange(cache_depth, dtype=jnp.int32)
    kept_mask = positions[None, :] < lengths[:, None]
    pieces = jnp.where(kept_mask[:, :, None], pieces, jnp.zeros((), jnp.bfloat16))
    outgoing_cache = (
        jnp.zeros((replicas * tp_count, cache_depth, kv_width), jnp.bfloat16).at[target].set(pieces)
    )
    arrived_cache = lax.all_to_all(
        outgoing_cache, ("req", "tp"), split_axis=0, concat_axis=1, tiled=True
    )
    decode_cache = arrived_cache.reshape(replicas, tp_count * cache_depth, kv_width)

    device_rows = tokens.shape[0]
    width = tokens.shape[1]
    seg_local = segment_ids.reshape(device_rows)
    row_span = jnp.arange(device_rows, dtype=jnp.int32)
    token_positions = where_tp * device_rows + row_span
    hidden = rms_gain(tokens, attention_gain)
    joined_everything = jnp.dot(hidden, joined_qkv, preferred_element_type=jnp.float32)
    query_span_width = QUERY_HEADS * HEAD_SIZE
    key_span_width = KEY_VALUE_HEADS * HEAD_SIZE
    float_places = token_positions.astype(jnp.float32)
    query_rows = apply_rotary(
        joined_everything[:, :query_span_width].reshape(device_rows, QUERY_HEADS, HEAD_SIZE),
        float_places,
    ).astype(jnp.bfloat16)
    key_row_list = apply_rotary(
        joined_everything[:, query_span_width : query_span_width + key_span_width].reshape(
            device_rows, KEY_VALUE_HEADS, HEAD_SIZE
        ),
        float_places,
    ).astype(jnp.bfloat16)
    value_rows = joined_everything[:, query_span_width + key_span_width :].astype(jnp.bfloat16)
    key_vals = jnp.concatenate(
        [key_row_list.reshape(device_rows, key_span_width), value_rows], axis=1
    )
    seg_rows = jnp.zeros((16, key_vals.shape[1]), jnp.bfloat16)
    seg_rows = seg_rows.at[0, :device_rows].set(seg_local.astype(jnp.bfloat16))
    block = jnp.concatenate([key_vals, seg_rows], axis=0)
    copies = jnp.broadcast_to(block[None], (tp_count,) + block.shape)
    gathered = lax.all_to_all(copies, "tp", split_axis=0, concat_axis=0, tiled=True)
    prompt_length = tp_count * device_rows
    kv_window = gathered[:, :device_rows, :].reshape(prompt_length, key_vals.shape[1])
    seg_all = gathered[:, device_rows, :device_rows].astype(jnp.int32).reshape(prompt_length)
    segment_count = 4
    below = jnp.sum(
        (seg_all[None, :] < jnp.arange(segment_count, dtype=jnp.int32)[:, None]).astype(jnp.int32),
        axis=1,
    )
    low = below[seg_local]
    high = token_positions
    first_block = jnp.min(low) // KEY_BLOCK
    end_block = jnp.max(high) // KEY_BLOCK + 1
    bounds = jnp.stack([first_block, end_block, jnp.max(low), jnp.min(high)]).astype(jnp.int32)
    heads_per_group = QUERY_HEADS // KEY_VALUE_HEADS
    grouped_queries = (
        query_rows.reshape(device_rows, KEY_VALUE_HEADS, heads_per_group, HEAD_SIZE)
        .transpose(1, 2, 0, 3)
        .reshape(KEY_VALUE_HEADS, heads_per_group * device_rows, HEAD_SIZE)
    )
    grouped_out = attention(
        bounds,
        grouped_queries,
        kv_window,
        jnp.tile(low, heads_per_group).reshape(-1, 1),
        jnp.tile(high, heads_per_group).reshape(-1, 1),
    )
    attended = (
        grouped_out.reshape(KEY_VALUE_HEADS, heads_per_group, device_rows, HEAD_SIZE)
        .transpose(2, 0, 1, 3)
        .reshape(device_rows, query_span_width)
    )
    projected = jnp.dot(attended, output_proj, preferred_element_type=jnp.float32)
    middle = (tokens.astype(jnp.float32) + projected).astype(jnp.bfloat16)
    normed = rms_gain(middle, expert_gain)
    decode_cache, normed = lax.optimization_barrier((decode_cache, normed))
    top_count = expert_ids.shape[1]
    held_count = expert_inner.shape[0]
    total_experts = held_count * tp_count
    capacity = 2 * device_rows * top_count // total_experts
    slots = total_experts * capacity
    pair_count = device_rows * top_count
    flat_ids = expert_ids.reshape(pair_count)
    onehot = (flat_ids[:, None] == jnp.arange(total_experts, dtype=jnp.int32)[None, :]).astype(
        jnp.bfloat16
    )
    pair_span = jnp.arange(pair_count, dtype=jnp.int32)
    earlier = (pair_span[None, :] <= pair_span[:, None]).astype(jnp.bfloat16)
    running_count = jnp.dot(earlier, onehot, preferred_element_type=jnp.float32)
    slot_rank = jnp.sum(running_count * onehot.astype(jnp.float32), axis=1).astype(jnp.int32) - 1
    column_index = flat_ids * capacity + slot_rank
    slot_span = jnp.arange(slots, dtype=jnp.int32)
    pick = (column_index[:, None] == slot_span[None, :]).astype(jnp.bfloat16)
    place = jnp.sum(pick.reshape(device_rows, top_count, slots), axis=1)
    outgoing = jnp.dot(place.T, normed, preferred_element_type=jnp.float32).astype(jnp.bfloat16)
    outgoing = outgoing.reshape(tp_count, held_count, capacity, width)
    hidden_width = expert_outer.shape[1]
    inner_out = jnp.einsum(
        "sgcd,gdf->sgcf",
        lax.all_to_all(outgoing, "tp", split_axis=0, concat_axis=0, tiled=True),
        expert_inner,
        preferred_element_type=jnp.float32,
    )
    active = (
        jnp.maximum(inner_out[..., :hidden_width], 0.0) * inner_out[..., hidden_width:]
    ).astype(jnp.bfloat16)
    final_output = jnp.einsum(
        "sgcf,gfd->sgcd", active, expert_outer, preferred_element_type=jnp.float32
    ).astype(jnp.bfloat16)
    returned = lax.all_to_all(final_output, "tp", split_axis=0, concat_axis=0, tiled=True)
    answers = jnp.dot(
        pick, returned.reshape(slots, width), preferred_element_type=jnp.float32
    ).reshape(device_rows, top_count, width)
    mixed = jnp.sum(answers * gate_weights[..., None], axis=1)
    layer_out = (middle.astype(jnp.float32) + mixed).astype(jnp.bfloat16)
    return (layer_out, decode_cache)


def solution(mesh):
    placed = (
        P(("req", "tp"), None),
        P("req", "tp"),
        P(),
        P(),
        P(),
        P(),
        P(("req", "tp"), None),
        P(("req", "tp"), None),
        P("tp", None, None),
        P("tp", None, None),
        P("req", "tp", None),
        P("req", None),
        P("req", None),
        P("req", None),
    )
    return jax.shard_map(
        local,
        mesh=mesh,
        in_specs=placed,
        out_specs=(P(("req", "tp"), None), P(("req", "tp"), None, None)),
        check_vma=False,
    )
```

```python
import functools

import jax
import jax.numpy as jnp
from jax import lax
from jax.experimental import pallas as pl
from jax.experimental.pallas import tpu as pltpu
from jax.sharding import PartitionSpec as P

QUERY_HEADS = 12
KEY_VALUE_HEADS = 2
HEAD_SIZE = 128
KEY_BLOCK = 256
LONGEST_SEGMENT = 2048


epsilon = 1e-06
rope_base = 1000000.0
NEGATIVE_FILL = -1e30


def rms_gain(values_in, gain_row):
    as_float = values_in.astype(jnp.float32)
    scale = lax.rsqrt(jnp.mean(as_float * as_float, axis=-1, keepdims=True) + epsilon)
    return (as_float * scale * gain_row).astype(jnp.bfloat16)


def apply_rotary(vectors, token_positions):
    half_dim = vectors.shape[-1] // 2
    frequency = rope_base ** (-jnp.arange(half_dim, dtype=jnp.float32) * 2.0 / vectors.shape[-1])
    angles = token_positions[:, None] * frequency[None, :]
    cosine = jnp.cos(angles)[:, None, :]
    sine_values = jnp.sin(angles)[:, None, :]
    first_half = vectors[..., :half_dim]
    second_half = vectors[..., half_dim:]
    return jnp.concatenate(
        [
            first_half * cosine - second_half * sine_values,
            second_half * cosine + first_half * sine_values,
        ],
        axis=-1,
    )


def attention_kernel(bounds_ref, q_ref, k_ref, v_ref, lo_ref, hi_ref, o_ref):
    first_block = bounds_ref[0]
    end_block = bounds_ref[1]
    top_low = bounds_ref[2]
    bottom_high = bounds_ref[3]
    queries = q_ref[...]
    low = lo_ref[...]
    high = hi_ref[...]
    rows = queries.shape[0]
    scale = HEAD_SIZE ** (-0.5)

    def scores_of(start):
        keys = k_ref[pl.ds(start, KEY_BLOCK), :]
        return (
            lax.dot_general(
                queries, keys, (((1,), (1,)), ((), ())), preferred_element_type=jnp.float32
            )
            * scale
        )

    def visible_of(start):
        places = start + lax.broadcasted_iota(jnp.int32, (1, KEY_BLOCK), 1)
        return (places >= low) & (places <= high)

    def whole(start):
        return (start >= top_low) & (start + KEY_BLOCK - 1 <= bottom_high)

    def max_step(block, best):
        start = pl.multiple_of(block * KEY_BLOCK, KEY_BLOCK)
        scores = scores_of(start)
        top = lax.cond(
            whole(start),
            lambda: jnp.max(scores, axis=1, keepdims=True),
            lambda: jnp.max(
                jnp.where(visible_of(start), scores, NEGATIVE_FILL), axis=1, keepdims=True
            ),
        )
        return jnp.maximum(best, top)

    best = lax.fori_loop(
        first_block, end_block, max_step, jnp.full((rows, 1), NEGATIVE_FILL, jnp.float32)
    )

    def sum_step(block, carry):
        totals, running = carry
        start = pl.multiple_of(block * KEY_BLOCK, KEY_BLOCK)
        scores = scores_of(start)
        weights = lax.cond(
            whole(start),
            lambda: jnp.exp(scores - best),
            lambda: jnp.where(visible_of(start), jnp.exp(scores - best), 0.0),
        )
        totals = totals + jnp.sum(weights, axis=1, keepdims=True)
        values = v_ref[pl.ds(start, KEY_BLOCK), :]
        running = running + jnp.dot(
            weights.astype(jnp.bfloat16), values, preferred_element_type=jnp.float32
        )
        return totals, running

    totals, running = lax.fori_loop(
        first_block,
        end_block,
        sum_step,
        (jnp.zeros((rows, 1), jnp.float32), jnp.zeros((rows, HEAD_SIZE), jnp.float32)),
    )
    o_ref[...] = (running / totals).astype(o_ref.dtype)


def attention(bounds, grouped_queries, key_vals, low, high):
    groups, rows, _ = grouped_queries.shape
    prompt_length = key_vals.shape[0]
    grid_spec = pltpu.PrefetchScalarGridSpec(
        num_scalar_prefetch=1,
        grid=(groups,),
        in_specs=[
            pl.BlockSpec((None, rows, HEAD_SIZE), lambda g, b: (g, 0, 0)),
            pl.BlockSpec((prompt_length, HEAD_SIZE), lambda g, b: (0, g)),
            pl.BlockSpec((prompt_length, HEAD_SIZE), lambda g, b: (0, groups + g)),
            pl.BlockSpec((rows, 1), lambda g, b: (0, 0)),
            pl.BlockSpec((rows, 1), lambda g, b: (0, 0)),
        ],
        out_specs=pl.BlockSpec((None, rows, HEAD_SIZE), lambda g, b: (g, 0, 0)),
    )
    return pl.pallas_call(
        attention_kernel,
        grid_spec=grid_spec,
        out_shape=jax.ShapeDtypeStruct((groups, rows, HEAD_SIZE), jnp.bfloat16),
    )(bounds, grouped_queries, key_vals, key_vals, low, high)


def local(
    tokens,
    segment_ids,
    attention_gain,
    joined_qkv,
    output_proj,
    expert_gain,
    expert_ids,
    gate_weights,
    expert_inner,
    expert_outer,
    cache_pool,
    finished,
    cache_len,
    destination,
):
    tp_count = lax.axis_size("tp")
    where_tp = lax.axis_index("tp")
    replicas = lax.axis_size("req")

    chosen = finished.reshape(-1)
    lengths = cache_len.reshape(-1)
    target = destination.reshape(-1)
    cache_depth = cache_pool.shape[1]
    kv_width = cache_pool.shape[2]
    pieces = cache_pool[chosen]
    positions = where_tp * cache_depth + jnp.arange(cache_depth, dtype=jnp.int32)
    kept_mask = positions[None, :] < lengths[:, None]
    pieces = jnp.where(kept_mask[:, :, None], pieces, jnp.zeros((), jnp.bfloat16))
    outgoing_cache = (
        jnp.zeros((replicas * tp_count, cache_depth, kv_width), jnp.bfloat16).at[target].set(pieces)
    )
    arrived_cache = lax.all_to_all(
        outgoing_cache, ("req", "tp"), split_axis=0, concat_axis=1, tiled=True
    )
    decode_cache = arrived_cache.reshape(replicas, tp_count * cache_depth, kv_width)

    device_rows = tokens.shape[0]
    width = tokens.shape[1]
    seg_local = segment_ids.reshape(device_rows)
    row_span = jnp.arange(device_rows, dtype=jnp.int32)
    token_positions = where_tp * device_rows + row_span
    hidden = rms_gain(tokens, attention_gain)
    joined_everything = jnp.dot(hidden, joined_qkv, preferred_element_type=jnp.float32)
    query_span_width = QUERY_HEADS * HEAD_SIZE
    key_span_width = KEY_VALUE_HEADS * HEAD_SIZE
    float_places = token_positions.astype(jnp.float32)
    query_rows = apply_rotary(
        joined_everything[:, :query_span_width].reshape(device_rows, QUERY_HEADS, HEAD_SIZE),
        float_places,
    ).astype(jnp.bfloat16)
    key_row_list = apply_rotary(
        joined_everything[:, query_span_width : query_span_width + key_span_width].reshape(
            device_rows, KEY_VALUE_HEADS, HEAD_SIZE
        ),
        float_places,
    ).astype(jnp.bfloat16)
    value_rows = joined_everything[:, query_span_width + key_span_width :].astype(jnp.bfloat16)
    key_vals = jnp.concatenate(
        [key_row_list.reshape(device_rows, key_span_width), value_rows], axis=1
    )
    copies = jnp.broadcast_to(key_vals[None], (tp_count,) + key_vals.shape)
    gathered = lax.all_to_all(copies, "tp", split_axis=0, concat_axis=0, tiled=True)
    prompt_length = tp_count * device_rows
    kv_window = gathered.reshape(prompt_length, key_vals.shape[1])
    seg_copies = jnp.broadcast_to(seg_local[None, None], (tp_count, 1, device_rows))
    seg_all = lax.all_to_all(seg_copies, "tp", split_axis=0, concat_axis=0, tiled=True)
    seg_all = seg_all.reshape(prompt_length)
    segment_count = 4
    below = jnp.sum(
        (seg_all[None, :] < jnp.arange(segment_count, dtype=jnp.int32)[:, None]).astype(jnp.int32),
        axis=1,
    )
    low = below[seg_local]
    high = token_positions
    first_block = jnp.min(low) // KEY_BLOCK
    end_block = jnp.max(high) // KEY_BLOCK + 1
    bounds = jnp.stack([first_block, end_block, jnp.max(low), jnp.min(high)]).astype(jnp.int32)
    heads_per_group = QUERY_HEADS // KEY_VALUE_HEADS
    grouped_queries = (
        query_rows.reshape(device_rows, KEY_VALUE_HEADS, heads_per_group, HEAD_SIZE)
        .transpose(1, 2, 0, 3)
        .reshape(KEY_VALUE_HEADS, heads_per_group * device_rows, HEAD_SIZE)
    )
    grouped_out = attention(
        bounds,
        grouped_queries,
        kv_window,
        jnp.tile(low, heads_per_group).reshape(-1, 1),
        jnp.tile(high, heads_per_group).reshape(-1, 1),
    )
    attended = (
        grouped_out.reshape(KEY_VALUE_HEADS, heads_per_group, device_rows, HEAD_SIZE)
        .transpose(2, 0, 1, 3)
        .reshape(device_rows, query_span_width)
    )
    projected = jnp.dot(attended, output_proj, preferred_element_type=jnp.float32)
    middle = (tokens.astype(jnp.float32) + projected).astype(jnp.bfloat16)
    normed = rms_gain(middle, expert_gain)
    decode_cache, normed = lax.optimization_barrier((decode_cache, normed))
    top_count = expert_ids.shape[1]
    held_count = expert_inner.shape[0]
    total_experts = held_count * tp_count
    capacity = 2 * device_rows * top_count // total_experts
    slots = total_experts * capacity
    pair_count = device_rows * top_count
    flat_ids = expert_ids.reshape(pair_count)
    onehot = (flat_ids[:, None] == jnp.arange(total_experts, dtype=jnp.int32)[None, :]).astype(
        jnp.bfloat16
    )
    pair_span = jnp.arange(pair_count, dtype=jnp.int32)
    earlier = (pair_span[None, :] <= pair_span[:, None]).astype(jnp.bfloat16)
    running_count = jnp.dot(earlier, onehot, preferred_element_type=jnp.float32)
    slot_rank = jnp.sum(running_count * onehot.astype(jnp.float32), axis=1).astype(jnp.int32) - 1
    column_index = flat_ids * capacity + slot_rank
    slot_span = jnp.arange(slots, dtype=jnp.int32)
    pick = (column_index[:, None] == slot_span[None, :]).astype(jnp.bfloat16)
    place = jnp.sum(pick.reshape(device_rows, top_count, slots), axis=1)
    outgoing = jnp.dot(place.T, normed, preferred_element_type=jnp.float32).astype(jnp.bfloat16)
    outgoing = outgoing.reshape(tp_count, held_count, capacity, width)
    hidden_width = expert_outer.shape[1]
    inner_out = jnp.einsum(
        "sgcd,gdf->sgcf",
        lax.all_to_all(outgoing, "tp", split_axis=0, concat_axis=0, tiled=True),
        expert_inner,
        preferred_element_type=jnp.float32,
    )
    active = (
        jnp.maximum(inner_out[..., :hidden_width], 0.0) * inner_out[..., hidden_width:]
    ).astype(jnp.bfloat16)
    final_output = jnp.einsum(
        "sgcf,gfd->sgcd", active, expert_outer, preferred_element_type=jnp.float32
    ).astype(jnp.bfloat16)
    returned = lax.all_to_all(final_output, "tp", split_axis=0, concat_axis=0, tiled=True)
    answers = jnp.dot(
        pick, returned.reshape(slots, width), preferred_element_type=jnp.float32
    ).reshape(device_rows, top_count, width)
    mixed = jnp.sum(answers * gate_weights[..., None], axis=1)
    layer_out = (middle.astype(jnp.float32) + mixed).astype(jnp.bfloat16)
    return (layer_out, decode_cache)


def solution(mesh):
    placed = (
        P(("req", "tp"), None),
        P("req", "tp"),
        P(),
        P(),
        P(),
        P(),
        P(("req", "tp"), None),
        P(("req", "tp"), None),
        P("tp", None, None),
        P("tp", None, None),
        P("req", "tp", None),
        P("req", None),
        P("req", None),
        P("req", None),
    )
    return jax.shard_map(
        local,
        mesh=mesh,
        in_specs=placed,
        out_specs=(P(("req", "tp"), None), P(("req", "tp"), None, None)),
        check_vma=False,
    )
```

```python
import functools

import jax
import jax.numpy as jnp
from jax import lax
from jax.experimental import pallas as pl
from jax.experimental.pallas import tpu as pltpu
from jax.sharding import PartitionSpec as P

QUERY_HEADS = 12
KEY_VALUE_HEADS = 2
HEAD_SIZE = 128
KEY_BLOCK = 512
SEG_ROWS = 16
LONGEST_SEGMENT = 2048


epsilon = 1e-06
rope_base = 1000000.0
NEGATIVE_FILL = -1e30


def rms_gain(values_in, gain_row):
    as_float = values_in.astype(jnp.float32)
    scale = lax.rsqrt(jnp.mean(as_float * as_float, axis=-1, keepdims=True) + epsilon)
    return (as_float * scale * gain_row).astype(jnp.bfloat16)


def apply_rotary(vectors, token_positions):
    half_dim = vectors.shape[-1] // 2
    frequency = rope_base ** (-jnp.arange(half_dim, dtype=jnp.float32) * 2.0 / vectors.shape[-1])
    angles = token_positions[:, None] * frequency[None, :]
    cosine = jnp.cos(angles)[:, None, :]
    sine_values = jnp.sin(angles)[:, None, :]
    first_half = vectors[..., :half_dim]
    second_half = vectors[..., half_dim:]
    return jnp.concatenate(
        [
            first_half * cosine - second_half * sine_values,
            second_half * cosine + first_half * sine_values,
        ],
        axis=-1,
    )


def attention_kernel(bounds_ref, q_ref, k_ref, v_ref, lo_ref, hi_ref, o_ref):
    ranges = (
        (bounds_ref[0], bounds_ref[1], True),
        (bounds_ref[1], bounds_ref[2], False),
        (bounds_ref[2], bounds_ref[3], True),
    )
    queries = q_ref[...]
    low = lo_ref[...]
    high = hi_ref[...]
    rows = queries.shape[0]
    chunk = k_ref.shape[1] - SEG_ROWS
    per_block = KEY_BLOCK // chunk
    scale = HEAD_SIZE ** (-0.5)

    def block_of(ref, block):
        part = ref[pl.ds(block * per_block, per_block), pl.ds(0, chunk), :]
        return part.reshape(KEY_BLOCK, HEAD_SIZE)

    def raw_scores(block):
        return lax.dot_general(
            queries, block_of(k_ref, block), (((1,), (1,)), ((), ())),
            preferred_element_type=jnp.float32,
        )

    def visible_of(block):
        places = block * KEY_BLOCK + lax.broadcasted_iota(jnp.int32, (1, KEY_BLOCK), 1)
        return (places >= low) & (places <= high)

    best = jnp.full((rows, 1), NEGATIVE_FILL, jnp.float32)
    for first, end, masked in ranges:

        def max_step(block, best, masked=masked):
            scores = raw_scores(block)
            if masked:
                scores = jnp.where(visible_of(block), scores, NEGATIVE_FILL)
            return jnp.maximum(best, jnp.max(scores, axis=1, keepdims=True))

        best = lax.fori_loop(first, end, max_step, best)
    best = best * scale
    carry = (jnp.zeros((rows, 1), jnp.float32), jnp.zeros((rows, HEAD_SIZE), jnp.float32))
    for first, end, masked in ranges:

        def sum_step(block, carry, masked=masked):
            totals, running = carry
            weights = jnp.exp(raw_scores(block) * scale - best)
            if masked:
                weights = jnp.where(visible_of(block), weights, 0.0)
            totals = totals + jnp.sum(weights, axis=1, keepdims=True)
            running = running + jnp.dot(
                weights.astype(jnp.bfloat16), block_of(v_ref, block),
                preferred_element_type=jnp.float32,
            )
            return totals, running

        carry = lax.fori_loop(first, end, sum_step, carry)
    totals, running = carry
    o_ref[...] = (running / totals).astype(o_ref.dtype)


def attention(bounds, grouped_queries, gathered, low, high):
    groups, rows, _ = grouped_queries.shape
    sources, block_rows, _ = gathered.shape
    grid_spec = pltpu.PrefetchScalarGridSpec(
        num_scalar_prefetch=1,
        grid=(groups,),
        in_specs=[
            pl.BlockSpec((None, rows, HEAD_SIZE), lambda g, b: (g, 0, 0)),
            pl.BlockSpec((sources, block_rows, HEAD_SIZE), lambda g, b: (0, 0, g)),
            pl.BlockSpec((sources, block_rows, HEAD_SIZE), lambda g, b: (0, 0, groups + g)),
            pl.BlockSpec((rows, 1), lambda g, b: (0, 0)),
            pl.BlockSpec((rows, 1), lambda g, b: (0, 0)),
        ],
        out_specs=pl.BlockSpec((None, rows, HEAD_SIZE), lambda g, b: (g, 0, 0)),
    )
    return pl.pallas_call(
        attention_kernel,
        grid_spec=grid_spec,
        out_shape=jax.ShapeDtypeStruct((groups, rows, HEAD_SIZE), jnp.bfloat16),
    )(bounds, grouped_queries, gathered, gathered, low, high)


def local(
    tokens,
    segment_ids,
    attention_gain,
    joined_qkv,
    output_proj,
    expert_gain,
    expert_ids,
    gate_weights,
    expert_inner,
    expert_outer,
    cache_pool,
    finished,
    cache_len,
    destination,
):
    tp_count = lax.axis_size("tp")
    where_tp = lax.axis_index("tp")
    replicas = lax.axis_size("req")

    chosen = finished.reshape(-1)
    lengths = cache_len.reshape(-1)
    target = destination.reshape(-1)
    cache_depth = cache_pool.shape[1]
    kv_width = cache_pool.shape[2]
    pieces = cache_pool[chosen]
    positions = where_tp * cache_depth + jnp.arange(cache_depth, dtype=jnp.int32)
    kept_mask = positions[None, :] < lengths[:, None]
    pieces = jnp.where(kept_mask[:, :, None], pieces, jnp.zeros((), jnp.bfloat16))
    outgoing_cache = (
        jnp.zeros((replicas * tp_count, cache_depth, kv_width), jnp.bfloat16).at[target].set(pieces)
    )
    arrived_cache = lax.all_to_all(
        outgoing_cache, ("req", "tp"), split_axis=0, concat_axis=1, tiled=True
    )
    decode_cache = arrived_cache.reshape(replicas, tp_count * cache_depth, kv_width)

    device_rows = tokens.shape[0]
    width = tokens.shape[1]
    seg_local = segment_ids.reshape(device_rows)
    row_span = jnp.arange(device_rows, dtype=jnp.int32)
    token_positions = where_tp * device_rows + row_span
    hidden = rms_gain(tokens, attention_gain)
    joined_everything = jnp.dot(hidden, joined_qkv, preferred_element_type=jnp.float32)
    query_span_width = QUERY_HEADS * HEAD_SIZE
    key_span_width = KEY_VALUE_HEADS * HEAD_SIZE
    float_places = token_positions.astype(jnp.float32)
    query_rows = apply_rotary(
        joined_everything[:, :query_span_width].reshape(device_rows, QUERY_HEADS, HEAD_SIZE),
        float_places,
    ).astype(jnp.bfloat16)
    key_row_list = apply_rotary(
        joined_everything[:, query_span_width : query_span_width + key_span_width].reshape(
            device_rows, KEY_VALUE_HEADS, HEAD_SIZE
        ),
        float_places,
    ).astype(jnp.bfloat16)
    value_rows = joined_everything[:, query_span_width + key_span_width :].astype(jnp.bfloat16)
    key_vals = jnp.concatenate(
        [key_row_list.reshape(device_rows, key_span_width), value_rows], axis=1
    )
    seg_rows = jnp.zeros((SEG_ROWS, key_vals.shape[1]), jnp.bfloat16)
    seg_rows = seg_rows.at[0, :device_rows].set(seg_local.astype(jnp.bfloat16))
    block = jnp.concatenate([key_vals, seg_rows], axis=0)
    copies = jnp.broadcast_to(block[None], (tp_count,) + block.shape)
    gathered = lax.all_to_all(copies, "tp", split_axis=0, concat_axis=0, tiled=True)
    prompt_length = tp_count * device_rows
    seg_all = gathered[:, device_rows, :device_rows].astype(jnp.int32).reshape(prompt_length)
    segment_count = 4
    below = jnp.sum(
        (seg_all[None, :] < jnp.arange(segment_count, dtype=jnp.int32)[:, None]).astype(jnp.int32),
        axis=1,
    )
    low = below[seg_local]
    high = token_positions
    first_block = jnp.min(low) // KEY_BLOCK
    end_block = jnp.max(high) // KEY_BLOCK + 1
    whole_first = jnp.clip(-(-jnp.max(low) // KEY_BLOCK), first_block, end_block)
    whole_end = jnp.clip((jnp.min(high) + 1) // KEY_BLOCK, whole_first, end_block)
    bounds = jnp.stack([first_block, whole_first, whole_end, end_block]).astype(jnp.int32)
    heads_per_group = QUERY_HEADS // KEY_VALUE_HEADS
    grouped_queries = (
        query_rows.reshape(device_rows, KEY_VALUE_HEADS, heads_per_group, HEAD_SIZE)
        .transpose(1, 2, 0, 3)
        .reshape(KEY_VALUE_HEADS, heads_per_group * device_rows, HEAD_SIZE)
    )
    grouped_out = attention(
        bounds,
        grouped_queries,
        gathered,
        jnp.tile(low, heads_per_group).reshape(-1, 1),
        jnp.tile(high, heads_per_group).reshape(-1, 1),
    )
    attended = (
        grouped_out.reshape(KEY_VALUE_HEADS, heads_per_group, device_rows, HEAD_SIZE)
        .transpose(2, 0, 1, 3)
        .reshape(device_rows, query_span_width)
    )
    projected = jnp.dot(attended, output_proj, preferred_element_type=jnp.float32)
    middle = (tokens.astype(jnp.float32) + projected).astype(jnp.bfloat16)
    normed = rms_gain(middle, expert_gain)
    decode_cache, normed = lax.optimization_barrier((decode_cache, normed))
    top_count = expert_ids.shape[1]
    held_count = expert_inner.shape[0]
    total_experts = held_count * tp_count
    capacity = 2 * device_rows * top_count // total_experts
    slots = total_experts * capacity
    pair_count = device_rows * top_count
    flat_ids = expert_ids.reshape(pair_count)
    onehot = (flat_ids[:, None] == jnp.arange(total_experts, dtype=jnp.int32)[None, :]).astype(
        jnp.bfloat16
    )
    pair_span = jnp.arange(pair_count, dtype=jnp.int32)
    earlier = (pair_span[None, :] <= pair_span[:, None]).astype(jnp.bfloat16)
    running_count = jnp.dot(earlier, onehot, preferred_element_type=jnp.float32)
    slot_rank = jnp.sum(running_count * onehot.astype(jnp.float32), axis=1).astype(jnp.int32) - 1
    column_index = flat_ids * capacity + slot_rank
    slot_span = jnp.arange(slots, dtype=jnp.int32)
    pick = (column_index[:, None] == slot_span[None, :]).astype(jnp.bfloat16)
    place = jnp.sum(pick.reshape(device_rows, top_count, slots), axis=1)
    outgoing = jnp.dot(place.T, normed, preferred_element_type=jnp.float32).astype(jnp.bfloat16)
    outgoing = outgoing.reshape(tp_count, held_count, capacity, width)
    hidden_width = expert_outer.shape[1]
    inner_out = jnp.einsum(
        "sgcd,gdf->sgcf",
        lax.all_to_all(outgoing, "tp", split_axis=0, concat_axis=0, tiled=True),
        expert_inner,
        preferred_element_type=jnp.float32,
    )
    active = (
        jnp.maximum(inner_out[..., :hidden_width], 0.0) * inner_out[..., hidden_width:]
    ).astype(jnp.bfloat16)
    final_output = jnp.einsum(
        "sgcf,gfd->sgcd", active, expert_outer, preferred_element_type=jnp.float32
    ).astype(jnp.bfloat16)
    returned = lax.all_to_all(final_output, "tp", split_axis=0, concat_axis=0, tiled=True)
    answers = jnp.dot(
        pick, returned.reshape(slots, width), preferred_element_type=jnp.float32
    ).reshape(device_rows, top_count, width)
    mixed = jnp.sum(answers * gate_weights[..., None], axis=1)
    layer_out = (middle.astype(jnp.float32) + mixed).astype(jnp.bfloat16)
    return (layer_out, decode_cache)


def solution(mesh):
    placed = (
        P(("req", "tp"), None),
        P("req", "tp"),
        P(),
        P(),
        P(),
        P(),
        P(("req", "tp"), None),
        P(("req", "tp"), None),
        P("tp", None, None),
        P("tp", None, None),
        P("req", "tp", None),
        P("req", None),
        P("req", None),
        P("req", None),
    )
    return jax.shard_map(
        local,
        mesh=mesh,
        in_specs=placed,
        out_specs=(P(("req", "tp"), None), P(("req", "tp"), None, None)),
        check_vma=False,
    )
```

```python
import functools

import jax
import jax.numpy as jnp
from jax import lax
from jax.experimental import pallas as pl
from jax.experimental.pallas import tpu as pltpu
from jax.sharding import Mesh, PartitionSpec as P

QUERY_HEADS = 12
KEY_VALUE_HEADS = 2
HEAD_SIZE = 128
KEY_BLOCK = 512
SEG_ROWS = 16
PLANE = 8
TP = ("z", "yx")
LONGEST_SEGMENT = 2048


epsilon = 1e-06
rope_base = 1000000.0
NEGATIVE_FILL = -1e30


def rms_gain(values_in, gain_row):
    as_float = values_in.astype(jnp.float32)
    scale = lax.rsqrt(jnp.mean(as_float * as_float, axis=-1, keepdims=True) + epsilon)
    return (as_float * scale * gain_row).astype(jnp.bfloat16)


def apply_rotary(vectors, token_positions):
    half_dim = vectors.shape[-1] // 2
    frequency = rope_base ** (-jnp.arange(half_dim, dtype=jnp.float32) * 2.0 / vectors.shape[-1])
    angles = token_positions[:, None] * frequency[None, :]
    cosine = jnp.cos(angles)[:, None, :]
    sine_values = jnp.sin(angles)[:, None, :]
    first_half = vectors[..., :half_dim]
    second_half = vectors[..., half_dim:]
    return jnp.concatenate(
        [
            first_half * cosine - second_half * sine_values,
            second_half * cosine + first_half * sine_values,
        ],
        axis=-1,
    )


def attention_kernel(bounds_ref, q_ref, k_ref, v_ref, lo_ref, hi_ref, o_ref):
    ranges = (
        (bounds_ref[0], bounds_ref[1], True),
        (bounds_ref[1], bounds_ref[2], False),
        (bounds_ref[2], bounds_ref[3], True),
    )
    queries = q_ref[...]
    low = lo_ref[...]
    high = hi_ref[...]
    rows = queries.shape[0]
    chunk = k_ref.shape[1] - SEG_ROWS
    per_block = KEY_BLOCK // chunk
    scale = HEAD_SIZE ** (-0.5)

    def block_of(ref, block):
        part = ref[pl.ds(block * per_block, per_block), pl.ds(0, chunk), :]
        return part.reshape(KEY_BLOCK, HEAD_SIZE)

    def raw_scores(block):
        return lax.dot_general(
            queries, block_of(k_ref, block), (((1,), (1,)), ((), ())),
            preferred_element_type=jnp.float32,
        )

    def visible_of(block):
        places = block * KEY_BLOCK + lax.broadcasted_iota(jnp.int32, (1, KEY_BLOCK), 1)
        return (places >= low) & (places <= high)

    best = jnp.full((rows, 1), NEGATIVE_FILL, jnp.float32)
    for first, end, masked in ranges:

        def max_step(block, best, masked=masked):
            scores = raw_scores(block)
            if masked:
                scores = jnp.where(visible_of(block), scores, NEGATIVE_FILL)
            return jnp.maximum(best, jnp.max(scores, axis=1, keepdims=True))

        best = lax.fori_loop(first, end, max_step, best)
    best = best * scale
    carry = (jnp.zeros((rows, 1), jnp.float32), jnp.zeros((rows, HEAD_SIZE), jnp.float32))
    for first, end, masked in ranges:

        def sum_step(block, carry, masked=masked):
            totals, running = carry
            weights = jnp.exp(raw_scores(block) * scale - best)
            if masked:
                weights = jnp.where(visible_of(block), weights, 0.0)
            totals = totals + jnp.sum(weights, axis=1, keepdims=True)
            running = running + jnp.dot(
                weights.astype(jnp.bfloat16), block_of(v_ref, block),
                preferred_element_type=jnp.float32,
            )
            return totals, running

        carry = lax.fori_loop(first, end, sum_step, carry)
    totals, running = carry
    o_ref[...] = (running / totals).astype(o_ref.dtype)


def attention(bounds, grouped_queries, gathered, low, high):
    groups, rows, _ = grouped_queries.shape
    sources, block_rows, _ = gathered.shape
    grid_spec = pltpu.PrefetchScalarGridSpec(
        num_scalar_prefetch=1,
        grid=(groups,),
        in_specs=[
            pl.BlockSpec((None, rows, HEAD_SIZE), lambda g, b: (g, 0, 0)),
            pl.BlockSpec((sources, block_rows, HEAD_SIZE), lambda g, b: (0, 0, g)),
            pl.BlockSpec((sources, block_rows, HEAD_SIZE), lambda g, b: (0, 0, groups + g)),
            pl.BlockSpec((rows, 1), lambda g, b: (0, 0)),
            pl.BlockSpec((rows, 1), lambda g, b: (0, 0)),
        ],
        out_specs=pl.BlockSpec((None, rows, HEAD_SIZE), lambda g, b: (g, 0, 0)),
    )
    return pl.pallas_call(
        attention_kernel,
        grid_spec=grid_spec,
        out_shape=jax.ShapeDtypeStruct((groups, rows, HEAD_SIZE), jnp.bfloat16),
    )(bounds, grouped_queries, gathered, gathered, low, high)


def local(
    tokens,
    segment_ids,
    attention_gain,
    joined_qkv,
    output_proj,
    expert_gain,
    expert_ids,
    gate_weights,
    expert_inner,
    expert_outer,
    cache_pool,
    finished,
    cache_len,
    destination,
):
    plane = lax.axis_size("yx")
    planes = lax.axis_size("z")
    where_z = lax.axis_index("z")
    tp_count = planes * plane
    where_tp = where_z * plane + lax.axis_index("yx")
    replicas = lax.axis_size("req")

    chosen = finished.reshape(-1)
    lengths = cache_len.reshape(-1)
    target = destination.reshape(-1)
    cache_depth = cache_pool.shape[1]
    kv_width = cache_pool.shape[2]
    pieces = cache_pool[chosen]
    positions = where_tp * cache_depth + jnp.arange(cache_depth, dtype=jnp.int32)
    kept_mask = positions[None, :] < lengths[:, None]
    pieces = jnp.where(kept_mask[:, :, None], pieces, jnp.zeros((), jnp.bfloat16))
    outgoing_cache = (
        jnp.zeros((replicas * tp_count, cache_depth, kv_width), jnp.bfloat16).at[target].set(pieces)
    )
    device_rows = tokens.shape[0]
    width = tokens.shape[1]
    seg_local = segment_ids.reshape(device_rows)
    row_span = jnp.arange(device_rows, dtype=jnp.int32)
    token_positions = where_tp * device_rows + row_span
    hidden = rms_gain(tokens, attention_gain)
    joined_everything = jnp.dot(hidden, joined_qkv, preferred_element_type=jnp.float32)
    query_span_width = QUERY_HEADS * HEAD_SIZE
    key_span_width = KEY_VALUE_HEADS * HEAD_SIZE
    float_places = token_positions.astype(jnp.float32)
    query_rows = apply_rotary(
        joined_everything[:, :query_span_width].reshape(device_rows, QUERY_HEADS, HEAD_SIZE),
        float_places,
    ).astype(jnp.bfloat16)
    key_row_list = apply_rotary(
        joined_everything[:, query_span_width : query_span_width + key_span_width].reshape(
            device_rows, KEY_VALUE_HEADS, HEAD_SIZE
        ),
        float_places,
    ).astype(jnp.bfloat16)
    value_rows = joined_everything[:, query_span_width + key_span_width :].astype(jnp.bfloat16)
    key_vals = jnp.concatenate(
        [key_row_list.reshape(device_rows, key_span_width), value_rows], axis=1
    )
    seg_rows = jnp.zeros((SEG_ROWS, key_vals.shape[1]), jnp.bfloat16)
    seg_rows = seg_rows.at[0, :device_rows].set(seg_local.astype(jnp.bfloat16))
    block = jnp.concatenate([key_vals, seg_rows], axis=0)
    reach = -(-(LONGEST_SEGMENT - 1) // device_rows)
    reach_planes = -(-reach // plane)
    copies = jnp.broadcast_to(block[None], (plane,) + block.shape)
    in_plane = lax.all_to_all(copies, "yx", split_axis=0, concat_axis=0, tiled=True)
    received = []
    for shift in range(reach_planes, 0, -1):
        pairs = [(i, i + shift) for i in range(planes - shift)]
        received.append(lax.ppermute(in_plane, "z", pairs))
    gathered = jnp.concatenate(received + [in_plane], axis=0)
    outgoing_cache, gathered = lax.optimization_barrier((outgoing_cache, gathered))
    arrived_cache = lax.all_to_all(
        outgoing_cache, ("req",) + TP, split_axis=0, concat_axis=1, tiled=True
    )
    decode_cache = arrived_cache.reshape(replicas, tp_count * cache_depth, kv_width)

    window_rows = gathered.shape[0] * device_rows
    seg_window = gathered[:, device_rows, :device_rows].astype(jnp.int32).reshape(window_rows)
    base = (where_z - reach_planes) * plane * device_rows
    window_places = base + jnp.arange(window_rows, dtype=jnp.int32)
    segment_count = 4
    below = jnp.sum(
        (
            (window_places[None, :] >= 0)
            & (seg_window[None, :] < jnp.arange(segment_count, dtype=jnp.int32)[:, None])
        ).astype(jnp.int32),
        axis=1,
    )
    low = jnp.maximum(base, 0) + below[seg_local] - base
    high = token_positions - base
    first_block = jnp.min(low) // KEY_BLOCK
    end_block = jnp.max(high) // KEY_BLOCK + 1
    whole_first = jnp.clip(-(-jnp.max(low) // KEY_BLOCK), first_block, end_block)
    whole_end = jnp.clip((jnp.min(high) + 1) // KEY_BLOCK, whole_first, end_block)
    bounds = jnp.stack([first_block, whole_first, whole_end, end_block]).astype(jnp.int32)
    heads_per_group = QUERY_HEADS // KEY_VALUE_HEADS
    grouped_queries = (
        query_rows.reshape(device_rows, KEY_VALUE_HEADS, heads_per_group, HEAD_SIZE)
        .transpose(1, 2, 0, 3)
        .reshape(KEY_VALUE_HEADS, heads_per_group * device_rows, HEAD_SIZE)
    )
    grouped_out = attention(
        bounds,
        grouped_queries,
        gathered,
        jnp.tile(low, heads_per_group).reshape(-1, 1),
        jnp.tile(high, heads_per_group).reshape(-1, 1),
    )
    attended = (
        grouped_out.reshape(KEY_VALUE_HEADS, heads_per_group, device_rows, HEAD_SIZE)
        .transpose(2, 0, 1, 3)
        .reshape(device_rows, query_span_width)
    )
    projected = jnp.dot(attended, output_proj, preferred_element_type=jnp.float32)
    middle = (tokens.astype(jnp.float32) + projected).astype(jnp.bfloat16)
    normed = rms_gain(middle, expert_gain)
    decode_cache, normed = lax.optimization_barrier((decode_cache, normed))
    top_count = expert_ids.shape[1]
    held_count = expert_inner.shape[0]
    total_experts = held_count * tp_count
    capacity = 2 * device_rows * top_count // total_experts
    slots = total_experts * capacity
    pair_count = device_rows * top_count
    flat_ids = expert_ids.reshape(pair_count)
    onehot = (flat_ids[:, None] == jnp.arange(total_experts, dtype=jnp.int32)[None, :]).astype(
        jnp.bfloat16
    )
    pair_span = jnp.arange(pair_count, dtype=jnp.int32)
    earlier = (pair_span[None, :] <= pair_span[:, None]).astype(jnp.bfloat16)
    running_count = jnp.dot(earlier, onehot, preferred_element_type=jnp.float32)
    slot_rank = jnp.sum(running_count * onehot.astype(jnp.float32), axis=1).astype(jnp.int32) - 1
    column_index = flat_ids * capacity + slot_rank
    slot_span = jnp.arange(slots, dtype=jnp.int32)
    pick = (column_index[:, None] == slot_span[None, :]).astype(jnp.bfloat16)
    place = jnp.sum(pick.reshape(device_rows, top_count, slots), axis=1)
    outgoing = jnp.dot(place.T, normed, preferred_element_type=jnp.float32).astype(jnp.bfloat16)
    outgoing = outgoing.reshape(tp_count, held_count, capacity, width)
    hidden_width = expert_outer.shape[1]
    inner_out = jnp.einsum(
        "sgcd,gdf->sgcf",
        lax.all_to_all(outgoing, TP, split_axis=0, concat_axis=0, tiled=True),
        expert_inner,
        preferred_element_type=jnp.float32,
    )
    active = (
        jnp.maximum(inner_out[..., :hidden_width], 0.0) * inner_out[..., hidden_width:]
    ).astype(jnp.bfloat16)
    final_output = jnp.einsum(
        "sgcf,gfd->sgcd", active, expert_outer, preferred_element_type=jnp.float32
    ).astype(jnp.bfloat16)
    returned = lax.all_to_all(final_output, TP, split_axis=0, concat_axis=0, tiled=True)
    answers = jnp.dot(
        pick, returned.reshape(slots, width), preferred_element_type=jnp.float32
    ).reshape(device_rows, top_count, width)
    mixed = jnp.sum(answers * gate_weights[..., None], axis=1)
    layer_out = (middle.astype(jnp.float32) + mixed).astype(jnp.bfloat16)
    return (layer_out, decode_cache)


def solution(mesh):
    fine = Mesh(
        mesh.devices.reshape(mesh.devices.shape[0], -1, PLANE), ("req",) + TP
    )
    placed = (
        P(("req",) + TP, None),
        P("req", TP),
        P(),
        P(),
        P(),
        P(),
        P(("req",) + TP, None),
        P(("req",) + TP, None),
        P(TP, None, None),
        P(TP, None, None),
        P("req", TP, None),
        P("req", None),
        P("req", None),
        P("req", None),
    )
    return jax.shard_map(
        local,
        mesh=fine,
        in_specs=placed,
        out_specs=(P(("req",) + TP, None), P(("req",) + TP, None, None)),
        check_vma=False,
    )
```

```python
import functools

import jax
import jax.numpy as jnp
from jax import lax
from jax.experimental import pallas as pl
from jax.experimental.pallas import tpu as pltpu
from jax.sharding import PartitionSpec as P

QUERY_HEADS = 12
KEY_VALUE_HEADS = 2
HEAD_SIZE = 128
KEY_BLOCK = 512
SEG_ROWS = 16
LONGEST_SEGMENT = 2048


epsilon = 1e-06
rope_base = 1000000.0
NEGATIVE_FILL = -1e30


def rms_gain(values_in, gain_row):
    as_float = values_in.astype(jnp.float32)
    scale = lax.rsqrt(jnp.mean(as_float * as_float, axis=-1, keepdims=True) + epsilon)
    return (as_float * scale * gain_row).astype(jnp.bfloat16)


def apply_rotary(vectors, token_positions):
    half_dim = vectors.shape[-1] // 2
    frequency = rope_base ** (-jnp.arange(half_dim, dtype=jnp.float32) * 2.0 / vectors.shape[-1])
    angles = token_positions[:, None] * frequency[None, :]
    cosine = jnp.cos(angles)[:, None, :]
    sine_values = jnp.sin(angles)[:, None, :]
    first_half = vectors[..., :half_dim]
    second_half = vectors[..., half_dim:]
    return jnp.concatenate(
        [
            first_half * cosine - second_half * sine_values,
            second_half * cosine + first_half * sine_values,
        ],
        axis=-1,
    )


def attention_kernel(bounds_ref, q_ref, k_ref, v_ref, lo_ref, hi_ref, o_ref):
    ranges = (
        (bounds_ref[0], bounds_ref[1], True),
        (bounds_ref[1], bounds_ref[2], False),
        (bounds_ref[2], bounds_ref[3], True),
    )
    queries = q_ref[...]
    low = lo_ref[...]
    high = hi_ref[...]
    rows = queries.shape[0]
    chunk = k_ref.shape[1] - SEG_ROWS
    per_block = KEY_BLOCK // chunk
    scale = HEAD_SIZE ** (-0.5)

    def block_of(ref, block):
        part = ref[pl.ds(block * per_block, per_block), pl.ds(0, chunk), :]
        return part.reshape(KEY_BLOCK, HEAD_SIZE)

    def raw_scores(block):
        return lax.dot_general(
            queries, block_of(k_ref, block), (((1,), (1,)), ((), ())),
            preferred_element_type=jnp.float32,
        )

    def visible_of(block):
        places = block * KEY_BLOCK + lax.broadcasted_iota(jnp.int32, (1, KEY_BLOCK), 1)
        return (places >= low) & (places <= high)

    best = jnp.full((rows, 1), NEGATIVE_FILL, jnp.float32)
    for first, end, masked in ranges:

        def max_step(block, best, masked=masked):
            scores = raw_scores(block)
            if masked:
                scores = jnp.where(visible_of(block), scores, NEGATIVE_FILL)
            return jnp.maximum(best, jnp.max(scores, axis=1, keepdims=True))

        best = lax.fori_loop(first, end, max_step, best)
    best = best * scale
    carry = (jnp.zeros((rows, 1), jnp.float32), jnp.zeros((rows, HEAD_SIZE), jnp.float32))
    for first, end, masked in ranges:

        def sum_step(block, carry, masked=masked):
            totals, running = carry
            weights = jnp.exp(raw_scores(block) * scale - best)
            if masked:
                weights = jnp.where(visible_of(block), weights, 0.0)
            totals = totals + jnp.sum(weights, axis=1, keepdims=True)
            running = running + jnp.dot(
                weights.astype(jnp.bfloat16), block_of(v_ref, block),
                preferred_element_type=jnp.float32,
            )
            return totals, running

        carry = lax.fori_loop(first, end, sum_step, carry)
    totals, running = carry
    o_ref[...] = (running / totals).astype(o_ref.dtype)


def attention(bounds, grouped_queries, gathered, low, high):
    groups, rows, _ = grouped_queries.shape
    sources, block_rows, _ = gathered.shape
    grid_spec = pltpu.PrefetchScalarGridSpec(
        num_scalar_prefetch=1,
        grid=(groups,),
        in_specs=[
            pl.BlockSpec((None, rows, HEAD_SIZE), lambda g, b: (g, 0, 0)),
            pl.BlockSpec((sources, block_rows, HEAD_SIZE), lambda g, b: (0, 0, g)),
            pl.BlockSpec((sources, block_rows, HEAD_SIZE), lambda g, b: (0, 0, groups + g)),
            pl.BlockSpec((rows, 1), lambda g, b: (0, 0)),
            pl.BlockSpec((rows, 1), lambda g, b: (0, 0)),
        ],
        out_specs=pl.BlockSpec((None, rows, HEAD_SIZE), lambda g, b: (g, 0, 0)),
    )
    return pl.pallas_call(
        attention_kernel,
        grid_spec=grid_spec,
        out_shape=jax.ShapeDtypeStruct((groups, rows, HEAD_SIZE), jnp.bfloat16),
    )(bounds, grouped_queries, gathered, gathered, low, high)


def local(
    tokens,
    segment_ids,
    attention_gain,
    joined_qkv,
    output_proj,
    expert_gain,
    expert_ids,
    gate_weights,
    expert_inner,
    expert_outer,
    cache_pool,
    finished,
    cache_len,
    destination,
):
    tp_count = lax.axis_size("tp")
    where_tp = lax.axis_index("tp")
    replicas = lax.axis_size("req")

    device_rows = tokens.shape[0]
    width = tokens.shape[1]
    seg_local = segment_ids.reshape(device_rows)
    row_span = jnp.arange(device_rows, dtype=jnp.int32)
    token_positions = where_tp * device_rows + row_span
    hidden = rms_gain(tokens, attention_gain)
    joined_everything = jnp.dot(hidden, joined_qkv, preferred_element_type=jnp.float32)
    query_span_width = QUERY_HEADS * HEAD_SIZE
    key_span_width = KEY_VALUE_HEADS * HEAD_SIZE
    float_places = token_positions.astype(jnp.float32)
    query_rows = apply_rotary(
        joined_everything[:, :query_span_width].reshape(device_rows, QUERY_HEADS, HEAD_SIZE),
        float_places,
    ).astype(jnp.bfloat16)
    key_row_list = apply_rotary(
        joined_everything[:, query_span_width : query_span_width + key_span_width].reshape(
            device_rows, KEY_VALUE_HEADS, HEAD_SIZE
        ),
        float_places,
    ).astype(jnp.bfloat16)
    value_rows = joined_everything[:, query_span_width + key_span_width :].astype(jnp.bfloat16)
    key_vals = jnp.concatenate(
        [key_row_list.reshape(device_rows, key_span_width), value_rows], axis=1
    )
    seg_rows = jnp.zeros((SEG_ROWS, key_vals.shape[1]), jnp.bfloat16)
    seg_rows = seg_rows.at[0, :device_rows].set(seg_local.astype(jnp.bfloat16))
    block = jnp.concatenate([key_vals, seg_rows], axis=0)
    copies = jnp.broadcast_to(block[None], (tp_count,) + block.shape)
    gathered = lax.all_to_all(copies, "tp", split_axis=0, concat_axis=0, tiled=True)
    prompt_length = tp_count * device_rows
    seg_all = gathered[:, device_rows, :device_rows].astype(jnp.int32).reshape(prompt_length)
    segment_count = 4
    below = jnp.sum(
        (seg_all[None, :] < jnp.arange(segment_count, dtype=jnp.int32)[:, None]).astype(jnp.int32),
        axis=1,
    )
    low = below[seg_local]
    high = token_positions
    first_block = jnp.min(low) // KEY_BLOCK
    end_block = jnp.max(high) // KEY_BLOCK + 1
    whole_first = jnp.clip(-(-jnp.max(low) // KEY_BLOCK), first_block, end_block)
    whole_end = jnp.clip((jnp.min(high) + 1) // KEY_BLOCK, whole_first, end_block)
    bounds = jnp.stack([first_block, whole_first, whole_end, end_block]).astype(jnp.int32)
    heads_per_group = QUERY_HEADS // KEY_VALUE_HEADS
    grouped_queries = (
        query_rows.reshape(device_rows, KEY_VALUE_HEADS, heads_per_group, HEAD_SIZE)
        .transpose(1, 2, 0, 3)
        .reshape(KEY_VALUE_HEADS, heads_per_group * device_rows, HEAD_SIZE)
    )
    chosen = finished.reshape(-1)
    lengths = cache_len.reshape(-1)
    target = destination.reshape(-1)
    cache_depth = cache_pool.shape[1]
    kv_width = cache_pool.shape[2]
    pieces = cache_pool[chosen]
    positions = where_tp * cache_depth + jnp.arange(cache_depth, dtype=jnp.int32)
    kept_mask = positions[None, :] < lengths[:, None]
    pieces = jnp.where(kept_mask[:, :, None], pieces, jnp.zeros((), jnp.bfloat16))
    pieces, grouped_queries = lax.optimization_barrier((pieces, grouped_queries))
    outgoing_cache = (
        jnp.zeros((replicas * tp_count, cache_depth, kv_width), jnp.bfloat16).at[target].set(pieces)
    )
    arrived_cache = lax.all_to_all(
        outgoing_cache, ("req", "tp"), split_axis=0, concat_axis=1, tiled=True
    )
    decode_cache = arrived_cache.reshape(replicas, tp_count * cache_depth, kv_width)

    grouped_out = attention(
        bounds,
        grouped_queries,
        gathered,
        jnp.tile(low, heads_per_group).reshape(-1, 1),
        jnp.tile(high, heads_per_group).reshape(-1, 1),
    )
    attended = (
        grouped_out.reshape(KEY_VALUE_HEADS, heads_per_group, device_rows, HEAD_SIZE)
        .transpose(2, 0, 1, 3)
        .reshape(device_rows, query_span_width)
    )
    projected = jnp.dot(attended, output_proj, preferred_element_type=jnp.float32)
    middle = (tokens.astype(jnp.float32) + projected).astype(jnp.bfloat16)
    normed = rms_gain(middle, expert_gain)
    decode_cache, normed = lax.optimization_barrier((decode_cache, normed))
    top_count = expert_ids.shape[1]
    held_count = expert_inner.shape[0]
    total_experts = held_count * tp_count
    capacity = 2 * device_rows * top_count // total_experts
    slots = total_experts * capacity
    pair_count = device_rows * top_count
    flat_ids = expert_ids.reshape(pair_count)
    onehot = (flat_ids[:, None] == jnp.arange(total_experts, dtype=jnp.int32)[None, :]).astype(
        jnp.bfloat16
    )
    pair_span = jnp.arange(pair_count, dtype=jnp.int32)
    earlier = (pair_span[None, :] <= pair_span[:, None]).astype(jnp.bfloat16)
    running_count = jnp.dot(earlier, onehot, preferred_element_type=jnp.float32)
    slot_rank = jnp.sum(running_count * onehot.astype(jnp.float32), axis=1).astype(jnp.int32) - 1
    column_index = flat_ids * capacity + slot_rank
    slot_span = jnp.arange(slots, dtype=jnp.int32)
    pick = (column_index[:, None] == slot_span[None, :]).astype(jnp.bfloat16)
    place = jnp.sum(pick.reshape(device_rows, top_count, slots), axis=1)
    outgoing = jnp.dot(place.T, normed, preferred_element_type=jnp.float32).astype(jnp.bfloat16)
    outgoing = outgoing.reshape(tp_count, held_count, capacity, width)
    hidden_width = expert_outer.shape[1]
    inner_out = jnp.einsum(
        "sgcd,gdf->sgcf",
        lax.all_to_all(outgoing, "tp", split_axis=0, concat_axis=0, tiled=True),
        expert_inner,
        preferred_element_type=jnp.float32,
    )
    active = (
        jnp.maximum(inner_out[..., :hidden_width], 0.0) * inner_out[..., hidden_width:]
    ).astype(jnp.bfloat16)
    final_output = jnp.einsum(
        "sgcf,gfd->sgcd", active, expert_outer, preferred_element_type=jnp.float32
    ).astype(jnp.bfloat16)
    returned = lax.all_to_all(final_output, "tp", split_axis=0, concat_axis=0, tiled=True)
    answers = jnp.dot(
        pick, returned.reshape(slots, width), preferred_element_type=jnp.float32
    ).reshape(device_rows, top_count, width)
    mixed = jnp.sum(answers * gate_weights[..., None], axis=1)
    layer_out = (middle.astype(jnp.float32) + mixed).astype(jnp.bfloat16)
    return (layer_out, decode_cache)


def solution(mesh):
    placed = (
        P(("req", "tp"), None),
        P("req", "tp"),
        P(),
        P(),
        P(),
        P(),
        P(("req", "tp"), None),
        P(("req", "tp"), None),
        P("tp", None, None),
        P("tp", None, None),
        P("req", "tp", None),
        P("req", None),
        P("req", None),
        P("req", None),
    )
    return jax.shard_map(
        local,
        mesh=mesh,
        in_specs=placed,
        out_specs=(P(("req", "tp"), None), P(("req", "tp"), None, None)),
        check_vma=False,
    )
```

```python
import functools

import jax
import jax.numpy as jnp
from jax import lax
from jax.experimental import pallas as pl
from jax.experimental.pallas import tpu as pltpu
from jax.sharding import PartitionSpec as P

QUERY_HEADS = 12
KEY_VALUE_HEADS = 2
HEAD_SIZE = 128
KEY_BLOCK = 512
SEG_ROWS = 16
LONGEST_SEGMENT = 2048


epsilon = 1e-06
rope_base = 1000000.0
NEGATIVE_FILL = -1e30


def rms_gain(values_in, gain_row):
    as_float = values_in.astype(jnp.float32)
    scale = lax.rsqrt(jnp.mean(as_float * as_float, axis=-1, keepdims=True) + epsilon)
    return (as_float * scale * gain_row).astype(jnp.bfloat16)


def apply_rotary(vectors, token_positions):
    half_dim = vectors.shape[-1] // 2
    frequency = rope_base ** (-jnp.arange(half_dim, dtype=jnp.float32) * 2.0 / vectors.shape[-1])
    angles = token_positions[:, None] * frequency[None, :]
    cosine = jnp.cos(angles)[:, None, :]
    sine_values = jnp.sin(angles)[:, None, :]
    first_half = vectors[..., :half_dim]
    second_half = vectors[..., half_dim:]
    return jnp.concatenate(
        [
            first_half * cosine - second_half * sine_values,
            second_half * cosine + first_half * sine_values,
        ],
        axis=-1,
    )


def attention_kernel(bounds_ref, q_ref, k_ref, v_ref, lo_ref, hi_ref, o_ref):
    ranges = (
        (bounds_ref[0], bounds_ref[1], True),
        (bounds_ref[1], bounds_ref[2], False),
        (bounds_ref[2], bounds_ref[3], True),
    )
    queries = q_ref[...]
    low = lo_ref[...]
    high = hi_ref[...]
    rows = queries.shape[0]
    chunk = k_ref.shape[1] - SEG_ROWS
    per_block = KEY_BLOCK // chunk
    scale = HEAD_SIZE ** (-0.5)

    def block_of(ref, block):
        part = ref[pl.ds(block * per_block, per_block), pl.ds(0, chunk), :]
        return part.reshape(KEY_BLOCK, HEAD_SIZE)

    def raw_scores(block):
        return lax.dot_general(
            queries, block_of(k_ref, block), (((1,), (1,)), ((), ())),
            preferred_element_type=jnp.float32,
        )

    def visible_of(block):
        places = block * KEY_BLOCK + lax.broadcasted_iota(jnp.int32, (1, KEY_BLOCK), 1)
        return (places >= low) & (places <= high)

    best = jnp.full((rows, 1), NEGATIVE_FILL, jnp.float32)
    for first, end, masked in ranges:

        def max_step(block, best, masked=masked):
            scores = raw_scores(block)
            if masked:
                scores = jnp.where(visible_of(block), scores, NEGATIVE_FILL)
            return jnp.maximum(best, jnp.max(scores, axis=1, keepdims=True))

        best = lax.fori_loop(first, end, max_step, best)
    best = best * scale
    carry = (jnp.zeros((rows, 1), jnp.float32), jnp.zeros((rows, HEAD_SIZE), jnp.float32))
    for first, end, masked in ranges:

        def sum_step(block, carry, masked=masked):
            totals, running = carry
            weights = jnp.exp(raw_scores(block) * scale - best)
            if masked:
                weights = jnp.where(visible_of(block), weights, 0.0)
            totals = totals + jnp.sum(weights, axis=1, keepdims=True)
            running = running + jnp.dot(
                weights.astype(jnp.bfloat16), block_of(v_ref, block),
                preferred_element_type=jnp.float32,
            )
            return totals, running

        carry = lax.fori_loop(first, end, sum_step, carry)
    totals, running = carry
    o_ref[...] = (running / totals).astype(o_ref.dtype)


def attention(bounds, grouped_queries, gathered, low, high):
    groups, rows, _ = grouped_queries.shape
    sources, block_rows, _ = gathered.shape
    grid_spec = pltpu.PrefetchScalarGridSpec(
        num_scalar_prefetch=1,
        grid=(groups,),
        in_specs=[
            pl.BlockSpec((None, rows, HEAD_SIZE), lambda g, b: (g, 0, 0)),
            pl.BlockSpec((sources, block_rows, HEAD_SIZE), lambda g, b: (0, 0, g)),
            pl.BlockSpec((sources, block_rows, HEAD_SIZE), lambda g, b: (0, 0, groups + g)),
            pl.BlockSpec((rows, 1), lambda g, b: (0, 0)),
            pl.BlockSpec((rows, 1), lambda g, b: (0, 0)),
        ],
        out_specs=pl.BlockSpec((None, rows, HEAD_SIZE), lambda g, b: (g, 0, 0)),
    )
    return pl.pallas_call(
        attention_kernel,
        grid_spec=grid_spec,
        out_shape=jax.ShapeDtypeStruct((groups, rows, HEAD_SIZE), jnp.bfloat16),
    )(bounds, grouped_queries, gathered, gathered, low, high)


def local(
    tokens,
    segment_ids,
    attention_gain,
    joined_qkv,
    output_proj,
    expert_gain,
    expert_ids,
    gate_weights,
    expert_inner,
    expert_outer,
    cache_pool,
    finished,
    cache_len,
    destination,
):
    tp_count = lax.axis_size("tp")
    where_tp = lax.axis_index("tp")
    replicas = lax.axis_size("req")

    device_rows = tokens.shape[0]
    width = tokens.shape[1]
    seg_local = segment_ids.reshape(device_rows)
    row_span = jnp.arange(device_rows, dtype=jnp.int32)
    token_positions = where_tp * device_rows + row_span
    hidden = rms_gain(tokens, attention_gain)
    joined_everything = jnp.dot(hidden, joined_qkv, preferred_element_type=jnp.float32)
    query_span_width = QUERY_HEADS * HEAD_SIZE
    key_span_width = KEY_VALUE_HEADS * HEAD_SIZE
    float_places = token_positions.astype(jnp.float32)
    query_rows = apply_rotary(
        joined_everything[:, :query_span_width].reshape(device_rows, QUERY_HEADS, HEAD_SIZE),
        float_places,
    ).astype(jnp.bfloat16)
    key_row_list = apply_rotary(
        joined_everything[:, query_span_width : query_span_width + key_span_width].reshape(
            device_rows, KEY_VALUE_HEADS, HEAD_SIZE
        ),
        float_places,
    ).astype(jnp.bfloat16)
    value_rows = joined_everything[:, query_span_width + key_span_width :].astype(jnp.bfloat16)
    key_vals = jnp.concatenate(
        [key_row_list.reshape(device_rows, key_span_width), value_rows], axis=1
    )
    seg_rows = jnp.zeros((SEG_ROWS, key_vals.shape[1]), jnp.bfloat16)
    seg_rows = seg_rows.at[0, :device_rows].set(seg_local.astype(jnp.bfloat16))
    block = jnp.concatenate([key_vals, seg_rows], axis=0)
    copies = jnp.broadcast_to(block[None], (tp_count,) + block.shape)
    gathered = lax.all_to_all(copies, "tp", split_axis=0, concat_axis=0, tiled=True)
    prompt_length = tp_count * device_rows
    seg_all = gathered[:, device_rows, :device_rows].astype(jnp.int32).reshape(prompt_length)
    segment_count = 4
    below = jnp.sum(
        (seg_all[None, :] < jnp.arange(segment_count, dtype=jnp.int32)[:, None]).astype(jnp.int32),
        axis=1,
    )
    low = below[seg_local]
    high = token_positions
    lowest = below[jnp.min(seg_local)]
    highest_low = below[jnp.max(seg_local)]
    first_place = where_tp * device_rows
    first_block = lowest // KEY_BLOCK
    end_block = (first_place + device_rows - 1) // KEY_BLOCK + 1
    whole_first = jnp.clip(-(-highest_low // KEY_BLOCK), first_block, end_block)
    whole_end = jnp.clip((first_place + 1) // KEY_BLOCK, whole_first, end_block)
    bounds = jnp.stack([first_block, whole_first, whole_end, end_block]).astype(jnp.int32)
    heads_per_group = QUERY_HEADS // KEY_VALUE_HEADS
    grouped_queries = (
        query_rows.reshape(device_rows, KEY_VALUE_HEADS, heads_per_group, HEAD_SIZE)
        .transpose(1, 2, 0, 3)
        .reshape(KEY_VALUE_HEADS, heads_per_group * device_rows, HEAD_SIZE)
    )
    chosen = finished.reshape(-1)
    lengths = cache_len.reshape(-1)
    target = destination.reshape(-1)
    cache_depth = cache_pool.shape[1]
    kv_width = cache_pool.shape[2]
    pieces = cache_pool[chosen]
    positions = where_tp * cache_depth + jnp.arange(cache_depth, dtype=jnp.int32)
    kept_mask = positions[None, :] < lengths[:, None]
    pieces = jnp.where(kept_mask[:, :, None], pieces, jnp.zeros((), jnp.bfloat16))
    pieces, grouped_queries, gathered = lax.optimization_barrier(
        (pieces, grouped_queries, gathered)
    )
    outgoing_cache = (
        jnp.zeros((replicas * tp_count, cache_depth, kv_width), jnp.bfloat16).at[target].set(pieces)
    )
    arrived_cache = lax.all_to_all(
        outgoing_cache, ("req", "tp"), split_axis=0, concat_axis=1, tiled=True
    )
    decode_cache = arrived_cache.reshape(replicas, tp_count * cache_depth, kv_width)
    decode_cache = jnp.where(jnp.min(lengths) > 0, decode_cache, jnp.zeros((), jnp.bfloat16))

    grouped_out = attention(
        bounds,
        grouped_queries,
        gathered,
        jnp.tile(low, heads_per_group).reshape(-1, 1),
        jnp.tile(high, heads_per_group).reshape(-1, 1),
    )
    attended = (
        grouped_out.reshape(KEY_VALUE_HEADS, heads_per_group, device_rows, HEAD_SIZE)
        .transpose(2, 0, 1, 3)
        .reshape(device_rows, query_span_width)
    )
    projected = jnp.dot(attended, output_proj, preferred_element_type=jnp.float32)
    middle = (tokens.astype(jnp.float32) + projected).astype(jnp.bfloat16)
    normed = rms_gain(middle, expert_gain)
    decode_cache, normed = lax.optimization_barrier((decode_cache, normed))
    top_count = expert_ids.shape[1]
    held_count = expert_inner.shape[0]
    total_experts = held_count * tp_count
    capacity = 2 * device_rows * top_count // total_experts
    slots = total_experts * capacity
    pair_count = device_rows * top_count
    flat_ids = expert_ids.reshape(pair_count)
    onehot = (flat_ids[:, None] == jnp.arange(total_experts, dtype=jnp.int32)[None, :]).astype(
        jnp.bfloat16
    )
    pair_span = jnp.arange(pair_count, dtype=jnp.int32)
    earlier = (pair_span[None, :] <= pair_span[:, None]).astype(jnp.bfloat16)
    running_count = jnp.dot(earlier, onehot, preferred_element_type=jnp.float32)
    slot_rank = jnp.sum(running_count * onehot.astype(jnp.float32), axis=1).astype(jnp.int32) - 1
    column_index = flat_ids * capacity + slot_rank
    slot_span = jnp.arange(slots, dtype=jnp.int32)
    pick = (column_index[:, None] == slot_span[None, :]).astype(jnp.bfloat16)
    place = jnp.sum(pick.reshape(device_rows, top_count, slots), axis=1)
    outgoing = jnp.dot(place.T, normed, preferred_element_type=jnp.float32).astype(jnp.bfloat16)
    outgoing = outgoing.reshape(tp_count, held_count, capacity, width)
    hidden_width = expert_outer.shape[1]
    inner_out = jnp.einsum(
        "sgcd,gdf->sgcf",
        lax.all_to_all(outgoing, "tp", split_axis=0, concat_axis=0, tiled=True),
        expert_inner,
        preferred_element_type=jnp.float32,
    )
    active = (
        jnp.maximum(inner_out[..., :hidden_width], 0.0) * inner_out[..., hidden_width:]
    ).astype(jnp.bfloat16)
    final_output = jnp.einsum(
        "sgcf,gfd->sgcd", active, expert_outer, preferred_element_type=jnp.float32
    ).astype(jnp.bfloat16)
    returned = lax.all_to_all(final_output, "tp", split_axis=0, concat_axis=0, tiled=True)
    answers = jnp.dot(
        pick, returned.reshape(slots, width), preferred_element_type=jnp.float32
    ).reshape(device_rows, top_count, width)
    mixed = jnp.sum(answers * gate_weights[..., None], axis=1)
    layer_out = (middle.astype(jnp.float32) + mixed).astype(jnp.bfloat16)
    return (layer_out, decode_cache)


def solution(mesh):
    placed = (
        P(("req", "tp"), None),
        P("req", "tp"),
        P(),
        P(),
        P(),
        P(),
        P(("req", "tp"), None),
        P(("req", "tp"), None),
        P("tp", None, None),
        P("tp", None, None),
        P("req", "tp", None),
        P("req", None),
        P("req", None),
        P("req", None),
    )
    return jax.shard_map(
        local,
        mesh=mesh,
        in_specs=placed,
        out_specs=(P(("req", "tp"), None), P(("req", "tp"), None, None)),
        check_vma=False,
    )
```

```python
import functools

import jax
import jax.numpy as jnp
from jax import lax
from jax.experimental import pallas as pl
from jax.experimental.pallas import tpu as pltpu
from jax.sharding import PartitionSpec as P

QUERY_HEADS = 12
KEY_VALUE_HEADS = 2
HEAD_SIZE = 128
KEY_BLOCK = 512
SEG_ROWS = 16
LONGEST_SEGMENT = 2048


epsilon = 1e-06
rope_base = 1000000.0
NEGATIVE_FILL = -1e30


def rms_gain(values_in, gain_row):
    as_float = values_in.astype(jnp.float32)
    scale = lax.rsqrt(jnp.mean(as_float * as_float, axis=-1, keepdims=True) + epsilon)
    return (as_float * scale * gain_row).astype(jnp.bfloat16)


def apply_rotary(vectors, token_positions):
    half_dim = vectors.shape[-1] // 2
    frequency = rope_base ** (-jnp.arange(half_dim, dtype=jnp.float32) * 2.0 / vectors.shape[-1])
    angles = token_positions[:, None] * frequency[None, :]
    cosine = jnp.cos(angles)[:, None, :]
    sine_values = jnp.sin(angles)[:, None, :]
    first_half = vectors[..., :half_dim]
    second_half = vectors[..., half_dim:]
    return jnp.concatenate(
        [
            first_half * cosine - second_half * sine_values,
            second_half * cosine + first_half * sine_values,
        ],
        axis=-1,
    )


def attention_kernel(bounds_ref, q_ref, k_ref, v_ref, lo_ref, hi_ref, o_ref):
    ranges = (
        (bounds_ref[0], bounds_ref[1], True),
        (bounds_ref[1], bounds_ref[2], False),
        (bounds_ref[2], bounds_ref[3], True),
    )
    queries = q_ref[...]
    low = lo_ref[...]
    high = hi_ref[...]
    rows = queries.shape[0]
    chunk = k_ref.shape[1] - SEG_ROWS
    per_block = KEY_BLOCK // chunk
    scale = HEAD_SIZE ** (-0.5)

    def block_of(ref, block):
        part = ref[pl.ds(block * per_block, per_block), pl.ds(0, chunk), :]
        return part.reshape(KEY_BLOCK, HEAD_SIZE)

    def raw_scores(block):
        return lax.dot_general(
            queries, block_of(k_ref, block), (((1,), (1,)), ((), ())),
            preferred_element_type=jnp.float32,
        )

    def visible_of(block):
        places = block * KEY_BLOCK + lax.broadcasted_iota(jnp.int32, (1, KEY_BLOCK), 1)
        return (places >= low) & (places <= high)

    best = jnp.full((rows, 1), NEGATIVE_FILL, jnp.float32)
    for first, end, masked in ranges:

        def max_step(block, best, masked=masked):
            scores = raw_scores(block)
            if masked:
                scores = jnp.where(visible_of(block), scores, NEGATIVE_FILL)
            return jnp.maximum(best, jnp.max(scores, axis=1, keepdims=True))

        best = lax.fori_loop(first, end, max_step, best)
    best = best * scale
    carry = (jnp.zeros((rows, 1), jnp.float32), jnp.zeros((rows, HEAD_SIZE), jnp.float32))
    for first, end, masked in ranges:

        def sum_step(block, carry, masked=masked):
            totals, running = carry
            weights = jnp.exp(raw_scores(block) * scale - best)
            if masked:
                weights = jnp.where(visible_of(block), weights, 0.0)
            totals = totals + jnp.sum(weights, axis=1, keepdims=True)
            running = running + jnp.dot(
                weights.astype(jnp.bfloat16), block_of(v_ref, block),
                preferred_element_type=jnp.float32,
            )
            return totals, running

        carry = lax.fori_loop(first, end, sum_step, carry)
    totals, running = carry
    o_ref[...] = (running / totals).astype(o_ref.dtype)


def attention(bounds, grouped_queries, gathered, low, high):
    groups, rows, _ = grouped_queries.shape
    sources, block_rows, _ = gathered.shape
    grid_spec = pltpu.PrefetchScalarGridSpec(
        num_scalar_prefetch=1,
        grid=(groups,),
        in_specs=[
            pl.BlockSpec((None, rows, HEAD_SIZE), lambda g, b: (g, 0, 0)),
            pl.BlockSpec((sources, block_rows, HEAD_SIZE), lambda g, b: (0, 0, g)),
            pl.BlockSpec((sources, block_rows, HEAD_SIZE), lambda g, b: (0, 0, groups + g)),
            pl.BlockSpec((rows, 1), lambda g, b: (0, 0)),
            pl.BlockSpec((rows, 1), lambda g, b: (0, 0)),
        ],
        out_specs=pl.BlockSpec((None, rows, HEAD_SIZE), lambda g, b: (g, 0, 0)),
    )
    return pl.pallas_call(
        attention_kernel,
        grid_spec=grid_spec,
        out_shape=jax.ShapeDtypeStruct((groups, rows, HEAD_SIZE), jnp.bfloat16),
    )(bounds, grouped_queries, gathered, gathered, low, high)


def local(
    tokens,
    segment_ids,
    attention_gain,
    joined_qkv,
    output_proj,
    expert_gain,
    expert_ids,
    gate_weights,
    expert_inner,
    expert_outer,
    cache_pool,
    finished,
    cache_len,
    destination,
):
    tp_count = lax.axis_size("tp")
    where_tp = lax.axis_index("tp")
    replicas = lax.axis_size("req")

    device_rows = tokens.shape[0]
    width = tokens.shape[1]
    seg_local = segment_ids.reshape(device_rows)
    row_span = jnp.arange(device_rows, dtype=jnp.int32)
    token_positions = where_tp * device_rows + row_span
    hidden = rms_gain(tokens, attention_gain)
    joined_everything = jnp.dot(hidden, joined_qkv, preferred_element_type=jnp.float32)
    query_span_width = QUERY_HEADS * HEAD_SIZE
    key_span_width = KEY_VALUE_HEADS * HEAD_SIZE
    float_places = token_positions.astype(jnp.float32)
    query_rows = apply_rotary(
        joined_everything[:, :query_span_width].reshape(device_rows, QUERY_HEADS, HEAD_SIZE),
        float_places,
    ).astype(jnp.bfloat16)
    key_row_list = apply_rotary(
        joined_everything[:, query_span_width : query_span_width + key_span_width].reshape(
            device_rows, KEY_VALUE_HEADS, HEAD_SIZE
        ),
        float_places,
    ).astype(jnp.bfloat16)
    value_rows = joined_everything[:, query_span_width + key_span_width :].astype(jnp.bfloat16)
    key_vals = jnp.concatenate(
        [key_row_list.reshape(device_rows, key_span_width), value_rows], axis=1
    )
    seg_rows = jnp.zeros((SEG_ROWS, key_vals.shape[1]), jnp.bfloat16)
    seg_rows = seg_rows.at[0, :device_rows].set(seg_local.astype(jnp.bfloat16))
    block = jnp.concatenate([key_vals, seg_rows], axis=0)
    copies = jnp.broadcast_to(block[None], (tp_count,) + block.shape)
    gathered = lax.all_to_all(copies, "tp", split_axis=0, concat_axis=0, tiled=True)
    prompt_length = tp_count * device_rows
    seg_all = gathered[:, device_rows, :device_rows].astype(jnp.int32).reshape(prompt_length)
    segment_count = 4
    below = jnp.sum(
        (seg_all[None, :] < jnp.arange(segment_count, dtype=jnp.int32)[:, None]).astype(jnp.int32),
        axis=1,
    )
    low = below[seg_local]
    high = token_positions
    lowest = below[jnp.min(seg_local)]
    highest_low = below[jnp.max(seg_local)]
    first_place = where_tp * device_rows
    first_block = lowest // KEY_BLOCK
    end_block = (first_place + device_rows - 1) // KEY_BLOCK + 1
    whole_first = jnp.clip(-(-highest_low // KEY_BLOCK), first_block, end_block)
    whole_end = jnp.clip((first_place + 1) // KEY_BLOCK, whole_first, end_block)
    bounds = jnp.stack([first_block, whole_first, whole_end, end_block]).astype(jnp.int32)
    heads_per_group = QUERY_HEADS // KEY_VALUE_HEADS
    grouped_queries = (
        query_rows.reshape(device_rows, KEY_VALUE_HEADS, heads_per_group, HEAD_SIZE)
        .transpose(1, 2, 0, 3)
        .reshape(KEY_VALUE_HEADS, heads_per_group * device_rows, HEAD_SIZE)
    )
    chosen = finished.reshape(-1)
    lengths = cache_len.reshape(-1)
    target = destination.reshape(-1)
    cache_depth = cache_pool.shape[1]
    kv_width = cache_pool.shape[2]
    pieces = cache_pool[chosen]
    positions = where_tp * cache_depth + jnp.arange(cache_depth, dtype=jnp.int32)
    kept_mask = positions[None, :] < lengths[:, None]
    pieces = jnp.where(kept_mask[:, :, None], pieces, jnp.zeros((), jnp.bfloat16))
    outgoing_cache = (
        jnp.zeros((replicas * tp_count, cache_depth, kv_width), jnp.bfloat16).at[target].set(pieces)
    )
    outgoing_cache, grouped_queries, gathered = lax.optimization_barrier(
        (outgoing_cache, grouped_queries, gathered)
    )
    arrived_cache = lax.all_to_all(
        outgoing_cache, ("req", "tp"), split_axis=0, concat_axis=1, tiled=True
    )
    decode_cache = arrived_cache.reshape(replicas, tp_count * cache_depth, kv_width)

    grouped_out = attention(
        bounds,
        grouped_queries,
        gathered,
        jnp.tile(low, heads_per_group).reshape(-1, 1),
        jnp.tile(high, heads_per_group).reshape(-1, 1),
    )
    attended = (
        grouped_out.reshape(KEY_VALUE_HEADS, heads_per_group, device_rows, HEAD_SIZE)
        .transpose(2, 0, 1, 3)
        .reshape(device_rows, query_span_width)
    )
    projected = jnp.dot(attended, output_proj, preferred_element_type=jnp.float32)
    middle = (tokens.astype(jnp.float32) + projected).astype(jnp.bfloat16)
    normed = rms_gain(middle, expert_gain)
    decode_cache, normed = lax.optimization_barrier((decode_cache, normed))
    top_count = expert_ids.shape[1]
    held_count = expert_inner.shape[0]
    total_experts = held_count * tp_count
    capacity = 2 * device_rows * top_count // total_experts
    slots = total_experts * capacity
    pair_count = device_rows * top_count
    flat_ids = expert_ids.reshape(pair_count)
    onehot = (flat_ids[:, None] == jnp.arange(total_experts, dtype=jnp.int32)[None, :]).astype(
        jnp.bfloat16
    )
    pair_span = jnp.arange(pair_count, dtype=jnp.int32)
    earlier = (pair_span[None, :] <= pair_span[:, None]).astype(jnp.bfloat16)
    running_count = jnp.dot(earlier, onehot, preferred_element_type=jnp.float32)
    slot_rank = jnp.sum(running_count * onehot.astype(jnp.float32), axis=1).astype(jnp.int32) - 1
    column_index = flat_ids * capacity + slot_rank
    slot_span = jnp.arange(slots, dtype=jnp.int32)
    pick = (column_index[:, None] == slot_span[None, :]).astype(jnp.bfloat16)
    place = jnp.sum(pick.reshape(device_rows, top_count, slots), axis=1)
    outgoing = jnp.dot(place.T, normed, preferred_element_type=jnp.float32).astype(jnp.bfloat16)
    outgoing = outgoing.reshape(tp_count, held_count, capacity, width)
    hidden_width = expert_outer.shape[1]
    inner_out = jnp.einsum(
        "sgcd,gdf->sgcf",
        lax.all_to_all(outgoing, "tp", split_axis=0, concat_axis=0, tiled=True),
        expert_inner,
        preferred_element_type=jnp.float32,
    )
    active = (
        jnp.maximum(inner_out[..., :hidden_width], 0.0) * inner_out[..., hidden_width:]
    ).astype(jnp.bfloat16)
    final_output = jnp.einsum(
        "sgcf,gfd->sgcd", active, expert_outer, preferred_element_type=jnp.float32
    ).astype(jnp.bfloat16)
    returned = lax.all_to_all(final_output, "tp", split_axis=0, concat_axis=0, tiled=True)
    answers = jnp.dot(
        pick, returned.reshape(slots, width), preferred_element_type=jnp.float32
    ).reshape(device_rows, top_count, width)
    mixed = jnp.sum(answers * gate_weights[..., None], axis=1)
    layer_out = (middle.astype(jnp.float32) + mixed).astype(jnp.bfloat16)
    return (layer_out, decode_cache)


def solution(mesh):
    placed = (
        P(("req", "tp"), None),
        P("req", "tp"),
        P(),
        P(),
        P(),
        P(),
        P(("req", "tp"), None),
        P(("req", "tp"), None),
        P("tp", None, None),
        P("tp", None, None),
        P("req", "tp", None),
        P("req", None),
        P("req", None),
        P("req", None),
    )
    return jax.shard_map(
        local,
        mesh=mesh,
        in_specs=placed,
        out_specs=(P(("req", "tp"), None), P(("req", "tp"), None, None)),
        check_vma=False,
    )
```

```python
import functools

import jax
import jax.numpy as jnp
from jax import lax
from jax.experimental import pallas as pl
from jax.experimental.pallas import tpu as pltpu
from jax.sharding import PartitionSpec as P

QUERY_HEADS = 12
KEY_VALUE_HEADS = 2
HEAD_SIZE = 128
KEY_BLOCK = 512
SEG_ROWS = 16
LONGEST_SEGMENT = 2048


epsilon = 1e-06
rope_base = 1000000.0
NEGATIVE_FILL = -1e30


def rms_gain(values_in, gain_row):
    as_float = values_in.astype(jnp.float32)
    scale = lax.rsqrt(jnp.mean(as_float * as_float, axis=-1, keepdims=True) + epsilon)
    return (as_float * scale * gain_row).astype(jnp.bfloat16)


def apply_rotary(vectors, token_positions):
    half_dim = vectors.shape[-1] // 2
    frequency = rope_base ** (-jnp.arange(half_dim, dtype=jnp.float32) * 2.0 / vectors.shape[-1])
    angles = token_positions[:, None] * frequency[None, :]
    cosine = jnp.cos(angles)[:, None, :]
    sine_values = jnp.sin(angles)[:, None, :]
    first_half = vectors[..., :half_dim]
    second_half = vectors[..., half_dim:]
    return jnp.concatenate(
        [
            first_half * cosine - second_half * sine_values,
            second_half * cosine + first_half * sine_values,
        ],
        axis=-1,
    )


def attention_kernel(bounds_ref, q_ref, k_ref, v_ref, lo_ref, hi_ref, o_ref):
    ranges = (
        (bounds_ref[0], bounds_ref[1], True),
        (bounds_ref[1], bounds_ref[2], False),
        (bounds_ref[2], bounds_ref[3], True),
    )
    queries = q_ref[...]
    low = lo_ref[...]
    high = hi_ref[...]
    rows = queries.shape[0]
    chunk = k_ref.shape[1] - SEG_ROWS
    per_block = KEY_BLOCK // chunk
    scale = HEAD_SIZE ** (-0.5)

    def block_of(ref, block):
        part = ref[pl.ds(block * per_block, per_block), pl.ds(0, chunk), :]
        return part.reshape(KEY_BLOCK, HEAD_SIZE)

    def raw_scores(block):
        return lax.dot_general(
            queries, block_of(k_ref, block), (((1,), (1,)), ((), ())),
            preferred_element_type=jnp.float32,
        )

    def visible_of(block):
        places = block * KEY_BLOCK + lax.broadcasted_iota(jnp.int32, (1, KEY_BLOCK), 1)
        return (places >= low) & (places <= high)

    best = jnp.full((rows, 1), NEGATIVE_FILL, jnp.float32)
    for first, end, masked in ranges:

        def max_step(block, best, masked=masked):
            scores = raw_scores(block)
            if masked:
                scores = jnp.where(visible_of(block), scores, NEGATIVE_FILL)
            return jnp.maximum(best, jnp.max(scores, axis=1, keepdims=True))

        best = lax.fori_loop(first, end, max_step, best)
    best = best * scale
    carry = (jnp.zeros((rows, 1), jnp.float32), jnp.zeros((rows, HEAD_SIZE), jnp.float32))
    for first, end, masked in ranges:

        def sum_step(block, carry, masked=masked):
            totals, running = carry
            weights = jnp.exp(raw_scores(block) * scale - best)
            if masked:
                weights = jnp.where(visible_of(block), weights, 0.0)
            totals = totals + jnp.sum(weights, axis=1, keepdims=True)
            running = running + jnp.dot(
                weights.astype(jnp.bfloat16), block_of(v_ref, block),
                preferred_element_type=jnp.float32,
            )
            return totals, running

        carry = lax.fori_loop(first, end, sum_step, carry)
    totals, running = carry
    o_ref[...] = (running / totals).astype(o_ref.dtype)


def attention(bounds, grouped_queries, gathered, low, high):
    groups, rows, _ = grouped_queries.shape
    sources, block_rows, _ = gathered.shape
    grid_spec = pltpu.PrefetchScalarGridSpec(
        num_scalar_prefetch=1,
        grid=(groups,),
        in_specs=[
            pl.BlockSpec((None, rows, HEAD_SIZE), lambda g, b: (g, 0, 0)),
            pl.BlockSpec((sources, block_rows, HEAD_SIZE), lambda g, b: (0, 0, g)),
            pl.BlockSpec((sources, block_rows, HEAD_SIZE), lambda g, b: (0, 0, groups + g)),
            pl.BlockSpec((rows, 1), lambda g, b: (0, 0)),
            pl.BlockSpec((rows, 1), lambda g, b: (0, 0)),
        ],
        out_specs=pl.BlockSpec((None, rows, HEAD_SIZE), lambda g, b: (g, 0, 0)),
    )
    return pl.pallas_call(
        attention_kernel,
        grid_spec=grid_spec,
        out_shape=jax.ShapeDtypeStruct((groups, rows, HEAD_SIZE), jnp.bfloat16),
    )(bounds, grouped_queries, gathered, gathered, low, high)


def local(
    tokens,
    segment_ids,
    attention_gain,
    joined_qkv,
    output_proj,
    expert_gain,
    expert_ids,
    gate_weights,
    expert_inner,
    expert_outer,
    cache_pool,
    finished,
    cache_len,
    destination,
):
    tp_count = lax.axis_size("tp")
    where_tp = lax.axis_index("tp")
    replicas = lax.axis_size("req")

    device_rows = tokens.shape[0]
    width = tokens.shape[1]
    seg_local = segment_ids.reshape(device_rows)
    row_span = jnp.arange(device_rows, dtype=jnp.int32)
    token_positions = where_tp * device_rows + row_span
    hidden = rms_gain(tokens, attention_gain)
    joined_everything = jnp.dot(hidden, joined_qkv, preferred_element_type=jnp.float32)
    query_span_width = QUERY_HEADS * HEAD_SIZE
    key_span_width = KEY_VALUE_HEADS * HEAD_SIZE
    float_places = token_positions.astype(jnp.float32)
    query_rows = apply_rotary(
        joined_everything[:, :query_span_width].reshape(device_rows, QUERY_HEADS, HEAD_SIZE),
        float_places,
    ).astype(jnp.bfloat16)
    key_row_list = apply_rotary(
        joined_everything[:, query_span_width : query_span_width + key_span_width].reshape(
            device_rows, KEY_VALUE_HEADS, HEAD_SIZE
        ),
        float_places,
    ).astype(jnp.bfloat16)
    value_rows = joined_everything[:, query_span_width + key_span_width :].astype(jnp.bfloat16)
    key_vals = jnp.concatenate(
        [key_row_list.reshape(device_rows, key_span_width), value_rows], axis=1
    )
    seg_rows = jnp.zeros((SEG_ROWS, key_vals.shape[1]), jnp.bfloat16)
    seg_rows = seg_rows.at[0, :device_rows].set(seg_local.astype(jnp.bfloat16))
    block = jnp.concatenate([key_vals, seg_rows], axis=0)
    copies = jnp.broadcast_to(block[None], (tp_count,) + block.shape)
    gathered = lax.all_to_all(copies, "tp", split_axis=0, concat_axis=0, tiled=True)
    prompt_length = tp_count * device_rows
    seg_all = gathered[:, device_rows, :device_rows].astype(jnp.int32).reshape(prompt_length)
    segment_count = 4
    below = jnp.sum(
        (seg_all[None, :] < jnp.arange(segment_count, dtype=jnp.int32)[:, None]).astype(jnp.int32),
        axis=1,
    )
    low = below[seg_local]
    high = token_positions
    lowest = below[jnp.min(seg_local)]
    highest_low = below[jnp.max(seg_local)]
    first_place = where_tp * device_rows
    block_shift = KEY_BLOCK.bit_length() - 1

    def blocks_of(places):
        return lax.shift_right_logical(places, jnp.int32(block_shift))

    first_block = blocks_of(lowest)
    end_block = blocks_of(first_place + device_rows - 1) + 1
    whole_first = jnp.clip(blocks_of(highest_low + KEY_BLOCK - 1), first_block, end_block)
    whole_end = jnp.clip(blocks_of(first_place + 1), whole_first, end_block)
    bounds = jnp.stack([first_block, whole_first, whole_end, end_block]).astype(jnp.int32)
    heads_per_group = QUERY_HEADS // KEY_VALUE_HEADS
    grouped_queries = (
        query_rows.reshape(device_rows, KEY_VALUE_HEADS, heads_per_group, HEAD_SIZE)
        .transpose(1, 2, 0, 3)
        .reshape(KEY_VALUE_HEADS, heads_per_group * device_rows, HEAD_SIZE)
    )
    chosen = finished.reshape(-1)
    lengths = cache_len.reshape(-1)
    target = destination.reshape(-1)
    cache_depth = cache_pool.shape[1]
    kv_width = cache_pool.shape[2]
    pieces = cache_pool[chosen]
    positions = where_tp * cache_depth + jnp.arange(cache_depth, dtype=jnp.int32)
    kept_mask = positions[None, :] < lengths[:, None]
    pieces = jnp.where(kept_mask[:, :, None], pieces, jnp.zeros((), jnp.bfloat16))
    outgoing_cache = (
        jnp.zeros((replicas * tp_count, cache_depth, kv_width), jnp.bfloat16).at[target].set(pieces)
    )
    outgoing_cache, grouped_queries, gathered = lax.optimization_barrier(
        (outgoing_cache, grouped_queries, gathered)
    )
    arrived_cache = lax.all_to_all(
        outgoing_cache, ("req", "tp"), split_axis=0, concat_axis=1, tiled=True
    )
    decode_cache = arrived_cache.reshape(replicas, tp_count * cache_depth, kv_width)

    grouped_out = attention(
        bounds,
        grouped_queries,
        gathered,
        jnp.tile(low, heads_per_group).reshape(-1, 1),
        jnp.tile(high, heads_per_group).reshape(-1, 1),
    )
    attended = (
        grouped_out.reshape(KEY_VALUE_HEADS, heads_per_group, device_rows, HEAD_SIZE)
        .transpose(2, 0, 1, 3)
        .reshape(device_rows, query_span_width)
    )
    projected = jnp.dot(attended, output_proj, preferred_element_type=jnp.float32)
    middle = (tokens.astype(jnp.float32) + projected).astype(jnp.bfloat16)
    normed = rms_gain(middle, expert_gain)
    decode_cache, normed = lax.optimization_barrier((decode_cache, normed))
    top_count = expert_ids.shape[1]
    held_count = expert_inner.shape[0]
    total_experts = held_count * tp_count
    capacity = 2 * device_rows * top_count // total_experts
    slots = total_experts * capacity
    pair_count = device_rows * top_count
    flat_ids = expert_ids.reshape(pair_count)
    onehot = (flat_ids[:, None] == jnp.arange(total_experts, dtype=jnp.int32)[None, :]).astype(
        jnp.bfloat16
    )
    pair_span = jnp.arange(pair_count, dtype=jnp.int32)
    earlier = (pair_span[None, :] <= pair_span[:, None]).astype(jnp.bfloat16)
    running_count = jnp.dot(earlier, onehot, preferred_element_type=jnp.float32)
    slot_rank = jnp.sum(running_count * onehot.astype(jnp.float32), axis=1).astype(jnp.int32) - 1
    column_index = flat_ids * capacity + slot_rank
    slot_span = jnp.arange(slots, dtype=jnp.int32)
    pick = (column_index[:, None] == slot_span[None, :]).astype(jnp.bfloat16)
    place = jnp.sum(pick.reshape(device_rows, top_count, slots), axis=1)
    outgoing = jnp.dot(place.T, normed, preferred_element_type=jnp.float32).astype(jnp.bfloat16)
    outgoing = outgoing.reshape(tp_count, held_count, capacity, width)
    hidden_width = expert_outer.shape[1]
    inner_out = jnp.einsum(
        "sgcd,gdf->sgcf",
        lax.all_to_all(outgoing, "tp", split_axis=0, concat_axis=0, tiled=True),
        expert_inner,
        preferred_element_type=jnp.float32,
    )
    active = (
        jnp.maximum(inner_out[..., :hidden_width], 0.0) * inner_out[..., hidden_width:]
    ).astype(jnp.bfloat16)
    final_output = jnp.einsum(
        "sgcf,gfd->sgcd", active, expert_outer, preferred_element_type=jnp.float32
    ).astype(jnp.bfloat16)
    returned = lax.all_to_all(final_output, "tp", split_axis=0, concat_axis=0, tiled=True)
    answers = jnp.dot(
        pick, returned.reshape(slots, width), preferred_element_type=jnp.float32
    ).reshape(device_rows, top_count, width)
    mixed = jnp.sum(answers * gate_weights[..., None], axis=1)
    layer_out = (middle.astype(jnp.float32) + mixed).astype(jnp.bfloat16)
    return (layer_out, decode_cache)


def solution(mesh):
    placed = (
        P(("req", "tp"), None),
        P("req", "tp"),
        P(),
        P(),
        P(),
        P(),
        P(("req", "tp"), None),
        P(("req", "tp"), None),
        P("tp", None, None),
        P("tp", None, None),
        P("req", "tp", None),
        P("req", None),
        P("req", None),
        P("req", None),
    )
    return jax.shard_map(
        local,
        mesh=mesh,
        in_specs=placed,
        out_specs=(P(("req", "tp"), None), P(("req", "tp"), None, None)),
        check_vma=False,
    )
```

```python
import functools

import jax
import jax.numpy as jnp
from jax import lax
from jax.experimental import pallas as pl
from jax.experimental.pallas import tpu as pltpu
from jax.sharding import PartitionSpec as P

QUERY_HEADS = 12
KEY_VALUE_HEADS = 2
HEAD_SIZE = 128
KEY_BLOCK = 512
SEG_ROWS = 16
LONGEST_SEGMENT = 2048


epsilon = 1e-06
rope_base = 1000000.0
NEGATIVE_FILL = -1e30


def rms_gain(values_in, gain_row):
    as_float = values_in.astype(jnp.float32)
    scale = lax.rsqrt(jnp.mean(as_float * as_float, axis=-1, keepdims=True) + epsilon)
    return (as_float * scale * gain_row).astype(jnp.bfloat16)


def apply_rotary(vectors, token_positions):
    half_dim = vectors.shape[-1] // 2
    frequency = rope_base ** (-jnp.arange(half_dim, dtype=jnp.float32) * 2.0 / vectors.shape[-1])
    angles = token_positions[:, None] * frequency[None, :]
    cosine = jnp.cos(angles)[:, None, :]
    sine_values = jnp.sin(angles)[:, None, :]
    first_half = vectors[..., :half_dim]
    second_half = vectors[..., half_dim:]
    return jnp.concatenate(
        [
            first_half * cosine - second_half * sine_values,
            second_half * cosine + first_half * sine_values,
        ],
        axis=-1,
    )


def attention_kernel(bounds_ref, q_ref, k_ref, v_ref, lo_ref, hi_ref, o_ref):
    ranges = (
        (bounds_ref[0], bounds_ref[1], True),
        (bounds_ref[1], bounds_ref[2], False),
        (bounds_ref[2], bounds_ref[3], True),
    )
    queries = q_ref[...]
    low = lo_ref[...]
    high = hi_ref[...]
    rows = queries.shape[0]
    chunk = k_ref.shape[1] - SEG_ROWS
    per_block = KEY_BLOCK // chunk
    scale = HEAD_SIZE ** (-0.5)

    def block_of(ref, block):
        part = ref[pl.ds(block * per_block, per_block), pl.ds(0, chunk), :]
        return part.reshape(KEY_BLOCK, HEAD_SIZE)

    def raw_scores(block):
        return lax.dot_general(
            queries, block_of(k_ref, block), (((1,), (1,)), ((), ())),
            preferred_element_type=jnp.float32,
        )

    def visible_of(block):
        places = block * KEY_BLOCK + lax.broadcasted_iota(jnp.int32, (1, KEY_BLOCK), 1)
        return (places >= low) & (places <= high)

    carry = (
        jnp.full((rows, 1), NEGATIVE_FILL, jnp.float32),
        jnp.zeros((rows, 1), jnp.float32),
        jnp.zeros((rows, HEAD_SIZE), jnp.float32),
    )
    for first, end, masked in ranges:

        def step(block, carry, masked=masked):
            best, totals, running = carry
            scores = raw_scores(block) * scale
            if masked:
                visible = visible_of(block)
                scores = jnp.where(visible, scores, NEGATIVE_FILL)
            fresh = jnp.maximum(best, jnp.max(scores, axis=1, keepdims=True))
            rescale = jnp.exp(best - fresh)
            weights = jnp.exp(scores - fresh)
            if masked:
                weights = jnp.where(visible, weights, 0.0)
            totals = totals * rescale + jnp.sum(weights, axis=1, keepdims=True)
            running = running * rescale + jnp.dot(
                weights.astype(jnp.bfloat16), block_of(v_ref, block),
                preferred_element_type=jnp.float32,
            )
            return fresh, totals, running

        carry = lax.fori_loop(first, end, step, carry)
    _, totals, running = carry
    o_ref[...] = (running / totals).astype(o_ref.dtype)


def attention(bounds, grouped_queries, gathered, low, high):
    groups, rows, _ = grouped_queries.shape
    sources, block_rows, _ = gathered.shape
    grid_spec = pltpu.PrefetchScalarGridSpec(
        num_scalar_prefetch=1,
        grid=(groups,),
        in_specs=[
            pl.BlockSpec((None, rows, HEAD_SIZE), lambda g, b: (g, 0, 0)),
            pl.BlockSpec((sources, block_rows, HEAD_SIZE), lambda g, b: (0, 0, g)),
            pl.BlockSpec((sources, block_rows, HEAD_SIZE), lambda g, b: (0, 0, groups + g)),
            pl.BlockSpec((rows, 1), lambda g, b: (0, 0)),
            pl.BlockSpec((rows, 1), lambda g, b: (0, 0)),
        ],
        out_specs=pl.BlockSpec((None, rows, HEAD_SIZE), lambda g, b: (g, 0, 0)),
    )
    return pl.pallas_call(
        attention_kernel,
        grid_spec=grid_spec,
        out_shape=jax.ShapeDtypeStruct((groups, rows, HEAD_SIZE), jnp.bfloat16),
    )(bounds, grouped_queries, gathered, gathered, low, high)


def local(
    tokens,
    segment_ids,
    attention_gain,
    joined_qkv,
    output_proj,
    expert_gain,
    expert_ids,
    gate_weights,
    expert_inner,
    expert_outer,
    cache_pool,
    finished,
    cache_len,
    destination,
):
    tp_count = lax.axis_size("tp")
    where_tp = lax.axis_index("tp")
    replicas = lax.axis_size("req")

    device_rows = tokens.shape[0]
    width = tokens.shape[1]
    seg_local = segment_ids.reshape(device_rows)
    row_span = jnp.arange(device_rows, dtype=jnp.int32)
    token_positions = where_tp * device_rows + row_span
    hidden = rms_gain(tokens, attention_gain)
    joined_everything = jnp.dot(hidden, joined_qkv, preferred_element_type=jnp.float32)
    query_span_width = QUERY_HEADS * HEAD_SIZE
    key_span_width = KEY_VALUE_HEADS * HEAD_SIZE
    float_places = token_positions.astype(jnp.float32)
    query_rows = apply_rotary(
        joined_everything[:, :query_span_width].reshape(device_rows, QUERY_HEADS, HEAD_SIZE),
        float_places,
    ).astype(jnp.bfloat16)
    key_row_list = apply_rotary(
        joined_everything[:, query_span_width : query_span_width + key_span_width].reshape(
            device_rows, KEY_VALUE_HEADS, HEAD_SIZE
        ),
        float_places,
    ).astype(jnp.bfloat16)
    value_rows = joined_everything[:, query_span_width + key_span_width :].astype(jnp.bfloat16)
    key_vals = jnp.concatenate(
        [key_row_list.reshape(device_rows, key_span_width), value_rows], axis=1
    )
    seg_rows = jnp.zeros((SEG_ROWS, key_vals.shape[1]), jnp.bfloat16)
    seg_rows = seg_rows.at[0, :device_rows].set(seg_local.astype(jnp.bfloat16))
    block = jnp.concatenate([key_vals, seg_rows], axis=0)
    copies = jnp.broadcast_to(block[None], (tp_count,) + block.shape)
    gathered = lax.all_to_all(copies, "tp", split_axis=0, concat_axis=0, tiled=True)
    prompt_length = tp_count * device_rows
    seg_all = gathered[:, device_rows, :device_rows].astype(jnp.int32).reshape(prompt_length)
    segment_count = 4
    below = jnp.sum(
        (seg_all[None, :] < jnp.arange(segment_count, dtype=jnp.int32)[:, None]).astype(jnp.int32),
        axis=1,
    )
    low = below[seg_local]
    high = token_positions
    lowest = below[jnp.min(seg_local)]
    highest_low = below[jnp.max(seg_local)]
    first_place = where_tp * device_rows
    first_block = lowest // KEY_BLOCK
    end_block = (first_place + device_rows - 1) // KEY_BLOCK + 1
    whole_first = jnp.clip(-(-highest_low // KEY_BLOCK), first_block, end_block)
    whole_end = jnp.clip((first_place + 1) // KEY_BLOCK, whole_first, end_block)
    bounds = jnp.stack([first_block, whole_first, whole_end, end_block]).astype(jnp.int32)
    heads_per_group = QUERY_HEADS // KEY_VALUE_HEADS
    grouped_queries = (
        query_rows.reshape(device_rows, KEY_VALUE_HEADS, heads_per_group, HEAD_SIZE)
        .transpose(1, 2, 0, 3)
        .reshape(KEY_VALUE_HEADS, heads_per_group * device_rows, HEAD_SIZE)
    )
    chosen = finished.reshape(-1)
    lengths = cache_len.reshape(-1)
    target = destination.reshape(-1)
    cache_depth = cache_pool.shape[1]
    kv_width = cache_pool.shape[2]
    pieces = cache_pool[chosen]
    positions = where_tp * cache_depth + jnp.arange(cache_depth, dtype=jnp.int32)
    kept_mask = positions[None, :] < lengths[:, None]
    pieces = jnp.where(kept_mask[:, :, None], pieces, jnp.zeros((), jnp.bfloat16))
    outgoing_cache = (
        jnp.zeros((replicas * tp_count, cache_depth, kv_width), jnp.bfloat16).at[target].set(pieces)
    )
    outgoing_cache, grouped_queries, gathered = lax.optimization_barrier(
        (outgoing_cache, grouped_queries, gathered)
    )
    arrived_cache = lax.all_to_all(
        outgoing_cache, ("req", "tp"), split_axis=0, concat_axis=1, tiled=True
    )
    decode_cache = arrived_cache.reshape(replicas, tp_count * cache_depth, kv_width)

    grouped_out = attention(
        bounds,
        grouped_queries,
        gathered,
        jnp.tile(low, heads_per_group).reshape(-1, 1),
        jnp.tile(high, heads_per_group).reshape(-1, 1),
    )
    attended = (
        grouped_out.reshape(KEY_VALUE_HEADS, heads_per_group, device_rows, HEAD_SIZE)
        .transpose(2, 0, 1, 3)
        .reshape(device_rows, query_span_width)
    )
    projected = jnp.dot(attended, output_proj, preferred_element_type=jnp.float32)
    middle = (tokens.astype(jnp.float32) + projected).astype(jnp.bfloat16)
    normed = rms_gain(middle, expert_gain)
    decode_cache, normed = lax.optimization_barrier((decode_cache, normed))
    top_count = expert_ids.shape[1]
    held_count = expert_inner.shape[0]
    total_experts = held_count * tp_count
    capacity = 2 * device_rows * top_count // total_experts
    slots = total_experts * capacity
    pair_count = device_rows * top_count
    flat_ids = expert_ids.reshape(pair_count)
    onehot = (flat_ids[:, None] == jnp.arange(total_experts, dtype=jnp.int32)[None, :]).astype(
        jnp.bfloat16
    )
    pair_span = jnp.arange(pair_count, dtype=jnp.int32)
    earlier = (pair_span[None, :] <= pair_span[:, None]).astype(jnp.bfloat16)
    running_count = jnp.dot(earlier, onehot, preferred_element_type=jnp.float32)
    slot_rank = jnp.sum(running_count * onehot.astype(jnp.float32), axis=1).astype(jnp.int32) - 1
    column_index = flat_ids * capacity + slot_rank
    slot_span = jnp.arange(slots, dtype=jnp.int32)
    pick = (column_index[:, None] == slot_span[None, :]).astype(jnp.bfloat16)
    place = jnp.sum(pick.reshape(device_rows, top_count, slots), axis=1)
    outgoing = jnp.dot(place.T, normed, preferred_element_type=jnp.float32).astype(jnp.bfloat16)
    outgoing = outgoing.reshape(tp_count, held_count, capacity, width)
    hidden_width = expert_outer.shape[1]
    inner_out = jnp.einsum(
        "sgcd,gdf->sgcf",
        lax.all_to_all(outgoing, "tp", split_axis=0, concat_axis=0, tiled=True),
        expert_inner,
        preferred_element_type=jnp.float32,
    )
    active = (
        jnp.maximum(inner_out[..., :hidden_width], 0.0) * inner_out[..., hidden_width:]
    ).astype(jnp.bfloat16)
    final_output = jnp.einsum(
        "sgcf,gfd->sgcd", active, expert_outer, preferred_element_type=jnp.float32
    ).astype(jnp.bfloat16)
    returned = lax.all_to_all(final_output, "tp", split_axis=0, concat_axis=0, tiled=True)
    answers = jnp.dot(
        pick, returned.reshape(slots, width), preferred_element_type=jnp.float32
    ).reshape(device_rows, top_count, width)
    mixed = jnp.sum(answers * gate_weights[..., None], axis=1)
    layer_out = (middle.astype(jnp.float32) + mixed).astype(jnp.bfloat16)
    return (layer_out, decode_cache)


def solution(mesh):
    placed = (
        P(("req", "tp"), None),
        P("req", "tp"),
        P(),
        P(),
        P(),
        P(),
        P(("req", "tp"), None),
        P(("req", "tp"), None),
        P("tp", None, None),
        P("tp", None, None),
        P("req", "tp", None),
        P("req", None),
        P("req", None),
        P("req", None),
    )
    return jax.shard_map(
        local,
        mesh=mesh,
        in_specs=placed,
        out_specs=(P(("req", "tp"), None), P(("req", "tp"), None, None)),
        check_vma=False,
    )
```

```python
import functools

import jax
import jax.numpy as jnp
from jax import lax
from jax.experimental import pallas as pl
from jax.experimental.pallas import tpu as pltpu
from jax.sharding import PartitionSpec as P

QUERY_HEADS = 12
KEY_VALUE_HEADS = 2
HEAD_SIZE = 128
KEY_BLOCK = 512
SEG_ROWS = 16
LONGEST_SEGMENT = 2048


epsilon = 1e-06
rope_base = 1000000.0
NEGATIVE_FILL = -1e30


def rms_gain(values_in, gain_row):
    as_float = values_in.astype(jnp.float32)
    scale = lax.rsqrt(jnp.mean(as_float * as_float, axis=-1, keepdims=True) + epsilon)
    return (as_float * scale * gain_row).astype(jnp.bfloat16)


def apply_rotary(vectors, token_positions):
    half_dim = vectors.shape[-1] // 2
    frequency = rope_base ** (-jnp.arange(half_dim, dtype=jnp.float32) * 2.0 / vectors.shape[-1])
    angles = token_positions[:, None] * frequency[None, :]
    cosine = jnp.cos(angles)[:, None, :]
    sine_values = jnp.sin(angles)[:, None, :]
    first_half = vectors[..., :half_dim]
    second_half = vectors[..., half_dim:]
    return jnp.concatenate(
        [
            first_half * cosine - second_half * sine_values,
            second_half * cosine + first_half * sine_values,
        ],
        axis=-1,
    )


def attention_kernel(bounds_ref, q_ref, k_ref, v_ref, lo_ref, hi_ref, o_ref):
    ranges = (
        (bounds_ref[0], bounds_ref[1], True),
        (bounds_ref[1], bounds_ref[2], False),
        (bounds_ref[2], bounds_ref[3], True),
    )
    queries = q_ref[...]
    low = lo_ref[...]
    high = hi_ref[...]
    rows = queries.shape[0]
    chunk = k_ref.shape[1] - SEG_ROWS
    per_block = KEY_BLOCK // chunk
    scale = HEAD_SIZE ** (-0.5)

    def block_of(ref, block):
        part = ref[pl.ds(block * per_block, per_block), pl.ds(0, chunk), :]
        return part.reshape(KEY_BLOCK, HEAD_SIZE)

    def raw_scores(block):
        return lax.dot_general(
            queries, block_of(k_ref, block), (((1,), (1,)), ((), ())),
            preferred_element_type=jnp.float32,
        )

    def visible_of(block):
        places = block * KEY_BLOCK + lax.broadcasted_iota(jnp.int32, (1, KEY_BLOCK), 1)
        return (places >= low) & (places <= high)

    best = jnp.full((rows, 1), NEGATIVE_FILL, jnp.float32)
    for first, end, masked in ranges:

        def max_step(block, best, masked=masked):
            scores = raw_scores(block)
            if masked:
                scores = jnp.where(visible_of(block), scores, NEGATIVE_FILL)
            return jnp.maximum(best, jnp.max(scores, axis=1, keepdims=True))

        best = lax.fori_loop(first, end, max_step, best)
    best = best * scale
    carry = (jnp.zeros((rows, 1), jnp.float32), jnp.zeros((rows, HEAD_SIZE), jnp.float32))
    for first, end, masked in ranges:

        def sum_step(block, carry, masked=masked):
            totals, running = carry
            weights = jnp.exp(raw_scores(block) * scale - best)
            if masked:
                weights = jnp.where(visible_of(block), weights, 0.0)
            totals = totals + jnp.sum(weights, axis=1, keepdims=True)
            running = running + jnp.dot(
                weights.astype(jnp.bfloat16), block_of(v_ref, block),
                preferred_element_type=jnp.float32,
            )
            return totals, running

        carry = lax.fori_loop(first, end, sum_step, carry)
    totals, running = carry
    o_ref[...] = (running / totals).astype(o_ref.dtype)


def attention(bounds, grouped_queries, gathered, low, high):
    groups, rows, _ = grouped_queries.shape
    sources, block_rows, _ = gathered.shape
    grid_spec = pltpu.PrefetchScalarGridSpec(
        num_scalar_prefetch=1,
        grid=(groups,),
        in_specs=[
            pl.BlockSpec((None, rows, HEAD_SIZE), lambda g, b: (g, 0, 0)),
            pl.BlockSpec((sources, block_rows, HEAD_SIZE), lambda g, b: (0, 0, g)),
            pl.BlockSpec((sources, block_rows, HEAD_SIZE), lambda g, b: (0, 0, groups + g)),
            pl.BlockSpec((rows, 1), lambda g, b: (0, 0)),
            pl.BlockSpec((rows, 1), lambda g, b: (0, 0)),
        ],
        out_specs=pl.BlockSpec((None, rows, HEAD_SIZE), lambda g, b: (g, 0, 0)),
    )
    return pl.pallas_call(
        attention_kernel,
        grid_spec=grid_spec,
        out_shape=jax.ShapeDtypeStruct((groups, rows, HEAD_SIZE), jnp.bfloat16),
    )(bounds, grouped_queries, gathered, gathered, low, high)


def local(
    tokens,
    segment_ids,
    attention_gain,
    joined_qkv,
    output_proj,
    expert_gain,
    expert_ids,
    gate_weights,
    expert_inner,
    expert_outer,
    cache_pool,
    finished,
    cache_len,
    destination,
):
    tp_count = lax.axis_size("tp")
    where_tp = lax.axis_index("tp")
    replicas = lax.axis_size("req")

    device_rows = tokens.shape[0]
    width = tokens.shape[1]
    seg_local = segment_ids.reshape(device_rows)
    row_span = jnp.arange(device_rows, dtype=jnp.int32)
    token_positions = where_tp * device_rows + row_span
    hidden = rms_gain(tokens, attention_gain)
    query_span_width = QUERY_HEADS * HEAD_SIZE
    key_span_width = KEY_VALUE_HEADS * HEAD_SIZE
    key_value_part = jnp.dot(
        hidden, joined_qkv[:, query_span_width:], preferred_element_type=jnp.float32
    )
    query_part = jnp.dot(
        hidden, joined_qkv[:, :query_span_width], preferred_element_type=jnp.float32
    )
    float_places = token_positions.astype(jnp.float32)
    query_rows = apply_rotary(
        query_part.reshape(device_rows, QUERY_HEADS, HEAD_SIZE),
        float_places,
    ).astype(jnp.bfloat16)
    key_row_list = apply_rotary(
        key_value_part[:, :key_span_width].reshape(device_rows, KEY_VALUE_HEADS, HEAD_SIZE),
        float_places,
    ).astype(jnp.bfloat16)
    value_rows = key_value_part[:, key_span_width:].astype(jnp.bfloat16)
    key_vals = jnp.concatenate(
        [key_row_list.reshape(device_rows, key_span_width), value_rows], axis=1
    )
    seg_rows = jnp.zeros((SEG_ROWS, key_vals.shape[1]), jnp.bfloat16)
    seg_rows = seg_rows.at[0, :device_rows].set(seg_local.astype(jnp.bfloat16))
    block = jnp.concatenate([key_vals, seg_rows], axis=0)
    copies = jnp.broadcast_to(block[None], (tp_count,) + block.shape)
    gathered = lax.all_to_all(copies, "tp", split_axis=0, concat_axis=0, tiled=True)
    prompt_length = tp_count * device_rows
    seg_all = gathered[:, device_rows, :device_rows].astype(jnp.int32).reshape(prompt_length)
    segment_count = 4
    below = jnp.sum(
        (seg_all[None, :] < jnp.arange(segment_count, dtype=jnp.int32)[:, None]).astype(jnp.int32),
        axis=1,
    )
    low = below[seg_local]
    high = token_positions
    lowest = below[jnp.min(seg_local)]
    highest_low = below[jnp.max(seg_local)]
    first_place = where_tp * device_rows
    first_block = lowest // KEY_BLOCK
    end_block = (first_place + device_rows - 1) // KEY_BLOCK + 1
    whole_first = jnp.clip(-(-highest_low // KEY_BLOCK), first_block, end_block)
    whole_end = jnp.clip((first_place + 1) // KEY_BLOCK, whole_first, end_block)
    bounds = jnp.stack([first_block, whole_first, whole_end, end_block]).astype(jnp.int32)
    heads_per_group = QUERY_HEADS // KEY_VALUE_HEADS
    grouped_queries = (
        query_rows.reshape(device_rows, KEY_VALUE_HEADS, heads_per_group, HEAD_SIZE)
        .transpose(1, 2, 0, 3)
        .reshape(KEY_VALUE_HEADS, heads_per_group * device_rows, HEAD_SIZE)
    )
    chosen = finished.reshape(-1)
    lengths = cache_len.reshape(-1)
    target = destination.reshape(-1)
    cache_depth = cache_pool.shape[1]
    kv_width = cache_pool.shape[2]
    pieces = cache_pool[chosen]
    positions = where_tp * cache_depth + jnp.arange(cache_depth, dtype=jnp.int32)
    kept_mask = positions[None, :] < lengths[:, None]
    pieces = jnp.where(kept_mask[:, :, None], pieces, jnp.zeros((), jnp.bfloat16))
    outgoing_cache = (
        jnp.zeros((replicas * tp_count, cache_depth, kv_width), jnp.bfloat16).at[target].set(pieces)
    )
    outgoing_cache, grouped_queries, gathered = lax.optimization_barrier(
        (outgoing_cache, grouped_queries, gathered)
    )
    arrived_cache = lax.all_to_all(
        outgoing_cache, ("req", "tp"), split_axis=0, concat_axis=1, tiled=True
    )
    decode_cache = arrived_cache.reshape(replicas, tp_count * cache_depth, kv_width)

    grouped_out = attention(
        bounds,
        grouped_queries,
        gathered,
        jnp.tile(low, heads_per_group).reshape(-1, 1),
        jnp.tile(high, heads_per_group).reshape(-1, 1),
    )
    attended = (
        grouped_out.reshape(KEY_VALUE_HEADS, heads_per_group, device_rows, HEAD_SIZE)
        .transpose(2, 0, 1, 3)
        .reshape(device_rows, query_span_width)
    )
    projected = jnp.dot(attended, output_proj, preferred_element_type=jnp.float32)
    middle = (tokens.astype(jnp.float32) + projected).astype(jnp.bfloat16)
    normed = rms_gain(middle, expert_gain)
    decode_cache, normed = lax.optimization_barrier((decode_cache, normed))
    top_count = expert_ids.shape[1]
    held_count = expert_inner.shape[0]
    total_experts = held_count * tp_count
    capacity = 2 * device_rows * top_count // total_experts
    slots = total_experts * capacity
    pair_count = device_rows * top_count
    flat_ids = expert_ids.reshape(pair_count)
    onehot = (flat_ids[:, None] == jnp.arange(total_experts, dtype=jnp.int32)[None, :]).astype(
        jnp.bfloat16
    )
    pair_span = jnp.arange(pair_count, dtype=jnp.int32)
    earlier = (pair_span[None, :] <= pair_span[:, None]).astype(jnp.bfloat16)
    running_count = jnp.dot(earlier, onehot, preferred_element_type=jnp.float32)
    slot_rank = jnp.sum(running_count * onehot.astype(jnp.float32), axis=1).astype(jnp.int32) - 1
    column_index = flat_ids * capacity + slot_rank
    slot_span = jnp.arange(slots, dtype=jnp.int32)
    pick = (column_index[:, None] == slot_span[None, :]).astype(jnp.bfloat16)
    place = jnp.sum(pick.reshape(device_rows, top_count, slots), axis=1)
    outgoing = jnp.dot(place.T, normed, preferred_element_type=jnp.float32).astype(jnp.bfloat16)
    outgoing = outgoing.reshape(tp_count, held_count, capacity, width)
    hidden_width = expert_outer.shape[1]
    inner_out = jnp.einsum(
        "sgcd,gdf->sgcf",
        lax.all_to_all(outgoing, "tp", split_axis=0, concat_axis=0, tiled=True),
        expert_inner,
        preferred_element_type=jnp.float32,
    )
    active = (
        jnp.maximum(inner_out[..., :hidden_width], 0.0) * inner_out[..., hidden_width:]
    ).astype(jnp.bfloat16)
    final_output = jnp.einsum(
        "sgcf,gfd->sgcd", active, expert_outer, preferred_element_type=jnp.float32
    ).astype(jnp.bfloat16)
    returned = lax.all_to_all(final_output, "tp", split_axis=0, concat_axis=0, tiled=True)
    answers = jnp.dot(
        pick, returned.reshape(slots, width), preferred_element_type=jnp.float32
    ).reshape(device_rows, top_count, width)
    mixed = jnp.sum(answers * gate_weights[..., None], axis=1)
    layer_out = (middle.astype(jnp.float32) + mixed).astype(jnp.bfloat16)
    return (layer_out, decode_cache)


def solution(mesh):
    placed = (
        P(("req", "tp"), None),
        P("req", "tp"),
        P(),
        P(),
        P(),
        P(),
        P(("req", "tp"), None),
        P(("req", "tp"), None),
        P("tp", None, None),
        P("tp", None, None),
        P("req", "tp", None),
        P("req", None),
        P("req", None),
        P("req", None),
    )
    return jax.shard_map(
        local,
        mesh=mesh,
        in_specs=placed,
        out_specs=(P(("req", "tp"), None), P(("req", "tp"), None, None)),
        check_vma=False,
    )
```

```python
import functools

import jax
import jax.numpy as jnp
from jax import lax
from jax.experimental import pallas as pl
from jax.experimental.pallas import tpu as pltpu
from jax.sharding import PartitionSpec as P

QUERY_HEADS = 12
KEY_VALUE_HEADS = 2
HEAD_SIZE = 128
KEY_BLOCK = 512
SEG_ROWS = 16
LONGEST_SEGMENT = 2048


epsilon = 1e-06
rope_base = 1000000.0
NEGATIVE_FILL = -1e30


def rms_gain(values_in, gain_row):
    as_float = values_in.astype(jnp.float32)
    scale = lax.rsqrt(jnp.mean(as_float * as_float, axis=-1, keepdims=True) + epsilon)
    return (as_float * scale * gain_row).astype(jnp.bfloat16)


def apply_rotary(vectors, token_positions):
    half_dim = vectors.shape[-1] // 2
    frequency = rope_base ** (-jnp.arange(half_dim, dtype=jnp.float32) * 2.0 / vectors.shape[-1])
    angles = token_positions[:, None] * frequency[None, :]
    cosine = jnp.cos(angles)[:, None, :]
    sine_values = jnp.sin(angles)[:, None, :]
    first_half = vectors[..., :half_dim]
    second_half = vectors[..., half_dim:]
    return jnp.concatenate(
        [
            first_half * cosine - second_half * sine_values,
            second_half * cosine + first_half * sine_values,
        ],
        axis=-1,
    )


def attention_kernel(bounds_ref, q_ref, k_ref, v_ref, lo_ref, hi_ref, o_ref):
    ranges = (
        (bounds_ref[0], bounds_ref[1], True),
        (bounds_ref[1], bounds_ref[2], False),
        (bounds_ref[2], bounds_ref[3], True),
    )
    queries = q_ref[...]
    rows = queries.shape[0]
    copies = rows // lo_ref.shape[0]
    low = jnp.concatenate([lo_ref[...]] * copies, axis=0)
    high = jnp.concatenate([hi_ref[...]] * copies, axis=0)
    chunk = k_ref.shape[1] - SEG_ROWS
    per_block = KEY_BLOCK // chunk
    scale = HEAD_SIZE ** (-0.5)

    def block_of(ref, block):
        part = ref[pl.ds(block * per_block, per_block), pl.ds(0, chunk), :]
        return part.reshape(KEY_BLOCK, HEAD_SIZE)

    def raw_scores(block):
        return lax.dot_general(
            queries, block_of(k_ref, block), (((1,), (1,)), ((), ())),
            preferred_element_type=jnp.float32,
        )

    def visible_of(block):
        places = block * KEY_BLOCK + lax.broadcasted_iota(jnp.int32, (1, KEY_BLOCK), 1)
        return (places >= low) & (places <= high)

    best = jnp.full((rows, 1), NEGATIVE_FILL, jnp.float32)
    for first, end, masked in ranges:

        def max_step(block, best, masked=masked):
            scores = raw_scores(block)
            if masked:
                scores = jnp.where(visible_of(block), scores, NEGATIVE_FILL)
            return jnp.maximum(best, jnp.max(scores, axis=1, keepdims=True))

        best = lax.fori_loop(first, end, max_step, best)
    best = best * scale
    carry = (jnp.zeros((rows, 1), jnp.float32), jnp.zeros((rows, HEAD_SIZE), jnp.float32))
    for first, end, masked in ranges:

        def sum_step(block, carry, masked=masked):
            totals, running = carry
            weights = jnp.exp(raw_scores(block) * scale - best)
            if masked:
                weights = jnp.where(visible_of(block), weights, 0.0)
            totals = totals + jnp.sum(weights, axis=1, keepdims=True)
            running = running + jnp.dot(
                weights.astype(jnp.bfloat16), block_of(v_ref, block),
                preferred_element_type=jnp.float32,
            )
            return totals, running

        carry = lax.fori_loop(first, end, sum_step, carry)
    totals, running = carry
    o_ref[...] = (running / totals).astype(o_ref.dtype)


def attention(bounds, grouped_queries, gathered, low, high):
    groups, rows, _ = grouped_queries.shape
    sources, block_rows, _ = gathered.shape
    grid_spec = pltpu.PrefetchScalarGridSpec(
        num_scalar_prefetch=1,
        grid=(groups,),
        in_specs=[
            pl.BlockSpec((None, rows, HEAD_SIZE), lambda g, b: (g, 0, 0)),
            pl.BlockSpec((sources, block_rows, HEAD_SIZE), lambda g, b: (0, 0, g)),
            pl.BlockSpec((sources, block_rows, HEAD_SIZE), lambda g, b: (0, 0, groups + g)),
            pl.BlockSpec(low.shape, lambda g, b: (0, 0)),
            pl.BlockSpec(high.shape, lambda g, b: (0, 0)),
        ],
        out_specs=pl.BlockSpec((None, rows, HEAD_SIZE), lambda g, b: (g, 0, 0)),
    )
    return pl.pallas_call(
        attention_kernel,
        grid_spec=grid_spec,
        out_shape=jax.ShapeDtypeStruct((groups, rows, HEAD_SIZE), jnp.bfloat16),
    )(bounds, grouped_queries, gathered, gathered, low, high)


def local(
    tokens,
    segment_ids,
    attention_gain,
    joined_qkv,
    output_proj,
    expert_gain,
    expert_ids,
    gate_weights,
    expert_inner,
    expert_outer,
    cache_pool,
    finished,
    cache_len,
    destination,
):
    tp_count = lax.axis_size("tp")
    where_tp = lax.axis_index("tp")
    replicas = lax.axis_size("req")

    device_rows = tokens.shape[0]
    width = tokens.shape[1]
    seg_local = segment_ids.reshape(device_rows)
    row_span = jnp.arange(device_rows, dtype=jnp.int32)
    token_positions = where_tp * device_rows + row_span
    hidden = rms_gain(tokens, attention_gain)
    query_span_width = QUERY_HEADS * HEAD_SIZE
    key_span_width = KEY_VALUE_HEADS * HEAD_SIZE
    key_value_part = jnp.dot(
        hidden, joined_qkv[:, query_span_width:], preferred_element_type=jnp.float32
    )
    query_part = jnp.dot(
        hidden, joined_qkv[:, :query_span_width], preferred_element_type=jnp.float32
    )
    float_places = token_positions.astype(jnp.float32)
    query_rows = apply_rotary(
        query_part.reshape(device_rows, QUERY_HEADS, HEAD_SIZE),
        float_places,
    ).astype(jnp.bfloat16)
    key_row_list = apply_rotary(
        key_value_part[:, :key_span_width].reshape(device_rows, KEY_VALUE_HEADS, HEAD_SIZE),
        float_places,
    ).astype(jnp.bfloat16)
    value_rows = key_value_part[:, key_span_width:].astype(jnp.bfloat16)
    key_vals = jnp.concatenate(
        [key_row_list.reshape(device_rows, key_span_width), value_rows], axis=1
    )
    seg_rows = jnp.zeros((SEG_ROWS, key_vals.shape[1]), jnp.bfloat16)
    seg_rows = seg_rows.at[0, :device_rows].set(seg_local.astype(jnp.bfloat16))
    block = jnp.concatenate([key_vals, seg_rows], axis=0)
    copies = jnp.broadcast_to(block[None], (tp_count,) + block.shape)
    gathered = lax.all_to_all(copies, "tp", split_axis=0, concat_axis=0, tiled=True)
    prompt_length = tp_count * device_rows
    seg_all = gathered[:, device_rows, :device_rows].astype(jnp.int32).reshape(prompt_length)
    segment_count = 4
    below = jnp.sum(
        (seg_all[None, :] < jnp.arange(segment_count, dtype=jnp.int32)[:, None]).astype(jnp.int32),
        axis=1,
    )
    low = below[seg_local]
    high = token_positions
    lowest = below[jnp.min(seg_local)]
    highest_low = below[jnp.max(seg_local)]
    first_place = where_tp * device_rows
    first_block = lowest // KEY_BLOCK
    end_block = (first_place + device_rows - 1) // KEY_BLOCK + 1
    whole_first = jnp.clip(-(-highest_low // KEY_BLOCK), first_block, end_block)
    whole_end = jnp.clip((first_place + 1) // KEY_BLOCK, whole_first, end_block)
    bounds = jnp.stack([first_block, whole_first, whole_end, end_block]).astype(jnp.int32)
    heads_per_group = QUERY_HEADS // KEY_VALUE_HEADS
    grouped_queries = (
        query_rows.reshape(device_rows, KEY_VALUE_HEADS, heads_per_group, HEAD_SIZE)
        .transpose(1, 2, 0, 3)
        .reshape(KEY_VALUE_HEADS, heads_per_group * device_rows, HEAD_SIZE)
    )
    chosen = finished.reshape(-1)
    lengths = cache_len.reshape(-1)
    target = destination.reshape(-1)
    cache_depth = cache_pool.shape[1]
    kv_width = cache_pool.shape[2]
    pieces = cache_pool[chosen]
    positions = where_tp * cache_depth + jnp.arange(cache_depth, dtype=jnp.int32)
    kept_mask = positions[None, :] < lengths[:, None]
    pieces = jnp.where(kept_mask[:, :, None], pieces, jnp.zeros((), jnp.bfloat16))
    outgoing_cache = (
        jnp.zeros((replicas * tp_count, cache_depth, kv_width), jnp.bfloat16).at[target].set(pieces)
    )
    outgoing_cache, grouped_queries, gathered = lax.optimization_barrier(
        (outgoing_cache, grouped_queries, gathered)
    )
    arrived_cache = lax.all_to_all(
        outgoing_cache, ("req", "tp"), split_axis=0, concat_axis=1, tiled=True
    )
    decode_cache = arrived_cache.reshape(replicas, tp_count * cache_depth, kv_width)

    grouped_out = attention(
        bounds,
        grouped_queries,
        gathered,
        low.reshape(-1, 1),
        high.reshape(-1, 1),
    )
    attended = (
        grouped_out.reshape(KEY_VALUE_HEADS, heads_per_group, device_rows, HEAD_SIZE)
        .transpose(2, 0, 1, 3)
        .reshape(device_rows, query_span_width)
    )
    projected = jnp.dot(attended, output_proj, preferred_element_type=jnp.float32)
    middle = (tokens.astype(jnp.float32) + projected).astype(jnp.bfloat16)
    normed = rms_gain(middle, expert_gain)
    decode_cache, normed = lax.optimization_barrier((decode_cache, normed))
    top_count = expert_ids.shape[1]
    held_count = expert_inner.shape[0]
    total_experts = held_count * tp_count
    capacity = 2 * device_rows * top_count // total_experts
    slots = total_experts * capacity
    pair_count = device_rows * top_count
    flat_ids = expert_ids.reshape(pair_count)
    onehot = (flat_ids[:, None] == jnp.arange(total_experts, dtype=jnp.int32)[None, :]).astype(
        jnp.bfloat16
    )
    pair_span = jnp.arange(pair_count, dtype=jnp.int32)
    earlier = (pair_span[None, :] <= pair_span[:, None]).astype(jnp.bfloat16)
    running_count = jnp.dot(earlier, onehot, preferred_element_type=jnp.float32)
    slot_rank = jnp.sum(running_count * onehot.astype(jnp.float32), axis=1).astype(jnp.int32) - 1
    column_index = flat_ids * capacity + slot_rank
    slot_span = jnp.arange(slots, dtype=jnp.int32)
    pick = (column_index[:, None] == slot_span[None, :]).astype(jnp.bfloat16)
    place = jnp.sum(pick.reshape(device_rows, top_count, slots), axis=1)
    outgoing = jnp.dot(place.T, normed, preferred_element_type=jnp.float32).astype(jnp.bfloat16)
    outgoing = outgoing.reshape(tp_count, held_count, capacity, width)
    hidden_width = expert_outer.shape[1]
    inner_out = jnp.einsum(
        "sgcd,gdf->sgcf",
        lax.all_to_all(outgoing, "tp", split_axis=0, concat_axis=0, tiled=True),
        expert_inner,
        preferred_element_type=jnp.float32,
    )
    active = (
        jnp.maximum(inner_out[..., :hidden_width], 0.0) * inner_out[..., hidden_width:]
    ).astype(jnp.bfloat16)
    final_output = jnp.einsum(
        "sgcf,gfd->sgcd", active, expert_outer, preferred_element_type=jnp.float32
    ).astype(jnp.bfloat16)
    returned = lax.all_to_all(final_output, "tp", split_axis=0, concat_axis=0, tiled=True)
    answers = jnp.dot(
        pick, returned.reshape(slots, width), preferred_element_type=jnp.float32
    ).reshape(device_rows, top_count, width)
    mixed = jnp.sum(answers * gate_weights[..., None], axis=1)
    layer_out = (middle.astype(jnp.float32) + mixed).astype(jnp.bfloat16)
    return (layer_out, decode_cache)


def solution(mesh):
    placed = (
        P(("req", "tp"), None),
        P("req", "tp"),
        P(),
        P(),
        P(),
        P(),
        P(("req", "tp"), None),
        P(("req", "tp"), None),
        P("tp", None, None),
        P("tp", None, None),
        P("req", "tp", None),
        P("req", None),
        P("req", None),
        P("req", None),
    )
    return jax.shard_map(
        local,
        mesh=mesh,
        in_specs=placed,
        out_specs=(P(("req", "tp"), None), P(("req", "tp"), None, None)),
        check_vma=False,
    )
```

```python
import functools

import jax
import jax.numpy as jnp
from jax import lax
from jax.experimental import pallas as pl
from jax.experimental.pallas import tpu as pltpu
from jax.sharding import PartitionSpec as P

QUERY_HEADS = 12
KEY_VALUE_HEADS = 2
HEAD_SIZE = 128
KEY_BLOCK = 1024
SEG_ROWS = 16
LONGEST_SEGMENT = 2048


epsilon = 1e-06
rope_base = 1000000.0
NEGATIVE_FILL = -1e30


def rms_gain(values_in, gain_row):
    as_float = values_in.astype(jnp.float32)
    scale = lax.rsqrt(jnp.mean(as_float * as_float, axis=-1, keepdims=True) + epsilon)
    return (as_float * scale * gain_row).astype(jnp.bfloat16)


def apply_rotary(vectors, token_positions):
    half_dim = vectors.shape[-1] // 2
    frequency = rope_base ** (-jnp.arange(half_dim, dtype=jnp.float32) * 2.0 / vectors.shape[-1])
    angles = token_positions[:, None] * frequency[None, :]
    cosine = jnp.cos(angles)[:, None, :]
    sine_values = jnp.sin(angles)[:, None, :]
    first_half = vectors[..., :half_dim]
    second_half = vectors[..., half_dim:]
    return jnp.concatenate(
        [
            first_half * cosine - second_half * sine_values,
            second_half * cosine + first_half * sine_values,
        ],
        axis=-1,
    )


def attention_kernel(bounds_ref, q_ref, k_ref, v_ref, lo_ref, hi_ref, o_ref):
    ranges = (
        (bounds_ref[0], bounds_ref[1], True),
        (bounds_ref[1], bounds_ref[2], False),
        (bounds_ref[2], bounds_ref[3], True),
    )
    queries = q_ref[...]
    low = lo_ref[...]
    high = hi_ref[...]
    rows = queries.shape[0]
    chunk = k_ref.shape[1] - SEG_ROWS
    per_block = KEY_BLOCK // chunk
    scale = HEAD_SIZE ** (-0.5)

    def block_of(ref, block):
        part = ref[pl.ds(block * per_block, per_block), pl.ds(0, chunk), :]
        return part.reshape(KEY_BLOCK, HEAD_SIZE)

    def raw_scores(block):
        return lax.dot_general(
            queries, block_of(k_ref, block), (((1,), (1,)), ((), ())),
            preferred_element_type=jnp.float32,
        )

    def visible_of(block):
        places = block * KEY_BLOCK + lax.broadcasted_iota(jnp.int32, (1, KEY_BLOCK), 1)
        return (places >= low) & (places <= high)

    best = jnp.full((rows, 1), NEGATIVE_FILL, jnp.float32)
    for first, end, masked in ranges:

        def max_step(block, best, masked=masked):
            scores = raw_scores(block)
            if masked:
                scores = jnp.where(visible_of(block), scores, NEGATIVE_FILL)
            return jnp.maximum(best, jnp.max(scores, axis=1, keepdims=True))

        best = lax.fori_loop(first, end, max_step, best)
    best = best * scale
    carry = (jnp.zeros((rows, 1), jnp.float32), jnp.zeros((rows, HEAD_SIZE), jnp.float32))
    for first, end, masked in ranges:

        def sum_step(block, carry, masked=masked):
            totals, running = carry
            weights = jnp.exp(raw_scores(block) * scale - best)
            if masked:
                weights = jnp.where(visible_of(block), weights, 0.0)
            totals = totals + jnp.sum(weights, axis=1, keepdims=True)
            running = running + jnp.dot(
                weights.astype(jnp.bfloat16), block_of(v_ref, block),
                preferred_element_type=jnp.float32,
            )
            return totals, running

        carry = lax.fori_loop(first, end, sum_step, carry)
    totals, running = carry
    o_ref[...] = (running / totals).astype(o_ref.dtype)


def attention(bounds, grouped_queries, gathered, low, high):
    groups, rows, _ = grouped_queries.shape
    sources, block_rows, _ = gathered.shape
    grid_spec = pltpu.PrefetchScalarGridSpec(
        num_scalar_prefetch=1,
        grid=(groups,),
        in_specs=[
            pl.BlockSpec((None, rows, HEAD_SIZE), lambda g, b: (g, 0, 0)),
            pl.BlockSpec((sources, block_rows, HEAD_SIZE), lambda g, b: (0, 0, g)),
            pl.BlockSpec((sources, block_rows, HEAD_SIZE), lambda g, b: (0, 0, groups + g)),
            pl.BlockSpec((rows, 1), lambda g, b: (0, 0)),
            pl.BlockSpec((rows, 1), lambda g, b: (0, 0)),
        ],
        out_specs=pl.BlockSpec((None, rows, HEAD_SIZE), lambda g, b: (g, 0, 0)),
    )
    return pl.pallas_call(
        attention_kernel,
        grid_spec=grid_spec,
        out_shape=jax.ShapeDtypeStruct((groups, rows, HEAD_SIZE), jnp.bfloat16),
    )(bounds, grouped_queries, gathered, gathered, low, high)


def local(
    tokens,
    segment_ids,
    attention_gain,
    joined_qkv,
    output_proj,
    expert_gain,
    expert_ids,
    gate_weights,
    expert_inner,
    expert_outer,
    cache_pool,
    finished,
    cache_len,
    destination,
):
    tp_count = lax.axis_size("tp")
    where_tp = lax.axis_index("tp")
    replicas = lax.axis_size("req")

    device_rows = tokens.shape[0]
    width = tokens.shape[1]
    seg_local = segment_ids.reshape(device_rows)
    row_span = jnp.arange(device_rows, dtype=jnp.int32)
    token_positions = where_tp * device_rows + row_span
    hidden = rms_gain(tokens, attention_gain)
    query_span_width = QUERY_HEADS * HEAD_SIZE
    key_span_width = KEY_VALUE_HEADS * HEAD_SIZE
    key_value_part = jnp.dot(
        hidden, joined_qkv[:, query_span_width:], preferred_element_type=jnp.float32
    )
    query_part = jnp.dot(
        hidden, joined_qkv[:, :query_span_width], preferred_element_type=jnp.float32
    )
    float_places = token_positions.astype(jnp.float32)
    query_rows = apply_rotary(
        query_part.reshape(device_rows, QUERY_HEADS, HEAD_SIZE),
        float_places,
    ).astype(jnp.bfloat16)
    key_row_list = apply_rotary(
        key_value_part[:, :key_span_width].reshape(device_rows, KEY_VALUE_HEADS, HEAD_SIZE),
        float_places,
    ).astype(jnp.bfloat16)
    value_rows = key_value_part[:, key_span_width:].astype(jnp.bfloat16)
    key_vals = jnp.concatenate(
        [key_row_list.reshape(device_rows, key_span_width), value_rows], axis=1
    )
    seg_rows = jnp.zeros((SEG_ROWS, key_vals.shape[1]), jnp.bfloat16)
    seg_rows = seg_rows.at[0, :device_rows].set(seg_local.astype(jnp.bfloat16))
    block = jnp.concatenate([key_vals, seg_rows], axis=0)
    copies = jnp.broadcast_to(block[None], (tp_count,) + block.shape)
    gathered = lax.all_to_all(copies, "tp", split_axis=0, concat_axis=0, tiled=True)
    prompt_length = tp_count * device_rows
    seg_all = gathered[:, device_rows, :device_rows].astype(jnp.int32).reshape(prompt_length)
    segment_count = 4
    below = jnp.sum(
        (seg_all[None, :] < jnp.arange(segment_count, dtype=jnp.int32)[:, None]).astype(jnp.int32),
        axis=1,
    )
    low = below[seg_local]
    high = token_positions
    lowest = below[jnp.min(seg_local)]
    highest_low = below[jnp.max(seg_local)]
    first_place = where_tp * device_rows
    first_block = lowest // KEY_BLOCK
    end_block = (first_place + device_rows - 1) // KEY_BLOCK + 1
    whole_first = jnp.clip(-(-highest_low // KEY_BLOCK), first_block, end_block)
    whole_end = jnp.clip((first_place + 1) // KEY_BLOCK, whole_first, end_block)
    bounds = jnp.stack([first_block, whole_first, whole_end, end_block]).astype(jnp.int32)
    heads_per_group = QUERY_HEADS // KEY_VALUE_HEADS
    grouped_queries = (
        query_rows.reshape(device_rows, KEY_VALUE_HEADS, heads_per_group, HEAD_SIZE)
        .transpose(1, 2, 0, 3)
        .reshape(KEY_VALUE_HEADS, heads_per_group * device_rows, HEAD_SIZE)
    )
    chosen = finished.reshape(-1)
    lengths = cache_len.reshape(-1)
    target = destination.reshape(-1)
    cache_depth = cache_pool.shape[1]
    kv_width = cache_pool.shape[2]
    pieces = cache_pool[chosen]
    positions = where_tp * cache_depth + jnp.arange(cache_depth, dtype=jnp.int32)
    kept_mask = positions[None, :] < lengths[:, None]
    pieces = jnp.where(kept_mask[:, :, None], pieces, jnp.zeros((), jnp.bfloat16))
    outgoing_cache = (
        jnp.zeros((replicas * tp_count, cache_depth, kv_width), jnp.bfloat16).at[target].set(pieces)
    )
    outgoing_cache, grouped_queries, gathered = lax.optimization_barrier(
        (outgoing_cache, grouped_queries, gathered)
    )
    arrived_cache = lax.all_to_all(
        outgoing_cache, ("req", "tp"), split_axis=0, concat_axis=1, tiled=True
    )
    decode_cache = arrived_cache.reshape(replicas, tp_count * cache_depth, kv_width)

    grouped_out = attention(
        bounds,
        grouped_queries,
        gathered,
        jnp.tile(low, heads_per_group).reshape(-1, 1),
        jnp.tile(high, heads_per_group).reshape(-1, 1),
    )
    attended = (
        grouped_out.reshape(KEY_VALUE_HEADS, heads_per_group, device_rows, HEAD_SIZE)
        .transpose(2, 0, 1, 3)
        .reshape(device_rows, query_span_width)
    )
    projected = jnp.dot(attended, output_proj, preferred_element_type=jnp.float32)
    middle = (tokens.astype(jnp.float32) + projected).astype(jnp.bfloat16)
    normed = rms_gain(middle, expert_gain)
    decode_cache, normed = lax.optimization_barrier((decode_cache, normed))
    top_count = expert_ids.shape[1]
    held_count = expert_inner.shape[0]
    total_experts = held_count * tp_count
    capacity = 2 * device_rows * top_count // total_experts
    slots = total_experts * capacity
    pair_count = device_rows * top_count
    flat_ids = expert_ids.reshape(pair_count)
    onehot = (flat_ids[:, None] == jnp.arange(total_experts, dtype=jnp.int32)[None, :]).astype(
        jnp.bfloat16
    )
    pair_span = jnp.arange(pair_count, dtype=jnp.int32)
    earlier = (pair_span[None, :] <= pair_span[:, None]).astype(jnp.bfloat16)
    running_count = jnp.dot(earlier, onehot, preferred_element_type=jnp.float32)
    slot_rank = jnp.sum(running_count * onehot.astype(jnp.float32), axis=1).astype(jnp.int32) - 1
    column_index = flat_ids * capacity + slot_rank
    slot_span = jnp.arange(slots, dtype=jnp.int32)
    pick = (column_index[:, None] == slot_span[None, :]).astype(jnp.bfloat16)
    place = jnp.sum(pick.reshape(device_rows, top_count, slots), axis=1)
    outgoing = jnp.dot(place.T, normed, preferred_element_type=jnp.float32).astype(jnp.bfloat16)
    outgoing = outgoing.reshape(tp_count, held_count, capacity, width)
    hidden_width = expert_outer.shape[1]
    inner_out = jnp.einsum(
        "sgcd,gdf->sgcf",
        lax.all_to_all(outgoing, "tp", split_axis=0, concat_axis=0, tiled=True),
        expert_inner,
        preferred_element_type=jnp.float32,
    )
    active = (
        jnp.maximum(inner_out[..., :hidden_width], 0.0) * inner_out[..., hidden_width:]
    ).astype(jnp.bfloat16)
    final_output = jnp.einsum(
        "sgcf,gfd->sgcd", active, expert_outer, preferred_element_type=jnp.float32
    ).astype(jnp.bfloat16)
    returned = lax.all_to_all(final_output, "tp", split_axis=0, concat_axis=0, tiled=True)
    answers = jnp.dot(
        pick, returned.reshape(slots, width), preferred_element_type=jnp.float32
    ).reshape(device_rows, top_count, width)
    mixed = jnp.sum(answers * gate_weights[..., None], axis=1)
    layer_out = (middle.astype(jnp.float32) + mixed).astype(jnp.bfloat16)
    return (layer_out, decode_cache)


def solution(mesh):
    placed = (
        P(("req", "tp"), None),
        P("req", "tp"),
        P(),
        P(),
        P(),
        P(),
        P(("req", "tp"), None),
        P(("req", "tp"), None),
        P("tp", None, None),
        P("tp", None, None),
        P("req", "tp", None),
        P("req", None),
        P("req", None),
        P("req", None),
    )
    return jax.shard_map(
        local,
        mesh=mesh,
        in_specs=placed,
        out_specs=(P(("req", "tp"), None), P(("req", "tp"), None, None)),
        check_vma=False,
    )
```
